32 devices in a mesh: groups: 2 (over x), blk: 16 (over z, y, core).
Axes of the slice: x: 2, y: 2, z: 4, core: 2. Of those that a mesh axis runs over, the one named last changes fastest.
Arguments:
- paths: bfloat16 [4096, 512], P(('groups', 'blk')), parts along dimension 0, may hold values from -6 to 6
- deltas: bfloat16 [4096, 512], P(('groups', 'blk')), parts along dimension 0, may hold values from -6 to 6
- payoffs: bfloat16 [4096], P(('groups', 'blk')), parts along dimension 0, may hold values from -6 to 6
- counts: int32 [32, 16], P('groups'), parts along dimension 0, may hold values from 0 to 8, as said below
- w_first: bfloat16 [1024, 1024], P(('groups', 'blk')), parts along dimension 0, may hold values from -0.25 to 0.25
- w_second: bfloat16 [2048, 1024], P(('groups', 'blk')), parts along dimension 0, may hold values from -0.1875 to 0.1875
- w_out: bfloat16 [2048], P('groups'), parts along dimension 0, may hold values from -0.1875 to 0.1875
- mom_first: float32 [1024, 1024], P(('groups', 'blk')), parts along dimension 0, may hold values from -6 to 6
- mom_second: float32 [2048, 1024], P(('groups', 'blk')), parts along dimension 0, may hold values from -6 to 6
- mom_out: float32 [2048], P('groups'), parts along dimension 0, may hold values from -6 to 6
Outputs:
- new_first: float32 [1024, 1024], P(('groups', 'blk')), parts along dimension 0
- new_second: float32 [2048, 1024], P(('groups', 'blk')), parts along dimension 0
- new_out: float32 [2048], P('groups'), parts along dimension 0
The draws below stay inside these ranges and needn't reach their ends.
There are 2 independent parts, one for each index of `groups`. The reference program is written for one: setup_inputs(seed, part) draws one part's arguments, and reference() takes and returns one part's arrays. A program takes and returns all parts, laid end to end along the dimension named above; each array names one. Nothing has to cross between parts.
Inputs may be any that keep to these rules, and one draw needn't show every extreme that they name: Source s hands its valid paths, slot 0 onward, to the trainers in order: counts[s, d] of them to trainer d. Every trainer receives 64 paths or fewer in all, and one receives exactly 64; one source hands 8 to every trainer.
All inputs are finite; a program needn't handle non-finite values.
Results may differ from the reference program's by a relative error of at most 0.00035.
The reference program's roundings to bfloat16 on the way count: a program that leaves them out, or rounds other values in their place, can miss the bound.
Values may be sent and summed in bfloat16 or wider, within the bound.
No kernel may reach another device: no remote copies, remote signals or barrier semaphores. Data moves between devices by JAX's collectives and lax.ppermute only.
A program may use at most 64 MiB of HBM per device.

```python
import jax
import jax.numpy as jnp
from jax import lax

ASSETS = 512
HIDDEN_SIZE = 1024
PAIR_CAP = 8
ROWS_DEV = 128
PATHS = 2048
N_BLK = 16


def draw_counts(key, part):
    key_order = jax.random.fold_in(key, 11)
    key_first = jax.random.fold_in(key, 12)
    key_share = jax.random.fold_in(key, 13)
    key_column = jax.random.fold_in(key, 14)
    half = N_BLK // 2
    order = jax.random.permutation(key_order, N_BLK)
    first = jax.random.randint(key_first, (half, N_BLK), 0, PAIR_CAP + 1)
    share = jax.random.randint(key_share, (half, N_BLK), 0, PAIR_CAP + 1)
    second = share * (PAIR_CAP - first) // PAIR_CAP
    column = jax.random.randint(key_column, (), 0, N_BLK)
    chosen = jnp.arange(N_BLK)[None, :] == column
    second = jnp.where(chosen, PAIR_CAP - first, second)
    first = first.at[0].set(PAIR_CAP)
    second = second.at[0].set(0)
    table = jnp.zeros((N_BLK, N_BLK), jnp.int32)
    table = table.at[order[0::2]].set(first.astype(jnp.int32))
    table = table.at[order[1::2]].set(second.astype(jnp.int32))
    return table


def block_levels(own_key, shape, split, smallest, largest):
    gain = 1.0
    for position, blocks in split:
        draws = jax.random.uniform(jax.random.fold_in(jax.random.fold_in(own_key, 6), position), (blocks,), jnp.float32, smallest / len(split), largest / len(split))
        gain = gain * jnp.repeat(jnp.exp(draws), shape[position] // blocks).reshape((-1,) + (1,) * (len(shape) - 1 - position))
    return gain


def normal_values(key, shape, deviation, limit, shards=(), held_as=jnp.bfloat16):
    result = deviation * jax.random.normal(key, shape, jnp.float32)
    if shards:
        result = result * block_levels(key, shape, shards, -0.22, 0.18)
    return jnp.clip(result, -limit, limit).astype(held_as)


def setup_inputs(seed: int = 0, part: int = 0) -> dict:
    streams_of = jax.random.split(jax.random.key(seed), 11)
    part_keys = jax.random.split(jax.random.fold_in(streams_of[10], part), 11)
    paths = normal_values(part_keys[0], (PATHS, ASSETS), 1.0, 6.0, ((0, 16),))
    deltas = normal_values(part_keys[1], (PATHS, ASSETS), 1.0, 6.0, ((0, 16),))
    payoffs = normal_values(part_keys[2], (PATHS,), 1.0, 6.0, ((0, 16),))
    counts = draw_counts(jax.random.fold_in(jax.random.fold_in(streams_of[10], part), 71), part)
    w_first = normal_values(part_keys[4], (ASSETS, HIDDEN_SIZE), ASSETS ** -0.5, 0.25, ((0, 16),))
    w_second = normal_values(part_keys[5], (HIDDEN_SIZE, HIDDEN_SIZE), HIDDEN_SIZE ** -0.5, 0.1875, ((0, 16),))
    w_out = normal_values(part_keys[6], (HIDDEN_SIZE,), HIDDEN_SIZE ** -0.5, 0.1875)
    mom_first = normal_values(part_keys[7], (ASSETS, HIDDEN_SIZE), 1.0, 6.0, ((0, 16),), jnp.float32)
    mom_second = normal_values(part_keys[8], (HIDDEN_SIZE, HIDDEN_SIZE), 1.0, 6.0, ((0, 16),), jnp.float32)
    mom_out = normal_values(part_keys[9], (HIDDEN_SIZE,), 1.0, 6.0, (), jnp.float32)
    return dict(paths=paths, deltas=deltas, payoffs=payoffs, counts=counts, w_first=w_first, w_second=w_second, w_out=w_out, mom_first=mom_first, mom_second=mom_second, mom_out=mom_out)


def rows_product(left, right):
    return lax.dot_general(left, right, (((0,), (0,)), ((), ())), preferred_element_type=jnp.float32)

def twin_terms(x_rows, z_rows, y_rows, mask, w_one, w_two, w_three):
    w_outf = w_three.astype(jnp.float32)
    a_one = jnp.dot(x_rows, w_one, preferred_element_type=jnp.float32)
    s_one = jax.nn.sigmoid(a_one)
    h_one = jax.nn.softplus(a_one).astype(jnp.bfloat16)
    a_two = jnp.dot(h_one, w_two, preferred_element_type=jnp.float32)
    s_two = jax.nn.sigmoid(a_two)
    h_two = jax.nn.softplus(a_two)
    value = lax.optimization_barrier(jnp.sum(h_two * w_outf[None, :], axis=1))
    g_two = (s_two * w_outf[None, :]).astype(jnp.bfloat16)
    c_one = lax.dot_general(g_two, w_two, (((1,), (1,)), ((), ())), preferred_element_type=jnp.float32)
    g_one = (c_one * s_one).astype(jnp.bfloat16)
    slope = lax.dot_general(g_one, w_one, (((1,), (1,)), ((), ())), preferred_element_type=jnp.float32)
    e_value = 2.0 * mask * (value - y_rows.astype(jnp.float32))
    e_slope = (2.0 * mask[:, None] * (slope - z_rows.astype(jnp.float32))).astype(jnp.bfloat16)
    e_gone = jnp.dot(e_slope, w_one, preferred_element_type=jnp.float32)
    e_cone = (e_gone * s_one).astype(jnp.bfloat16)
    e_sone = e_gone * c_one
    e_gtwo = jnp.dot(e_cone, w_two, preferred_element_type=jnp.float32)
    grad_three = lax.optimization_barrier(jnp.sum(e_gtwo * s_two + e_value[:, None] * h_two, axis=0))
    e_atwo = (e_gtwo * w_outf[None, :] * s_two * (1.0 - s_two) + e_value[:, None] * w_outf[None, :] * s_two).astype(jnp.bfloat16)
    e_hone = lax.dot_general(e_atwo, w_two, (((1,), (1,)), ((), ())), preferred_element_type=jnp.float32)
    e_aone = (e_sone * s_one * (1.0 - s_one) + e_hone * s_one).astype(jnp.bfloat16)
    return (e_slope, g_one, e_aone, e_cone, g_two, h_one, e_atwo, grad_three)

def normalized(grad):
    return grad / jnp.sqrt(lax.optimization_barrier(jnp.mean(grad * grad, axis=-1, keepdims=True)) + 1e-06)

def reference(paths, deltas, payoffs, counts, w_first, w_second, w_out, mom_first, mom_second, mom_out):
    totals = lax.optimization_barrier(jnp.sum(counts, axis=1)).astype(jnp.int32)
    x_blocks = paths.reshape(N_BLK, ROWS_DEV, ASSETS)
    z_blocks = deltas.reshape(N_BLK, ROWS_DEV, ASSETS)
    y_blocks = payoffs.reshape(N_BLK, ROWS_DEV)

    def accumulate(carry, item):
        x_rows, z_rows, y_rows, total = item
        mask = (jnp.arange(ROWS_DEV, dtype=jnp.int32) < total).astype(jnp.float32)
        e_slope, g_one, e_aone, e_cone, g_two, h_one, e_atwo, grad_three = twin_terms(x_rows, z_rows, y_rows, mask, w_first, w_second, w_out)
        first = rows_product(x_rows, e_aone) + rows_product(e_slope, g_one)
        second = rows_product(e_cone, g_two) + rows_product(h_one, e_atwo)
        return ((carry[0] + first, carry[1] + second, carry[2] + grad_three), None)
    init = (jnp.zeros((ASSETS, HIDDEN_SIZE), jnp.float32), jnp.zeros((HIDDEN_SIZE, HIDDEN_SIZE), jnp.float32), jnp.zeros((HIDDEN_SIZE,), jnp.float32))
    grads, _ = lax.scan(accumulate, init, (x_blocks, z_blocks, y_blocks, totals))
    new_first = 0.8 * mom_first + 0.2 * normalized(grads[0])
    new_second = 0.8 * mom_second + 0.2 * normalized(grads[1])
    new_out = 0.8 * mom_out + 0.2 * normalized(grads[2])
    return (new_first, new_second, new_out)
```

```python
import jax
import jax.numpy as jnp
from jax import lax
from jax.sharding import PartitionSpec as P


def rows_product(left, right):
    return lax.dot_general(
        left, right, (((0,), (0,)), ((), ())), preferred_element_type=jnp.float32
    )


def twin_terms(x_rows, z_rows, y_rows, mask, w_one, w_two, w_three):
    w_outf = w_three.astype(jnp.float32)
    a_one = jnp.dot(x_rows, w_one, preferred_element_type=jnp.float32)
    s_one = jax.nn.sigmoid(a_one)
    h_one = jax.nn.softplus(a_one).astype(jnp.bfloat16)
    a_two = jnp.dot(h_one, w_two, preferred_element_type=jnp.float32)
    s_two = jax.nn.sigmoid(a_two)
    h_two = jax.nn.softplus(a_two)
    value = jnp.sum(h_two * w_outf[None, :], axis=1)
    g_two = (s_two * w_outf[None, :]).astype(jnp.bfloat16)
    c_one = lax.dot_general(
        g_two, w_two, (((1,), (1,)), ((), ())), preferred_element_type=jnp.float32
    )
    g_one = (c_one * s_one).astype(jnp.bfloat16)
    slope = lax.dot_general(
        g_one, w_one, (((1,), (1,)), ((), ())), preferred_element_type=jnp.float32
    )
    e_value = 2.0 * mask * (value - y_rows.astype(jnp.float32))
    e_slope = (2.0 * mask[:, None] * (slope - z_rows.astype(jnp.float32))).astype(jnp.bfloat16)
    e_gone = jnp.dot(e_slope, w_one, preferred_element_type=jnp.float32)
    e_cone = (e_gone * s_one).astype(jnp.bfloat16)
    e_sone = e_gone * c_one
    e_gtwo = jnp.dot(e_cone, w_two, preferred_element_type=jnp.float32)
    grad_three = jnp.sum(e_gtwo * s_two + e_value[:, None] * h_two, axis=0)
    e_atwo = (
        e_gtwo * w_outf[None, :] * s_two * (1.0 - s_two)
        + e_value[:, None] * w_outf[None, :] * s_two
    ).astype(jnp.bfloat16)
    e_hone = lax.dot_general(
        e_atwo, w_two, (((1,), (1,)), ((), ())), preferred_element_type=jnp.float32
    )
    e_aone = (e_sone * s_one * (1.0 - s_one) + e_hone * s_one).astype(jnp.bfloat16)
    return (e_slope, g_one, e_aone, e_cone, g_two, h_one, e_atwo, grad_three)


def normalized(grad):
    return grad / jnp.sqrt(jnp.mean(grad * grad, axis=-1, keepdims=True) + 1e-06)


def per_device(
    paths, deltas, payoffs, counts, w_first, w_second, w_out, mom_first, mom_second, mom_out
):
    position = lax.axis_index("blk")
    n_blk = lax.axis_size("blk")
    rows_dev = paths.shape[0]
    r_one, r_two = w_first.shape[0], w_second.shape[0]
    hidden = w_first.shape[1]
    gathered = lax.all_gather(
        jnp.concatenate([w_first, w_second], axis=0), "blk", axis=0, tiled=False
    )
    w_one = gathered[:, :r_one].reshape(n_blk * r_one, hidden)
    w_two = gathered[:, r_one:].reshape(n_blk * r_two, hidden)
    sending = lax.dynamic_index_in_dim(counts, position, 0, keepdims=False)
    x_rows, z_rows, y_rows = (paths, deltas, payoffs)
    total = jnp.sum(sending)
    mask = (jnp.arange(rows_dev, dtype=jnp.int32) < total).astype(jnp.float32)
    e_slope, g_one, e_aone, e_cone, g_two, h_one, e_atwo, grad_three = twin_terms(
        x_rows, z_rows, y_rows, mask, w_one, w_two, w_out
    )
    part_one = rows_product(x_rows, e_aone) + rows_product(e_slope, g_one)
    part_two = rows_product(e_cone, g_two) + rows_product(h_one, e_atwo)
    blocks = jnp.concatenate(
        [
            part_one.reshape(n_blk, r_one, hidden),
            part_two.reshape(n_blk, r_two, hidden),
        ],
        axis=1,
    )
    reduced = lax.psum_scatter(blocks, "blk", scatter_dimension=0, tiled=True)[0]
    grad_one = reduced[:r_one]
    grad_two = reduced[r_one:]
    grad_out = lax.psum(grad_three, "blk")
    new_first = 0.8 * mom_first + 0.2 * normalized(grad_one)
    new_second = 0.8 * mom_second + 0.2 * normalized(grad_two)
    new_out = 0.8 * mom_out + 0.2 * normalized(grad_out)
    return (new_first, new_second, new_out)


def solution(mesh):
    in_specs = (
        P(("groups", "blk"), None),
        P(("groups", "blk"), None),
        P(("groups", "blk")),
        P("groups", None),
        P(("groups", "blk"), None),
        P(("groups", "blk"), None),
        P("groups"),
        P(("groups", "blk"), None),
        P(("groups", "blk"), None),
        P("groups"),
    )
    out_specs = (P(("groups", "blk"), None), P(("groups", "blk"), None), P("groups"))
    return jax.shard_map(
        per_device, mesh=mesh, in_specs=in_specs, out_specs=out_specs, check_vma=False
    )
```

```python
import functools

import jax
import jax.numpy as jnp
from jax import lax
from jax.sharding import PartitionSpec as P


def rows_product(left, right):
    return lax.dot_general(
        left, right, (((0,), (0,)), ((), ())), preferred_element_type=jnp.float32
    )


def twin_terms(x_rows, z_rows, y_rows, mask, w_one, w_two, w_three):
    w_outf = w_three.astype(jnp.float32)
    a_one = jnp.dot(x_rows, w_one, preferred_element_type=jnp.float32)
    s_one = jax.nn.sigmoid(a_one)
    h_one = jax.nn.softplus(a_one).astype(jnp.bfloat16)
    a_two = jnp.dot(h_one, w_two, preferred_element_type=jnp.float32)
    s_two = jax.nn.sigmoid(a_two)
    h_two = jax.nn.softplus(a_two)
    value = jnp.sum(h_two * w_outf[None, :], axis=1)
    g_two = (s_two * w_outf[None, :]).astype(jnp.bfloat16)
    c_one = lax.dot_general(
        g_two, w_two, (((1,), (1,)), ((), ())), preferred_element_type=jnp.float32
    )
    g_one = (c_one * s_one).astype(jnp.bfloat16)
    slope = lax.dot_general(
        g_one, w_one, (((1,), (1,)), ((), ())), preferred_element_type=jnp.float32
    )
    e_value = 2.0 * mask * (value - y_rows.astype(jnp.float32))
    e_slope = (2.0 * mask[:, None] * (slope - z_rows.astype(jnp.float32))).astype(jnp.bfloat16)
    e_gone = jnp.dot(e_slope, w_one, preferred_element_type=jnp.float32)
    e_cone = (e_gone * s_one).astype(jnp.bfloat16)
    e_sone = e_gone * c_one
    e_gtwo = jnp.dot(e_cone, w_two, preferred_element_type=jnp.float32)
    grad_three = jnp.sum(e_gtwo * s_two + e_value[:, None] * h_two, axis=0)
    e_atwo = (
        e_gtwo * w_outf[None, :] * s_two * (1.0 - s_two)
        + e_value[:, None] * w_outf[None, :] * s_two
    ).astype(jnp.bfloat16)
    e_hone = lax.dot_general(
        e_atwo, w_two, (((1,), (1,)), ((), ())), preferred_element_type=jnp.float32
    )
    e_aone = (e_sone * s_one * (1.0 - s_one) + e_hone * s_one).astype(jnp.bfloat16)
    return (e_slope, g_one, e_aone, e_cone, g_two, h_one, e_atwo, grad_three)


def normalized(grad):
    return grad / jnp.sqrt(jnp.mean(grad * grad, axis=-1, keepdims=True) + 1e-06)


def ring_plan(n_blk):
    chips = n_blk // 2
    snake = list(range(0, chips, 2)) + list(range(chips - 1, 0, -2))
    place = [0] * chips
    for p, q in enumerate(snake):
        place[q] = p
    cw = [(2 * snake[p] + c, 2 * snake[(p + 1) % chips] + c) for p in range(chips) for c in range(2)]
    ccw = [(b, a) for a, b in cw]
    partner = [(b, b ^ 1) for b in range(n_blk)]
    return chips, snake, place, cw, ccw, partner


def ring_all_gather(x, n_blk):
    chips, snake, place, cw, ccw, partner = ring_plan(n_blk)
    ahead = chips // 2
    behind = chips - 1 - ahead
    position = lax.axis_index("blk")
    core, chip = position % 2, position // 2
    spot = jnp.asarray(place, jnp.int32)[chip]
    rel = [None] * chips
    rel[0] = x
    left = right = x
    for s in range(1, ahead + 1):
        left = lax.ppermute(left, "blk", cw)
        rel[chips - s] = left
        if s <= behind:
            right = lax.ppermute(right, "blk", ccw)
            rel[s] = right
    mine = jnp.stack(rel)
    other = lax.ppermute(mine, "blk", partner)
    both = jnp.concatenate([mine, other], axis=0)
    dest = jnp.arange(n_blk, dtype=jnp.int32)
    dest_chip, dest_core = dest // 2, dest % 2
    k = (jnp.asarray(place, jnp.int32)[dest_chip] - spot) % chips
    index = jnp.where(dest_core == core, 0, chips) + k
    return jnp.take(both, index, axis=0)


def ring_reduce_scatter(blocks, extra, n_blk):
    chips, snake, place, cw, ccw, partner = ring_plan(n_blk)
    ahead = chips // 2
    behind = chips - 1 - ahead
    rows = blocks.shape[1]
    position = lax.axis_index("blk")
    core, chip = position % 2, position // 2
    spot = jnp.asarray(place, jnp.int32)[chip]
    order = jnp.asarray(snake, jnp.int32)
    pairs = blocks.reshape(chips, 2, rows, blocks.shape[2])
    kept = lax.dynamic_index_in_dim(pairs, core, 1, keepdims=False)
    given = lax.dynamic_index_in_dim(pairs, 1 - core, 1, keepdims=False)
    sent = jnp.concatenate([given.reshape(chips * rows, -1), extra[None]], axis=0)
    got = lax.ppermute(sent, "blk", partner)
    summed = kept + got[: chips * rows].reshape(chips, rows, -1)
    chip_extra = extra + got[chips * rows]

    def block_at(k):
        return lax.dynamic_index_in_dim(summed, order[(spot + k) % chips], 0, keepdims=False)

    rel = [None] * chips
    rel[0] = chip_extra
    acc = block_at(ahead)
    carried = chip_extra
    for s in range(1, ahead + 1):
        got = lax.ppermute(jnp.concatenate([acc, carried[None]], axis=0), "blk", cw)
        acc = got[:rows] + block_at(ahead - s)
        carried = got[rows]
        rel[chips - s] = carried
    if behind:
        acc_back = block_at(chips - behind)
        carried = chip_extra
        for s in range(1, behind + 1):
            got = lax.ppermute(jnp.concatenate([acc_back, carried[None]], axis=0), "blk", ccw)
            carried = got[rows]
            rel[s] = carried
            if s < behind:
                acc_back = got[:rows] + block_at(chips - behind + s)
            else:
                acc = acc + got[:rows]
    by_rel = jnp.stack(rel)
    k = (jnp.asarray(place, jnp.int32) - spot) % chips
    by_chip = jnp.take(by_rel, k, axis=0)
    return acc, jnp.sum(by_chip, axis=0)


def per_device(
    paths, deltas, payoffs, counts, w_first, w_second, w_out, mom_first, mom_second, mom_out,
    n_blk,
):
    position = lax.axis_index("blk")
    rows_dev = paths.shape[0]
    r_one, r_two = w_first.shape[0], w_second.shape[0]
    hidden = w_first.shape[1]
    gathered = ring_all_gather(jnp.concatenate([w_first, w_second], axis=0), n_blk)
    w_one = gathered[:, :r_one].reshape(n_blk * r_one, hidden)
    w_two = gathered[:, r_one:].reshape(n_blk * r_two, hidden)
    sending = lax.dynamic_index_in_dim(counts, position, 0, keepdims=False)
    x_rows, z_rows, y_rows = (paths, deltas, payoffs)
    total = jnp.sum(sending)
    mask = (jnp.arange(rows_dev, dtype=jnp.int32) < total).astype(jnp.float32)
    e_slope, g_one, e_aone, e_cone, g_two, h_one, e_atwo, grad_three = twin_terms(
        x_rows, z_rows, y_rows, mask, w_one, w_two, w_out
    )
    part_one = rows_product(x_rows, e_aone) + rows_product(e_slope, g_one)
    part_two = rows_product(e_cone, g_two) + rows_product(h_one, e_atwo)
    blocks = jnp.concatenate(
        [
            part_one.reshape(n_blk, r_one, hidden),
            part_two.reshape(n_blk, r_two, hidden),
        ],
        axis=1,
    )
    reduced, grad_out = ring_reduce_scatter(blocks, grad_three, n_blk)
    grad_one = reduced[:r_one]
    grad_two = reduced[r_one:]
    new_first = 0.8 * mom_first + 0.2 * normalized(grad_one)
    new_second = 0.8 * mom_second + 0.2 * normalized(grad_two)
    new_out = 0.8 * mom_out + 0.2 * normalized(grad_out)
    return (new_first, new_second, new_out)


def solution(mesh):
    in_specs = (
        P(("groups", "blk"), None),
        P(("groups", "blk"), None),
        P(("groups", "blk")),
        P("groups", None),
        P(("groups", "blk"), None),
        P(("groups", "blk"), None),
        P("groups"),
        P(("groups", "blk"), None),
        P(("groups", "blk"), None),
        P("groups"),
    )
    out_specs = (P(("groups", "blk"), None), P(("groups", "blk"), None), P("groups"))
    return jax.shard_map(
        functools.partial(per_device, n_blk=mesh.shape["blk"]),
        mesh=mesh, in_specs=in_specs, out_specs=out_specs, check_vma=False,
    )
```

```python
import functools

import jax
import jax.numpy as jnp
from jax import lax
from jax.sharding import PartitionSpec as P


def rows_product(left, right):
    return lax.dot_general(
        left, right, (((0,), (0,)), ((), ())), preferred_element_type=jnp.float32
    )


def twin_terms(x_rows, z_rows, y_rows, mask, w_one, w_two, w_three):
    w_outf = w_three.astype(jnp.float32)
    a_one = jnp.dot(x_rows, w_one, preferred_element_type=jnp.float32)
    s_one = jax.nn.sigmoid(a_one)
    h_one = jax.nn.softplus(a_one).astype(jnp.bfloat16)
    a_two = jnp.dot(h_one, w_two, preferred_element_type=jnp.float32)
    s_two = jax.nn.sigmoid(a_two)
    h_two = jax.nn.softplus(a_two)
    value = jnp.sum(h_two * w_outf[None, :], axis=1)
    g_two = (s_two * w_outf[None, :]).astype(jnp.bfloat16)
    c_one = lax.dot_general(
        g_two, w_two, (((1,), (1,)), ((), ())), preferred_element_type=jnp.float32
    )
    g_one = (c_one * s_one).astype(jnp.bfloat16)
    slope = lax.dot_general(
        g_one, w_one, (((1,), (1,)), ((), ())), preferred_element_type=jnp.float32
    )
    e_value = 2.0 * mask * (value - y_rows.astype(jnp.float32))
    e_slope = (2.0 * mask[:, None] * (slope - z_rows.astype(jnp.float32))).astype(jnp.bfloat16)
    e_gone = jnp.dot(e_slope, w_one, preferred_element_type=jnp.float32)
    e_cone = (e_gone * s_one).astype(jnp.bfloat16)
    e_sone = e_gone * c_one
    e_gtwo = jnp.dot(e_cone, w_two, preferred_element_type=jnp.float32)
    grad_three = jnp.sum(e_gtwo * s_two + e_value[:, None] * h_two, axis=0)
    e_atwo = (
        e_gtwo * w_outf[None, :] * s_two * (1.0 - s_two)
        + e_value[:, None] * w_outf[None, :] * s_two
    ).astype(jnp.bfloat16)
    e_hone = lax.dot_general(
        e_atwo, w_two, (((1,), (1,)), ((), ())), preferred_element_type=jnp.float32
    )
    e_aone = (e_sone * s_one * (1.0 - s_one) + e_hone * s_one).astype(jnp.bfloat16)
    return (e_slope, g_one, e_aone, e_cone, g_two, h_one, e_atwo, grad_three)


def normalized(grad):
    return grad / jnp.sqrt(jnp.mean(grad * grad, axis=-1, keepdims=True) + 1e-06)


def ring_plan(n_blk):
    chips = n_blk // 2
    snake = list(range(0, chips, 2)) + list(range(chips - 1, 0, -2))
    place = [0] * chips
    for p, q in enumerate(snake):
        place[q] = p
    cw = [(2 * snake[p] + c, 2 * snake[(p + 1) % chips] + c) for p in range(chips) for c in range(2)]
    ccw = [(b, a) for a, b in cw]
    partner = [(b, b ^ 1) for b in range(n_blk)]
    return chips, snake, place, cw, ccw, partner


def ring_all_gather(x, n_blk):
    chips, snake, place, cw, ccw, partner = ring_plan(n_blk)
    ahead = chips // 2
    behind = chips - 1 - ahead
    position = lax.axis_index("blk")
    core, chip = position % 2, position // 2
    spot = jnp.asarray(place, jnp.int32)[chip]
    rel = [None] * chips
    rel[0] = x
    left = right = x
    for s in range(1, ahead + 1):
        left = lax.ppermute(left, "blk", cw)
        rel[chips - s] = left
        if s <= behind:
            right = lax.ppermute(right, "blk", ccw)
            rel[s] = right
    mine = jnp.stack(rel)
    other = lax.ppermute(mine, "blk", partner)
    both = jnp.concatenate([mine, other], axis=0)
    dest = jnp.arange(n_blk, dtype=jnp.int32)
    dest_chip, dest_core = dest // 2, dest % 2
    k = (jnp.asarray(place, jnp.int32)[dest_chip] - spot) % chips
    index = jnp.where(dest_core == core, 0, chips) + k
    return jnp.take(both, index, axis=0)


def ring_reduce_scatter(summed, extra, n_blk):
    chips, snake, place, cw, ccw, partner = ring_plan(n_blk)
    ahead = chips // 2
    behind = chips - 1 - ahead
    position = lax.axis_index("blk")
    chip = position // 2
    spot = jnp.asarray(place, jnp.int32)[chip]
    order = jnp.asarray(snake, jnp.int32)

    def block_at(k):
        return lax.dynamic_index_in_dim(summed, order[(spot + k) % chips], 0, keepdims=False)

    rel = [None] * chips
    rel[0] = extra
    acc = block_at(ahead)
    carried = extra
    for s in range(1, ahead + 1):
        acc = lax.ppermute(acc, "blk", cw) + block_at(ahead - s)
        carried = lax.ppermute(carried, "blk", cw)
        rel[chips - s] = carried
    if behind:
        acc_back = block_at(chips - behind)
        carried = extra
        for s in range(1, behind + 1):
            acc_back = lax.ppermute(acc_back, "blk", ccw)
            carried = lax.ppermute(carried, "blk", ccw)
            rel[s] = carried
            if s < behind:
                acc_back = acc_back + block_at(chips - behind + s)
        acc = acc + acc_back
    by_rel = jnp.stack(rel)
    k = (jnp.asarray(place, jnp.int32) - spot) % chips
    by_chip = jnp.take(by_rel, k, axis=0)
    return acc, jnp.sum(by_chip, axis=0)


def slots_product(left, right):
    return lax.dot_general(
        left, right, (((0,), (0,)), ((), ())), preferred_element_type=jnp.float32
    )


def per_device(
    paths, deltas, payoffs, counts, w_first, w_second, w_out, mom_first, mom_second, mom_out,
    n_blk,
):
    chips, snake, place, cw, ccw, partner = ring_plan(n_blk)
    position = lax.axis_index("blk")
    core = position % 2
    rows_dev = paths.shape[0]
    r_one, r_two = w_first.shape[0], w_second.shape[0]
    hidden = w_first.shape[1]
    gathered = ring_all_gather(jnp.concatenate([w_first, w_second], axis=0), n_blk)
    w_one = gathered[:, :r_one].reshape(n_blk * r_one, hidden)
    w_two = gathered[:, r_one:].reshape(n_blk * r_two, hidden)
    sending = lax.dynamic_index_in_dim(counts, position, 0, keepdims=False)
    x_rows, z_rows, y_rows = (paths, deltas, payoffs)
    total = jnp.sum(sending)
    mask = (jnp.arange(rows_dev, dtype=jnp.int32) < total).astype(jnp.float32)
    e_slope, g_one, e_aone, e_cone, g_two, h_one, e_atwo, grad_three = twin_terms(
        x_rows, z_rows, y_rows, mask, w_one, w_two, w_out
    )
    a_all = jnp.concatenate([x_rows, e_slope], axis=0).reshape(2 * rows_dev, chips, 2, r_one)
    c_all = jnp.concatenate([e_cone, h_one], axis=0).reshape(2 * rows_dev, chips, 2, r_two)
    b_me = jnp.concatenate([e_aone, g_one], axis=0)
    d_me = jnp.concatenate([g_two, e_atwo], axis=0)
    a_keep = lax.dynamic_index_in_dim(a_all, core, 2, keepdims=False)
    a_give = lax.dynamic_index_in_dim(a_all, 1 - core, 2, keepdims=False)
    c_keep = lax.dynamic_index_in_dim(c_all, core, 2, keepdims=False)
    c_give = lax.dynamic_index_in_dim(c_all, 1 - core, 2, keepdims=False)
    a_got = lax.ppermute(a_give, "blk", partner)
    b_got = lax.ppermute(b_me, "blk", partner)
    c_got = lax.ppermute(c_give, "blk", partner)
    d_got = lax.ppermute(d_me, "blk", partner)
    extra = grad_three + lax.ppermute(grad_three, "blk", partner)
    part_one = slots_product(a_keep, b_me) + slots_product(a_got, b_got)
    part_two = slots_product(c_keep, d_me) + slots_product(c_got, d_got)
    summed = jnp.concatenate([part_one, part_two], axis=1)
    reduced, grad_out = ring_reduce_scatter(summed, extra, n_blk)
    grad_one = reduced[:r_one]
    grad_two = reduced[r_one:]
    new_first = 0.8 * mom_first + 0.2 * normalized(grad_one)
    new_second = 0.8 * mom_second + 0.2 * normalized(grad_two)
    new_out = 0.8 * mom_out + 0.2 * normalized(grad_out)
    return (new_first, new_second, new_out)


def solution(mesh):
    in_specs = (
        P(("groups", "blk"), None),
        P(("groups", "blk"), None),
        P(("groups", "blk")),
        P("groups", None),
        P(("groups", "blk"), None),
        P(("groups", "blk"), None),
        P("groups"),
        P(("groups", "blk"), None),
        P(("groups", "blk"), None),
        P("groups"),
    )
    out_specs = (P(("groups", "blk"), None), P(("groups", "blk"), None), P("groups"))
    return jax.shard_map(
        functools.partial(per_device, n_blk=mesh.shape["blk"]),
        mesh=mesh, in_specs=in_specs, out_specs=out_specs, check_vma=False,
    )
```

```python
import functools

import jax
import jax.numpy as jnp
from jax import lax
from jax.sharding import PartitionSpec as P


def rows_product(left, right):
    return lax.dot_general(
        left, right, (((0,), (0,)), ((), ())), preferred_element_type=jnp.float32
    )


def twin_terms(x_rows, z_rows, y_rows, mask, w_one, w_two, w_three):
    w_outf = w_three.astype(jnp.float32)
    a_one = jnp.dot(x_rows, w_one, preferred_element_type=jnp.float32)
    s_one = jax.nn.sigmoid(a_one)
    h_one = jax.nn.softplus(a_one).astype(jnp.bfloat16)
    a_two = jnp.dot(h_one, w_two, preferred_element_type=jnp.float32)
    s_two = jax.nn.sigmoid(a_two)
    h_two = jax.nn.softplus(a_two)
    value = jnp.sum(h_two * w_outf[None, :], axis=1)
    g_two = (s_two * w_outf[None, :]).astype(jnp.bfloat16)
    c_one = lax.dot_general(
        g_two, w_two, (((1,), (1,)), ((), ())), preferred_element_type=jnp.float32
    )
    g_one = (c_one * s_one).astype(jnp.bfloat16)
    slope = lax.dot_general(
        g_one, w_one, (((1,), (1,)), ((), ())), preferred_element_type=jnp.float32
    )
    e_value = 2.0 * mask * (value - y_rows.astype(jnp.float32))
    e_slope = (2.0 * mask[:, None] * (slope - z_rows.astype(jnp.float32))).astype(jnp.bfloat16)
    e_gone = jnp.dot(e_slope, w_one, preferred_element_type=jnp.float32)
    e_cone = (e_gone * s_one).astype(jnp.bfloat16)
    e_sone = e_gone * c_one
    e_gtwo = jnp.dot(e_cone, w_two, preferred_element_type=jnp.float32)
    grad_three = jnp.sum(e_gtwo * s_two + e_value[:, None] * h_two, axis=0)
    e_atwo = (
        e_gtwo * w_outf[None, :] * s_two * (1.0 - s_two)
        + e_value[:, None] * w_outf[None, :] * s_two
    ).astype(jnp.bfloat16)
    e_hone = lax.dot_general(
        e_atwo, w_two, (((1,), (1,)), ((), ())), preferred_element_type=jnp.float32
    )
    e_aone = (e_sone * s_one * (1.0 - s_one) + e_hone * s_one).astype(jnp.bfloat16)
    return (e_slope, g_one, e_aone, e_cone, g_two, h_one, e_atwo, grad_three)


def normalized(grad):
    return grad / jnp.sqrt(jnp.mean(grad * grad, axis=-1, keepdims=True) + 1e-06)


def ring_plan(n_blk):
    chips = n_blk // 2
    snake = list(range(0, chips, 2)) + list(range(chips - 1, 0, -2))
    place = [0] * chips
    for p, q in enumerate(snake):
        place[q] = p
    cw = [(2 * snake[p] + c, 2 * snake[(p + 1) % chips] + c) for p in range(chips) for c in range(2)]
    ccw = [(b, a) for a, b in cw]
    partner = [(b, b ^ 1) for b in range(n_blk)]
    return chips, snake, place, cw, ccw, partner


def ring_all_gather(x, n_blk):
    chips, snake, place, cw, ccw, partner = ring_plan(n_blk)
    ahead = chips // 2
    behind = chips - 1 - ahead
    position = lax.axis_index("blk")
    core, chip = position % 2, position // 2
    spot = jnp.asarray(place, jnp.int32)[chip]
    rel = [None] * chips
    rel[0] = x
    left = right = x
    for s in range(1, ahead + 1):
        left = lax.ppermute(left, "blk", cw)
        rel[chips - s] = left
        if s <= behind:
            right = lax.ppermute(right, "blk", ccw)
            rel[s] = right
    mine = jnp.stack(rel)
    other = lax.ppermute(mine, "blk", partner)
    both = jnp.concatenate([mine, other], axis=0)
    dest = jnp.arange(n_blk, dtype=jnp.int32)
    dest_chip, dest_core = dest // 2, dest % 2
    k = (jnp.asarray(place, jnp.int32)[dest_chip] - spot) % chips
    index = jnp.where(dest_core == core, 0, chips) + k
    return jnp.take(both, index, axis=0)


def ring_reduce_scatter(summed, n_blk):
    chips, snake, place, cw, ccw, partner = ring_plan(n_blk)
    ahead = chips // 2
    behind = chips - 1 - ahead
    acc = summed[ahead % chips]
    for s in range(1, ahead + 1):
        acc = lax.ppermute(acc, "blk", cw) + summed[(ahead - s) % chips]
    if behind:
        acc_back = summed[chips - behind]
        for s in range(1, behind + 1):
            acc_back = lax.ppermute(acc_back, "blk", ccw)
            if s < behind:
                acc_back = acc_back + summed[chips - behind + s]
        acc = acc + acc_back
    return acc


def slots_product(left, right):
    return lax.dot_general(
        left, right, (((0,), (0,)), ((), ())), preferred_element_type=jnp.float32
    )


def per_device(
    paths, deltas, payoffs, counts, w_first, w_second, w_out, mom_first, mom_second, mom_out,
    n_blk,
):
    chips, snake, place, cw, ccw, partner = ring_plan(n_blk)
    position = lax.axis_index("blk")
    core = position % 2
    rows_dev = paths.shape[0]
    r_one, r_two = w_first.shape[0], w_second.shape[0]
    hidden = w_first.shape[1]
    gathered = ring_all_gather(jnp.concatenate([w_first, w_second], axis=0), n_blk)
    w_one = gathered[:, :r_one].reshape(n_blk * r_one, hidden)
    w_two = gathered[:, r_one:].reshape(n_blk * r_two, hidden)
    sending = lax.dynamic_index_in_dim(counts, position, 0, keepdims=False)
    x_rows, z_rows, y_rows = (paths, deltas, payoffs)
    total = jnp.sum(sending)
    mask = (jnp.arange(rows_dev, dtype=jnp.int32) < total).astype(jnp.float32)
    e_slope, g_one, e_aone, e_cone, g_two, h_one, e_atwo, grad_three = twin_terms(
        x_rows, z_rows, y_rows, mask, w_one, w_two, w_out
    )
    a_all = jnp.concatenate([x_rows, e_slope], axis=0).reshape(2 * rows_dev, chips, 2, r_one)
    c_all = jnp.concatenate([e_cone, h_one], axis=0).reshape(2 * rows_dev, chips, 2, r_two)
    b_me = jnp.concatenate([e_aone, g_one], axis=0)
    d_me = jnp.concatenate([g_two, e_atwo], axis=0)
    a_keep = lax.dynamic_index_in_dim(a_all, core, 2, keepdims=False)
    a_give = lax.dynamic_index_in_dim(a_all, 1 - core, 2, keepdims=False)
    c_keep = lax.dynamic_index_in_dim(c_all, core, 2, keepdims=False)
    c_give = lax.dynamic_index_in_dim(c_all, 1 - core, 2, keepdims=False)
    a_got = lax.ppermute(a_give, "blk", partner)
    b_got = lax.ppermute(b_me, "blk", partner)
    c_got = lax.ppermute(c_give, "blk", partner)
    d_got = lax.ppermute(d_me, "blk", partner)
    chip_out = grad_three + lax.ppermute(grad_three, "blk", partner)
    chip = position // 2
    spot = jnp.asarray(place, jnp.int32)[chip]
    ring_chips = jnp.asarray(snake, jnp.int32)[(spot + jnp.arange(chips, dtype=jnp.int32)) % chips]
    a_keep, a_got, c_keep, c_got = (
        jnp.take(f, ring_chips, axis=1) for f in (a_keep, a_got, c_keep, c_got)
    )
    part_one = slots_product(a_keep, b_me) + slots_product(a_got, b_got)
    part_two = slots_product(c_keep, d_me) + slots_product(c_got, d_got)
    own_row = jnp.arange(chips, dtype=jnp.int32)[:, None] == chip
    outs = jnp.where(own_row, chip_out[None, :], 0.0)
    summed = jnp.concatenate(
        [part_one, part_two, jnp.broadcast_to(outs, (chips,) + outs.shape)], axis=1
    )
    reduced = ring_reduce_scatter(summed, n_blk)
    grad_out = jnp.sum(reduced[r_one + r_two:], axis=0)
    grad_one = reduced[:r_one]
    grad_two = reduced[r_one:r_one + r_two]
    new_first = 0.8 * mom_first + 0.2 * normalized(grad_one)
    new_second = 0.8 * mom_second + 0.2 * normalized(grad_two)
    new_out = 0.8 * mom_out + 0.2 * normalized(grad_out)
    return (new_first, new_second, new_out)


def solution(mesh):
    in_specs = (
        P(("groups", "blk"), None),
        P(("groups", "blk"), None),
        P(("groups", "blk")),
        P("groups", None),
        P(("groups", "blk"), None),
        P(("groups", "blk"), None),
        P("groups"),
        P(("groups", "blk"), None),
        P(("groups", "blk"), None),
        P("groups"),
    )
    out_specs = (P(("groups", "blk"), None), P(("groups", "blk"), None), P("groups"))
    return jax.shard_map(
        functools.partial(per_device, n_blk=mesh.shape["blk"]),
        mesh=mesh, in_specs=in_specs, out_specs=out_specs, check_vma=False,
    )
```

```python
import functools

import jax
import jax.numpy as jnp
from jax import lax
from jax.sharding import PartitionSpec as P


def rows_product(left, right):
    return lax.dot_general(
        left, right, (((0,), (0,)), ((), ())), preferred_element_type=jnp.float32
    )


def twin_terms(x_rows, z_rows, y_rows, mask, w_one, w_two, w_three):
    w_outf = w_three.astype(jnp.float32)
    a_one = jnp.dot(x_rows, w_one, preferred_element_type=jnp.float32)
    s_one = jax.nn.sigmoid(a_one)
    h_one = jax.nn.softplus(a_one).astype(jnp.bfloat16)
    a_two = jnp.dot(h_one, w_two, preferred_element_type=jnp.float32)
    s_two = jax.nn.sigmoid(a_two)
    h_two = jax.nn.softplus(a_two)
    value = jnp.sum(h_two * w_outf[None, :], axis=1)
    g_two = (s_two * w_outf[None, :]).astype(jnp.bfloat16)
    c_one = lax.dot_general(
        g_two, w_two, (((1,), (1,)), ((), ())), preferred_element_type=jnp.float32
    )
    g_one = (c_one * s_one).astype(jnp.bfloat16)
    slope = lax.dot_general(
        g_one, w_one, (((1,), (1,)), ((), ())), preferred_element_type=jnp.float32
    )
    e_value = 2.0 * mask * (value - y_rows.astype(jnp.float32))
    e_slope = (2.0 * mask[:, None] * (slope - z_rows.astype(jnp.float32))).astype(jnp.bfloat16)
    e_gone = jnp.dot(e_slope, w_one, preferred_element_type=jnp.float32)
    e_cone = (e_gone * s_one).astype(jnp.bfloat16)
    e_sone = e_gone * c_one
    e_gtwo = jnp.dot(e_cone, w_two, preferred_element_type=jnp.float32)
    grad_three = jnp.sum(e_gtwo * s_two + e_value[:, None] * h_two, axis=0)
    e_atwo = (
        e_gtwo * w_outf[None, :] * s_two * (1.0 - s_two)
        + e_value[:, None] * w_outf[None, :] * s_two
    ).astype(jnp.bfloat16)
    e_hone = lax.dot_general(
        e_atwo, w_two, (((1,), (1,)), ((), ())), preferred_element_type=jnp.float32
    )
    e_aone = (e_sone * s_one * (1.0 - s_one) + e_hone * s_one).astype(jnp.bfloat16)
    return (e_slope, g_one, e_aone, e_cone, g_two, h_one, e_atwo, grad_three)


def normalized(grad):
    return grad / jnp.sqrt(jnp.mean(grad * grad, axis=-1, keepdims=True) + 1e-06)


def ring_plan(n_blk):
    chips = n_blk // 2
    snake = list(range(0, chips, 2)) + list(range(chips - 1, 0, -2))
    place = [0] * chips
    for p, q in enumerate(snake):
        place[q] = p
    cw = [(2 * snake[p] + c, 2 * snake[(p + 1) % chips] + c) for p in range(chips) for c in range(2)]
    ccw = [(b, a) for a, b in cw]
    partner = [(b, b ^ 1) for b in range(n_blk)]
    return chips, snake, place, cw, ccw, partner


def ring_all_gather(x, n_blk):
    chips, snake, place, cw, ccw, partner = ring_plan(n_blk)
    ahead = chips // 2
    behind = chips - 1 - ahead
    position = lax.axis_index("blk")
    core, chip = position % 2, position // 2
    spot = jnp.asarray(place, jnp.int32)[chip]
    rel = [None] * chips
    rel_other = [None] * chips
    rel[0] = x
    rel_other[0] = lax.ppermute(x, "blk", partner)
    left = right = x
    for s in range(1, ahead + 1):
        left = lax.ppermute(left, "blk", cw)
        rel[chips - s] = left
        rel_other[chips - s] = lax.ppermute(left, "blk", partner)
        if s <= behind:
            right = lax.ppermute(right, "blk", ccw)
            rel[s] = right
            rel_other[s] = lax.ppermute(right, "blk", partner)
    mine = jnp.stack(rel)
    other = jnp.stack(rel_other)
    both = jnp.concatenate([mine, other], axis=0)
    dest = jnp.arange(n_blk, dtype=jnp.int32)
    dest_chip, dest_core = dest // 2, dest % 2
    k = (jnp.asarray(place, jnp.int32)[dest_chip] - spot) % chips
    index = jnp.where(dest_core == core, 0, chips) + k
    return jnp.take(both, index, axis=0)


def ring_reduce_scatter(summed, n_blk):
    chips, snake, place, cw, ccw, partner = ring_plan(n_blk)
    ahead = chips // 2
    behind = chips - 1 - ahead
    acc = summed[ahead % chips]
    for s in range(1, ahead + 1):
        acc = lax.ppermute(acc, "blk", cw) + summed[(ahead - s) % chips]
    if behind:
        acc_back = summed[chips - behind]
        for s in range(1, behind + 1):
            acc_back = lax.ppermute(acc_back, "blk", ccw)
            if s < behind:
                acc_back = acc_back + summed[chips - behind + s]
        acc = acc + acc_back
    return acc


def slots_product(left, right):
    return lax.dot_general(
        left, right, (((0,), (0,)), ((), ())), preferred_element_type=jnp.float32
    )


def per_device(
    paths, deltas, payoffs, counts, w_first, w_second, w_out, mom_first, mom_second, mom_out,
    n_blk,
):
    chips, snake, place, cw, ccw, partner = ring_plan(n_blk)
    position = lax.axis_index("blk")
    core = position % 2
    rows_dev = paths.shape[0]
    r_one, r_two = w_first.shape[0], w_second.shape[0]
    hidden = w_first.shape[1]
    gathered = ring_all_gather(jnp.concatenate([w_first, w_second], axis=0), n_blk)
    w_one = gathered[:, :r_one].reshape(n_blk * r_one, hidden)
    w_two = gathered[:, r_one:].reshape(n_blk * r_two, hidden)
    sending = lax.dynamic_index_in_dim(counts, position, 0, keepdims=False)
    x_rows, z_rows, y_rows = (paths, deltas, payoffs)
    total = jnp.sum(sending)
    mask = (jnp.arange(rows_dev, dtype=jnp.int32) < total).astype(jnp.float32)
    e_slope, g_one, e_aone, e_cone, g_two, h_one, e_atwo, grad_three = twin_terms(
        x_rows, z_rows, y_rows, mask, w_one, w_two, w_out
    )
    chip = position // 2
    spot = jnp.asarray(place, jnp.int32)[chip]
    ring_chips = jnp.asarray(snake, jnp.int32)[(spot + jnp.arange(chips, dtype=jnp.int32)) % chips]

    def split_cols(f, width):
        f = jnp.take(f.reshape(rows_dev, chips, 2, width), ring_chips, axis=1)
        keep = lax.dynamic_index_in_dim(f, core, 2, keepdims=False)
        give = lax.dynamic_index_in_dim(f, 1 - core, 2, keepdims=False)
        return keep, lax.ppermute(give, "blk", partner)

    def swap(f):
        return lax.ppermute(f, "blk", partner)

    x_keep, x_got = split_cols(x_rows, r_one)
    h_keep, h_got = split_cols(h_one, r_two)
    g2_got = swap(g_two)
    g1_got = swap(g_one)
    ed_keep, ed_got = split_cols(e_slope, r_one)
    ec_keep, ec_got = split_cols(e_cone, r_two)
    ea2_got = swap(e_atwo)
    ea1_got = swap(e_aone)
    chip_out = grad_three + swap(grad_three)
    part_two = (
        slots_product(ec_keep, g_two) + slots_product(ec_got, g2_got)
        + slots_product(h_keep, e_atwo) + slots_product(h_got, ea2_got)
    )
    part_one = (
        slots_product(ed_keep, g_one) + slots_product(ed_got, g1_got)
        + slots_product(x_keep, e_aone) + slots_product(x_got, ea1_got)
    )
    own_row = jnp.arange(chips, dtype=jnp.int32)[:, None] == chip
    outs = jnp.where(own_row, chip_out[None, :], 0.0)
    summed = jnp.concatenate(
        [part_one, part_two, jnp.broadcast_to(outs, (chips,) + outs.shape)], axis=1
    )
    reduced = ring_reduce_scatter(summed, n_blk)
    grad_out = jnp.sum(reduced[r_one + r_two:], axis=0)
    grad_one = reduced[:r_one]
    grad_two = reduced[r_one:r_one + r_two]
    new_first = 0.8 * mom_first + 0.2 * normalized(grad_one)
    new_second = 0.8 * mom_second + 0.2 * normalized(grad_two)
    new_out = 0.8 * mom_out + 0.2 * normalized(grad_out)
    return (new_first, new_second, new_out)


def solution(mesh):
    in_specs = (
        P(("groups", "blk"), None),
        P(("groups", "blk"), None),
        P(("groups", "blk")),
        P("groups", None),
        P(("groups", "blk"), None),
        P(("groups", "blk"), None),
        P("groups"),
        P(("groups", "blk"), None),
        P(("groups", "blk"), None),
        P("groups"),
    )
    out_specs = (P(("groups", "blk"), None), P(("groups", "blk"), None), P("groups"))
    return jax.shard_map(
        functools.partial(per_device, n_blk=mesh.shape["blk"]),
        mesh=mesh, in_specs=in_specs, out_specs=out_specs, check_vma=False,
    )
```

```python
import functools

import jax
import jax.numpy as jnp
from jax import lax
from jax.sharding import PartitionSpec as P


def rows_product(left, right):
    return lax.dot_general(
        left, right, (((0,), (0,)), ((), ())), preferred_element_type=jnp.float32
    )


def twin_terms(x_rows, z_rows, y_rows, mask, w_one, w_two, w_three):
    w_outf = w_three.astype(jnp.float32)
    a_one = jnp.dot(x_rows, w_one, preferred_element_type=jnp.float32)
    s_one = jax.nn.sigmoid(a_one)
    h_one = jax.nn.softplus(a_one).astype(jnp.bfloat16)
    a_two = jnp.dot(h_one, w_two, preferred_element_type=jnp.float32)
    s_two = jax.nn.sigmoid(a_two)
    h_two = jax.nn.softplus(a_two)
    value = jnp.sum(h_two * w_outf[None, :], axis=1)
    g_two = (s_two * w_outf[None, :]).astype(jnp.bfloat16)
    c_one = lax.dot_general(
        g_two, w_two, (((1,), (1,)), ((), ())), preferred_element_type=jnp.float32
    )
    g_one = (c_one * s_one).astype(jnp.bfloat16)
    slope = lax.dot_general(
        g_one, w_one, (((1,), (1,)), ((), ())), preferred_element_type=jnp.float32
    )
    e_value = 2.0 * mask * (value - y_rows.astype(jnp.float32))
    e_slope = (2.0 * mask[:, None] * (slope - z_rows.astype(jnp.float32))).astype(jnp.bfloat16)
    e_gone = jnp.dot(e_slope, w_one, preferred_element_type=jnp.float32)
    e_cone = (e_gone * s_one).astype(jnp.bfloat16)
    e_sone = e_gone * c_one
    e_gtwo = jnp.dot(e_cone, w_two, preferred_element_type=jnp.float32)
    grad_three = jnp.sum(e_gtwo * s_two + e_value[:, None] * h_two, axis=0)
    e_atwo = (
        e_gtwo * w_outf[None, :] * s_two * (1.0 - s_two)
        + e_value[:, None] * w_outf[None, :] * s_two
    ).astype(jnp.bfloat16)
    e_hone = lax.dot_general(
        e_atwo, w_two, (((1,), (1,)), ((), ())), preferred_element_type=jnp.float32
    )
    e_aone = (e_sone * s_one * (1.0 - s_one) + e_hone * s_one).astype(jnp.bfloat16)
    return (e_slope, g_one, e_aone, e_cone, g_two, h_one, e_atwo, grad_three)


def normalized(grad):
    return grad / jnp.sqrt(jnp.mean(grad * grad, axis=-1, keepdims=True) + 1e-06)


def ring_plan(n_blk):
    chips = n_blk // 2
    snake = list(range(0, chips, 2)) + list(range(chips - 1, 0, -2))
    place = [0] * chips
    for p, q in enumerate(snake):
        place[q] = p
    cw = [(2 * snake[p] + c, 2 * snake[(p + 1) % chips] + c) for p in range(chips) for c in range(2)]
    ccw = [(b, a) for a, b in cw]
    partner = [(b, b ^ 1) for b in range(n_blk)]
    return chips, snake, place, cw, ccw, partner


def ring_all_gather(x, n_blk):
    chips, snake, place, cw, ccw, partner = ring_plan(n_blk)
    ahead = chips // 2
    behind = chips - 1 - ahead
    position = lax.axis_index("blk")
    core, chip = position % 2, position // 2
    spot = jnp.asarray(place, jnp.int32)[chip]
    rel = [None] * chips
    rel[0] = x
    left = right = x
    for s in range(1, ahead + 1):
        left = lax.ppermute(left, "blk", cw)
        rel[chips - s] = left
        if s <= behind:
            right = lax.ppermute(right, "blk", ccw)
            rel[s] = right
    mine = jnp.stack(rel)
    other = lax.ppermute(mine, "blk", partner)
    both = jnp.concatenate([mine, other], axis=0)
    dest = jnp.arange(n_blk, dtype=jnp.int32)
    dest_chip, dest_core = dest // 2, dest % 2
    k = (jnp.asarray(place, jnp.int32)[dest_chip] - spot) % chips
    index = jnp.where(dest_core == core, 0, chips) + k
    return jnp.take(both, index, axis=0)


def ring_reduce_scatter(summed, n_blk):
    chips, snake, place, cw, ccw, partner = ring_plan(n_blk)
    ahead = chips // 2
    behind = chips - 1 - ahead
    acc = summed[ahead % chips]
    for s in range(1, ahead + 1):
        acc = lax.ppermute(acc, "blk", cw) + summed[(ahead - s) % chips]
    if behind:
        acc_back = summed[chips - behind]
        for s in range(1, behind + 1):
            acc_back = lax.ppermute(acc_back, "blk", ccw)
            if s < behind:
                acc_back = acc_back + summed[chips - behind + s]
        acc = acc + acc_back
    return acc


def slots_product(left, right):
    return lax.dot_general(
        left, right, (((0,), (0,)), ((), ())), preferred_element_type=jnp.float32
    )


def per_device(
    paths, deltas, payoffs, counts, w_first, w_second, w_out, mom_first, mom_second, mom_out,
    n_blk,
):
    chips, snake, place, cw, ccw, partner = ring_plan(n_blk)
    position = lax.axis_index("blk")
    core = position % 2
    rows_dev = paths.shape[0]
    r_one, r_two = w_first.shape[0], w_second.shape[0]
    hidden = w_first.shape[1]
    gathered = ring_all_gather(jnp.concatenate([w_first, w_second], axis=0), n_blk)
    w_one = gathered[:, :r_one].reshape(n_blk * r_one, hidden)
    w_two = gathered[:, r_one:].reshape(n_blk * r_two, hidden)
    sending = lax.dynamic_index_in_dim(counts, position, 0, keepdims=False)
    x_rows, z_rows, y_rows = (paths, deltas, payoffs)
    total = jnp.sum(sending)
    mask = (jnp.arange(rows_dev, dtype=jnp.int32) < total).astype(jnp.float32)
    e_slope, g_one, e_aone, e_cone, g_two, h_one, e_atwo, grad_three = twin_terms(
        x_rows, z_rows, y_rows, mask, w_one, w_two, w_out
    )
    chip = position // 2
    spot = jnp.asarray(place, jnp.int32)[chip]
    ring_chips = jnp.asarray(snake, jnp.int32)[(spot + jnp.arange(chips, dtype=jnp.int32)) % chips]

    def split_cols(f, width):
        f = jnp.take(f.reshape(rows_dev, chips, 2, width), ring_chips, axis=1)
        keep = lax.dynamic_index_in_dim(f, core, 2, keepdims=False)
        give = lax.dynamic_index_in_dim(f, 1 - core, 2, keepdims=False)
        return keep, lax.ppermute(give, "blk", partner)

    def swap(f):
        return lax.ppermute(f, "blk", partner)

    x_keep, x_got = split_cols(x_rows, r_one)
    h_keep, h_got = split_cols(h_one, r_two)
    g2_got = swap(g_two)
    g1_got = swap(g_one)
    ed_keep, ed_got = split_cols(e_slope, r_one)
    ec_keep, ec_got = split_cols(e_cone, r_two)
    ea2_got = swap(e_atwo)
    ea1_got = swap(e_aone)
    chip_out = grad_three + swap(grad_three)
    part_two = (
        slots_product(ec_keep, g_two) + slots_product(ec_got, g2_got)
        + slots_product(h_keep, e_atwo) + slots_product(h_got, ea2_got)
    )
    part_one = (
        slots_product(ed_keep, g_one) + slots_product(ed_got, g1_got)
        + slots_product(x_keep, e_aone) + slots_product(x_got, ea1_got)
    )
    own_row = jnp.arange(chips, dtype=jnp.int32)[:, None] == chip
    outs = jnp.where(own_row, chip_out[None, :], 0.0)
    summed = jnp.concatenate(
        [part_one, part_two, jnp.broadcast_to(outs, (chips,) + outs.shape)], axis=1
    )
    reduced = ring_reduce_scatter(summed, n_blk)
    grad_out = jnp.sum(reduced[r_one + r_two:], axis=0)
    grad_one = reduced[:r_one]
    grad_two = reduced[r_one:r_one + r_two]
    new_first = 0.8 * mom_first + 0.2 * normalized(grad_one)
    new_second = 0.8 * mom_second + 0.2 * normalized(grad_two)
    new_out = 0.8 * mom_out + 0.2 * normalized(grad_out)
    return (new_first, new_second, new_out)


def solution(mesh):
    in_specs = (
        P(("groups", "blk"), None),
        P(("groups", "blk"), None),
        P(("groups", "blk")),
        P("groups", None),
        P(("groups", "blk"), None),
        P(("groups", "blk"), None),
        P("groups"),
        P(("groups", "blk"), None),
        P(("groups", "blk"), None),
        P("groups"),
    )
    out_specs = (P(("groups", "blk"), None), P(("groups", "blk"), None), P("groups"))
    return jax.shard_map(
        functools.partial(per_device, n_blk=mesh.shape["blk"]),
        mesh=mesh, in_specs=in_specs, out_specs=out_specs, check_vma=False,
    )
```

```python
import functools

import jax
import jax.numpy as jnp
from jax import lax
from jax.sharding import PartitionSpec as P


def rows_product(left, right):
    return lax.dot_general(
        left, right, (((0,), (0,)), ((), ())), preferred_element_type=jnp.float32
    )


def twin_terms(x_rows, z_rows, y_rows, mask, w_one, w_two, w_three):
    w_outf = w_three.astype(jnp.float32)
    a_one = jnp.dot(x_rows, w_one, preferred_element_type=jnp.float32)
    s_one = jax.nn.sigmoid(a_one)
    h_one = jax.nn.softplus(a_one).astype(jnp.bfloat16)
    a_two = jnp.dot(h_one, w_two, preferred_element_type=jnp.float32)
    s_two = jax.nn.sigmoid(a_two)
    h_two = jax.nn.softplus(a_two)
    value = jnp.sum(h_two * w_outf[None, :], axis=1)
    g_two = (s_two * w_outf[None, :]).astype(jnp.bfloat16)
    c_one = lax.dot_general(
        g_two, w_two, (((1,), (1,)), ((), ())), preferred_element_type=jnp.float32
    )
    g_one = (c_one * s_one).astype(jnp.bfloat16)
    slope = lax.dot_general(
        g_one, w_one, (((1,), (1,)), ((), ())), preferred_element_type=jnp.float32
    )
    e_value = 2.0 * mask * (value - y_rows.astype(jnp.float32))
    e_slope = (2.0 * mask[:, None] * (slope - z_rows.astype(jnp.float32))).astype(jnp.bfloat16)
    e_gone = jnp.dot(e_slope, w_one, preferred_element_type=jnp.float32)
    e_cone = (e_gone * s_one).astype(jnp.bfloat16)
    e_sone = e_gone * c_one
    e_gtwo = jnp.dot(e_cone, w_two, preferred_element_type=jnp.float32)
    grad_three = jnp.sum(e_gtwo * s_two + e_value[:, None] * h_two, axis=0)
    e_atwo = (
        e_gtwo * w_outf[None, :] * s_two * (1.0 - s_two)
        + e_value[:, None] * w_outf[None, :] * s_two
    ).astype(jnp.bfloat16)
    e_hone = lax.dot_general(
        e_atwo, w_two, (((1,), (1,)), ((), ())), preferred_element_type=jnp.float32
    )
    e_aone = (e_sone * s_one * (1.0 - s_one) + e_hone * s_one).astype(jnp.bfloat16)
    return (e_slope, g_one, e_aone, e_cone, g_two, h_one, e_atwo, grad_three)


def normalized(grad):
    return grad / jnp.sqrt(jnp.mean(grad * grad, axis=-1, keepdims=True) + 1e-06)


def ring_plan(n_blk):
    chips = n_blk // 2
    snake = list(range(0, chips, 2)) + list(range(chips - 1, 0, -2))
    place = [0] * chips
    for p, q in enumerate(snake):
        place[q] = p
    cw = [(2 * snake[p] + c, 2 * snake[(p + 1) % chips] + c) for p in range(chips) for c in range(2)]
    ccw = [(b, a) for a, b in cw]
    partner = [(b, b ^ 1) for b in range(n_blk)]
    return chips, snake, place, cw, ccw, partner


def ring_all_gather(x, n_blk):
    chips, snake, place, cw, ccw, partner = ring_plan(n_blk)
    ahead = chips // 2
    behind = chips - 1 - ahead
    position = lax.axis_index("blk")
    core, chip = position % 2, position // 2
    spot = jnp.asarray(place, jnp.int32)[chip]
    rel = [None] * chips
    rel[0] = x
    left = right = x
    for s in range(1, ahead + 1):
        left = lax.ppermute(left, "blk", cw)
        rel[chips - s] = left
        if s <= behind:
            right = lax.ppermute(right, "blk", ccw)
            rel[s] = right
    mine = jnp.stack(rel)
    other = lax.ppermute(mine, "blk", partner)
    both = jnp.concatenate([mine, other], axis=0)
    dest = jnp.arange(n_blk, dtype=jnp.int32)
    dest_chip, dest_core = dest // 2, dest % 2
    k = (jnp.asarray(place, jnp.int32)[dest_chip] - spot) % chips
    index = jnp.where(dest_core == core, 0, chips) + k
    return jnp.take(both, index, axis=0)


def ring_reduce_scatter(summed, n_blk):
    chips, snake, place, cw, ccw, partner = ring_plan(n_blk)
    ahead = chips // 2
    behind = chips - 1 - ahead
    rows = summed.shape[1]
    split = (rows // 16) * 8

    def forward(part, window):
        acc = part[window % chips]
        for s in range(1, window + 1):
            acc = lax.ppermute(acc, "blk", cw) + part[(window - s) % chips]
        return acc

    def backward(part, window):
        acc = part[chips - window]
        for s in range(1, window + 1):
            acc = lax.ppermute(acc, "blk", ccw)
            if s < window:
                acc = acc + part[chips - window + s]
        return acc

    def both_ways(part, one, other):
        total = forward(part, one)
        if other:
            total = total + backward(part, other)
        return total

    if split == 0 or behind == ahead:
        return both_ways(summed, ahead, behind)
    first = both_ways(summed[:, :split], ahead, behind)
    second = both_ways(summed[:, split:], behind, ahead)
    return jnp.concatenate([first, second], axis=0)


def slots_product(left, right):
    return lax.dot_general(
        left, right, (((0,), (0,)), ((), ())), preferred_element_type=jnp.float32
    )


def per_device(
    paths, deltas, payoffs, counts, w_first, w_second, w_out, mom_first, mom_second, mom_out,
    n_blk,
):
    chips, snake, place, cw, ccw, partner = ring_plan(n_blk)
    position = lax.axis_index("blk")
    core = position % 2
    rows_dev = paths.shape[0]
    r_one, r_two = w_first.shape[0], w_second.shape[0]
    hidden = w_first.shape[1]
    gathered = ring_all_gather(jnp.concatenate([w_first, w_second], axis=0), n_blk)
    w_one = gathered[:, :r_one].reshape(n_blk * r_one, hidden)
    w_two = gathered[:, r_one:].reshape(n_blk * r_two, hidden)
    sending = lax.dynamic_index_in_dim(counts, position, 0, keepdims=False)
    x_rows, z_rows, y_rows = (paths, deltas, payoffs)
    total = jnp.sum(sending)
    mask = (jnp.arange(rows_dev, dtype=jnp.int32) < total).astype(jnp.float32)
    e_slope, g_one, e_aone, e_cone, g_two, h_one, e_atwo, grad_three = twin_terms(
        x_rows, z_rows, y_rows, mask, w_one, w_two, w_out
    )
    chip = position // 2
    spot = jnp.asarray(place, jnp.int32)[chip]
    ring_chips = jnp.asarray(snake, jnp.int32)[(spot + jnp.arange(chips, dtype=jnp.int32)) % chips]

    def split_cols(f, width):
        f = jnp.take(f.reshape(rows_dev, chips, 2, width), ring_chips, axis=1)
        keep = lax.dynamic_index_in_dim(f, core, 2, keepdims=False)
        give = lax.dynamic_index_in_dim(f, 1 - core, 2, keepdims=False)
        return keep, lax.ppermute(give, "blk", partner)

    def swap(f):
        return lax.ppermute(f, "blk", partner)

    x_keep, x_got = split_cols(x_rows, r_one)
    h_keep, h_got = split_cols(h_one, r_two)
    g2_got = swap(g_two)
    g1_got = swap(g_one)
    ed_keep, ed_got = split_cols(e_slope, r_one)
    ec_keep, ec_got = split_cols(e_cone, r_two)
    ea2_got = swap(e_atwo)
    ea1_got = swap(e_aone)
    chip_out = grad_three + swap(grad_three)
    part_two = (
        slots_product(ec_keep, g_two) + slots_product(ec_got, g2_got)
        + slots_product(h_keep, e_atwo) + slots_product(h_got, ea2_got)
    )
    part_one = (
        slots_product(ed_keep, g_one) + slots_product(ed_got, g1_got)
        + slots_product(x_keep, e_aone) + slots_product(x_got, ea1_got)
    )
    own_row = jnp.arange(chips, dtype=jnp.int32)[:, None] == chip
    outs = jnp.where(own_row, chip_out[None, :], 0.0)
    summed = jnp.concatenate(
        [part_one, part_two, jnp.broadcast_to(outs, (chips,) + outs.shape)], axis=1
    )
    reduced = ring_reduce_scatter(summed, n_blk)
    grad_out = jnp.sum(reduced[r_one + r_two:], axis=0)
    grad_one = reduced[:r_one]
    grad_two = reduced[r_one:r_one + r_two]
    new_first = 0.8 * mom_first + 0.2 * normalized(grad_one)
    new_second = 0.8 * mom_second + 0.2 * normalized(grad_two)
    new_out = 0.8 * mom_out + 0.2 * normalized(grad_out)
    return (new_first, new_second, new_out)


def solution(mesh):
    in_specs = (
        P(("groups", "blk"), None),
        P(("groups", "blk"), None),
        P(("groups", "blk")),
        P("groups", None),
        P(("groups", "blk"), None),
        P(("groups", "blk"), None),
        P("groups"),
        P(("groups", "blk"), None),
        P(("groups", "blk"), None),
        P("groups"),
    )
    out_specs = (P(("groups", "blk"), None), P(("groups", "blk"), None), P("groups"))
    return jax.shard_map(
        functools.partial(per_device, n_blk=mesh.shape["blk"]),
        mesh=mesh, in_specs=in_specs, out_specs=out_specs, check_vma=False,
    )
```

```python
import functools

import jax
import jax.numpy as jnp
from jax import lax
from jax.sharding import PartitionSpec as P


def rows_product(left, right):
    return lax.dot_general(
        left, right, (((0,), (0,)), ((), ())), preferred_element_type=jnp.float32
    )


def twin_terms(x_rows, z_rows, y_rows, mask, w_one, w_two, w_three):
    w_outf = w_three.astype(jnp.float32)
    a_one = jnp.dot(x_rows, w_one, preferred_element_type=jnp.float32)
    s_one = jax.nn.sigmoid(a_one)
    h_one = jax.nn.softplus(a_one).astype(jnp.bfloat16)
    a_two = jnp.dot(h_one, w_two, preferred_element_type=jnp.float32)
    s_two = jax.nn.sigmoid(a_two)
    h_two = jax.nn.softplus(a_two)
    value = jnp.sum(h_two * w_outf[None, :], axis=1)
    g_two = (s_two * w_outf[None, :]).astype(jnp.bfloat16)
    c_one = lax.dot_general(
        g_two, w_two, (((1,), (1,)), ((), ())), preferred_element_type=jnp.float32
    )
    g_one = (c_one * s_one).astype(jnp.bfloat16)
    slope = lax.dot_general(
        g_one, w_one, (((1,), (1,)), ((), ())), preferred_element_type=jnp.float32
    )
    e_value = 2.0 * mask * (value - y_rows.astype(jnp.float32))
    e_slope = (2.0 * mask[:, None] * (slope - z_rows.astype(jnp.float32))).astype(jnp.bfloat16)
    e_gone = jnp.dot(e_slope, w_one, preferred_element_type=jnp.float32)
    e_cone = (e_gone * s_one).astype(jnp.bfloat16)
    e_sone = e_gone * c_one
    e_gtwo = jnp.dot(e_cone, w_two, preferred_element_type=jnp.float32)
    grad_three = jnp.sum(e_gtwo * s_two + e_value[:, None] * h_two, axis=0)
    e_atwo = (
        e_gtwo * w_outf[None, :] * s_two * (1.0 - s_two)
        + e_value[:, None] * w_outf[None, :] * s_two
    ).astype(jnp.bfloat16)
    e_hone = lax.dot_general(
        e_atwo, w_two, (((1,), (1,)), ((), ())), preferred_element_type=jnp.float32
    )
    e_aone = (e_sone * s_one * (1.0 - s_one) + e_hone * s_one).astype(jnp.bfloat16)
    return (e_slope, g_one, e_aone, e_cone, g_two, h_one, e_atwo, grad_three)


def normalized(grad):
    return grad / jnp.sqrt(jnp.mean(grad * grad, axis=-1, keepdims=True) + 1e-06)


def ring_plan(n_blk):
    chips = n_blk // 2
    snake = list(range(0, chips, 2)) + list(range(chips - 1, 0, -2))
    place = [0] * chips
    for p, q in enumerate(snake):
        place[q] = p
    cw = [(2 * snake[p] + c, 2 * snake[(p + 1) % chips] + c) for p in range(chips) for c in range(2)]
    ccw = [(b, a) for a, b in cw]
    partner = [(b, b ^ 1) for b in range(n_blk)]
    return chips, snake, place, cw, ccw, partner


def ring_all_gather(x, n_blk):
    chips, snake, place, cw, ccw, partner = ring_plan(n_blk)
    ahead = chips // 2
    behind = chips - 1 - ahead
    position = lax.axis_index("blk")
    core, chip = position % 2, position // 2
    spot = jnp.asarray(place, jnp.int32)[chip]
    rel = [None] * chips
    rel[0] = x
    left = right = x
    for s in range(1, ahead + 1):
        left = lax.ppermute(left, "blk", cw)
        rel[chips - s] = left
        if s <= behind:
            right = lax.ppermute(right, "blk", ccw)
            rel[s] = right
    mine = jnp.stack(rel)
    other = lax.ppermute(mine, "blk", partner)
    both = jnp.concatenate([mine, other], axis=0)
    dest = jnp.arange(n_blk, dtype=jnp.int32)
    dest_chip, dest_core = dest // 2, dest % 2
    k = (jnp.asarray(place, jnp.int32)[dest_chip] - spot) % chips
    index = jnp.where(dest_core == core, 0, chips) + k
    return jnp.take(both, index, axis=0)


def ring_reduce_scatter(summed, n_blk):
    chips, snake, place, cw, ccw, partner = ring_plan(n_blk)
    ahead = chips // 2
    behind = chips - 1 - ahead
    rows = summed.shape[1]
    split = (rows // 16) * 8

    def forward(part, window):
        acc = part[window % chips]
        for s in range(1, window + 1):
            acc = lax.ppermute(acc, "blk", cw) + part[(window - s) % chips]
        return acc

    def backward(part, window):
        acc = part[chips - window]
        for s in range(1, window + 1):
            acc = lax.ppermute(acc, "blk", ccw)
            if s < window:
                acc = acc + part[chips - window + s]
        return acc

    def both_ways(part, one, other):
        total = forward(part, one)
        if other:
            total = total + backward(part, other)
        return total

    if split == 0 or behind == ahead:
        return both_ways(summed, ahead, behind)
    first = both_ways(summed[:, :split], ahead, behind)
    second = both_ways(summed[:, split:], behind, ahead)
    return jnp.concatenate([first, second], axis=0)


def slots_product(left, right):
    return lax.dot_general(
        left, right, (((0,), (0,)), ((), ())), preferred_element_type=jnp.float32
    )


def per_device(
    paths, deltas, payoffs, counts, w_first, w_second, w_out, mom_first, mom_second, mom_out,
    n_blk,
):
    chips, snake, place, cw, ccw, partner = ring_plan(n_blk)
    position = lax.axis_index("blk")
    core = position % 2
    rows_dev = paths.shape[0]
    r_one, r_two = w_first.shape[0], w_second.shape[0]
    hidden = w_first.shape[1]
    gathered = ring_all_gather(jnp.concatenate([w_first, w_second], axis=0), n_blk)
    w_one = gathered[:, :r_one].reshape(n_blk * r_one, hidden)
    w_two = gathered[:, r_one:].reshape(n_blk * r_two, hidden)
    sending = lax.dynamic_index_in_dim(counts, position, 0, keepdims=False)
    x_rows, z_rows, y_rows = (paths, deltas, payoffs)
    total = jnp.sum(sending)
    mask = (jnp.arange(rows_dev, dtype=jnp.int32) < total).astype(jnp.float32)
    e_slope, g_one, e_aone, e_cone, g_two, h_one, e_atwo, grad_three = twin_terms(
        x_rows, z_rows, y_rows, mask, w_one, w_two, w_out
    )
    chip = position // 2
    spot = jnp.asarray(place, jnp.int32)[chip]
    ring_chips = jnp.asarray(snake, jnp.int32)[(spot + jnp.arange(chips, dtype=jnp.int32)) % chips]

    def split_cols(f, width):
        f = jnp.take(f.reshape(rows_dev, chips, 2, width), ring_chips, axis=1)
        keep = lax.dynamic_index_in_dim(f, core, 2, keepdims=False)
        give = lax.dynamic_index_in_dim(f, 1 - core, 2, keepdims=False)
        return keep, lax.ppermute(give, "blk", partner)

    def swap(f):
        return lax.ppermute(f, "blk", partner)

    x_keep, x_got = split_cols(x_rows, r_one)
    h_keep, h_got = split_cols(h_one, r_two)
    g2_got = swap(g_two)
    g1_got = swap(g_one)
    ed_keep, ed_got = split_cols(e_slope, r_one)
    ec_keep, ec_got = split_cols(e_cone, r_two)
    ea2_got = swap(e_atwo)
    ea1_got = swap(e_aone)
    chip_out = grad_three + swap(grad_three)
    part_two = (
        slots_product(ec_keep, g_two) + slots_product(ec_got, g2_got)
        + slots_product(h_keep, e_atwo) + slots_product(h_got, ea2_got)
    )
    part_one = (
        slots_product(ed_keep, g_one) + slots_product(ed_got, g1_got)
        + slots_product(x_keep, e_aone) + slots_product(x_got, ea1_got)
    )
    own_row = jnp.arange(chips, dtype=jnp.int32)[:, None] == chip
    outs = jnp.where(own_row, chip_out[None, :], 0.0)
    summed = jnp.concatenate(
        [part_two, jnp.broadcast_to(outs, (chips,) + outs.shape), part_one], axis=1
    )
    reduced = ring_reduce_scatter(summed, n_blk)
    grad_two = reduced[:r_two]
    grad_out = jnp.sum(reduced[r_two:r_two + chips], axis=0)
    grad_one = reduced[r_two + chips:]
    new_first = 0.8 * mom_first + 0.2 * normalized(grad_one)
    new_second = 0.8 * mom_second + 0.2 * normalized(grad_two)
    new_out = 0.8 * mom_out + 0.2 * normalized(grad_out)
    return (new_first, new_second, new_out)


def solution(mesh):
    in_specs = (
        P(("groups", "blk"), None),
        P(("groups", "blk"), None),
        P(("groups", "blk")),
        P("groups", None),
        P(("groups", "blk"), None),
        P(("groups", "blk"), None),
        P("groups"),
        P(("groups", "blk"), None),
        P(("groups", "blk"), None),
        P("groups"),
    )
    out_specs = (P(("groups", "blk"), None), P(("groups", "blk"), None), P("groups"))
    return jax.shard_map(
        functools.partial(per_device, n_blk=mesh.shape["blk"]),
        mesh=mesh, in_specs=in_specs, out_specs=out_specs, check_vma=False,
    )
```

```python
import functools

import jax
import jax.numpy as jnp
from jax import lax
from jax.sharding import PartitionSpec as P


def rows_product(left, right):
    return lax.dot_general(
        left, right, (((0,), (0,)), ((), ())), preferred_element_type=jnp.float32
    )


def twin_terms(x_rows, z_rows, y_rows, mask, w_one, w_two, w_three):
    w_outf = w_three.astype(jnp.float32)
    a_one = jnp.dot(x_rows, w_one, preferred_element_type=jnp.float32)
    s_one = jax.nn.sigmoid(a_one)
    h_one = jax.nn.softplus(a_one).astype(jnp.bfloat16)
    a_two = jnp.dot(h_one, w_two, preferred_element_type=jnp.float32)
    s_two = jax.nn.sigmoid(a_two)
    h_two = jax.nn.softplus(a_two)
    value = jnp.sum(h_two * w_outf[None, :], axis=1)
    g_two = (s_two * w_outf[None, :]).astype(jnp.bfloat16)
    c_one = lax.dot_general(
        g_two, w_two, (((1,), (1,)), ((), ())), preferred_element_type=jnp.float32
    )
    g_one = (c_one * s_one).astype(jnp.bfloat16)
    slope = lax.dot_general(
        g_one, w_one, (((1,), (1,)), ((), ())), preferred_element_type=jnp.float32
    )
    e_value = 2.0 * mask * (value - y_rows.astype(jnp.float32))
    e_slope = (2.0 * mask[:, None] * (slope - z_rows.astype(jnp.float32))).astype(jnp.bfloat16)
    e_gone = jnp.dot(e_slope, w_one, preferred_element_type=jnp.float32)
    e_cone = (e_gone * s_one).astype(jnp.bfloat16)
    e_sone = e_gone * c_one
    e_gtwo = jnp.dot(e_cone, w_two, preferred_element_type=jnp.float32)
    grad_three = jnp.sum(e_gtwo * s_two + e_value[:, None] * h_two, axis=0)
    e_atwo = (
        e_gtwo * w_outf[None, :] * s_two * (1.0 - s_two)
        + e_value[:, None] * w_outf[None, :] * s_two
    ).astype(jnp.bfloat16)
    e_hone = lax.dot_general(
        e_atwo, w_two, (((1,), (1,)), ((), ())), preferred_element_type=jnp.float32
    )
    e_aone = (e_sone * s_one * (1.0 - s_one) + e_hone * s_one).astype(jnp.bfloat16)
    return (e_slope, g_one, e_aone, e_cone, g_two, h_one, e_atwo, grad_three)


def normalized(grad):
    return grad / jnp.sqrt(jnp.mean(grad * grad, axis=-1, keepdims=True) + 1e-06)


def ring_plan(n_blk):
    chips = n_blk // 2
    snake = list(range(0, chips, 2)) + list(range(chips - 1, 0, -2))
    place = [0] * chips
    for p, q in enumerate(snake):
        place[q] = p
    cw = [(2 * snake[p] + c, 2 * snake[(p + 1) % chips] + c) for p in range(chips) for c in range(2)]
    ccw = [(b, a) for a, b in cw]
    partner = [(b, b ^ 1) for b in range(n_blk)]
    return chips, snake, place, cw, ccw, partner


def ring_all_gather(x, n_blk):
    chips, snake, place, cw, ccw, partner = ring_plan(n_blk)
    ahead = chips // 2
    behind = chips - 1 - ahead
    position = lax.axis_index("blk")
    core, chip = position % 2, position // 2
    spot = jnp.asarray(place, jnp.int32)[chip]
    rel = [None] * chips
    rel[0] = x
    left = right = x
    for s in range(1, ahead + 1):
        left = lax.ppermute(left, "blk", cw)
        rel[chips - s] = left
        if s <= behind:
            right = lax.ppermute(right, "blk", ccw)
            rel[s] = right
    half = ahead // 2
    early = [0] + [chips - s for s in range(1, half + 1)] + [s for s in range(1, min(half, behind) + 1)]
    late = [k for k in range(chips) if k not in early]
    slot = [0] * chips
    for i, k in enumerate(early + late):
        slot[k] = i
    mine = jnp.stack(rel)
    other_early = lax.ppermute(jnp.stack([rel[k] for k in early]), "blk", partner)
    other_late = lax.ppermute(jnp.stack([rel[k] for k in late]), "blk", partner)
    both = jnp.concatenate([mine, other_early, other_late], axis=0)
    dest = jnp.arange(n_blk, dtype=jnp.int32)
    dest_chip, dest_core = dest // 2, dest % 2
    k = (jnp.asarray(place, jnp.int32)[dest_chip] - spot) % chips
    index = jnp.where(dest_core == core, k, chips + jnp.asarray(slot, jnp.int32)[k])
    return jnp.take(both, index, axis=0)


def ring_reduce_scatter(summed, n_blk):
    chips, snake, place, cw, ccw, partner = ring_plan(n_blk)
    ahead = chips // 2
    behind = chips - 1 - ahead
    rows = summed.shape[1]
    split = (rows // 16) * 8

    def forward(part, window):
        acc = part[window % chips]
        for s in range(1, window + 1):
            acc = lax.ppermute(acc, "blk", cw) + part[(window - s) % chips]
        return acc

    def backward(part, window):
        acc = part[chips - window]
        for s in range(1, window + 1):
            acc = lax.ppermute(acc, "blk", ccw)
            if s < window:
                acc = acc + part[chips - window + s]
        return acc

    def both_ways(part, one, other):
        total = forward(part, one)
        if other:
            total = total + backward(part, other)
        return total

    if split == 0 or behind == ahead:
        return both_ways(summed, ahead, behind)
    first = both_ways(summed[:, :split], ahead, behind)
    second = both_ways(summed[:, split:], behind, ahead)
    return jnp.concatenate([first, second], axis=0)


def slots_product(left, right):
    return lax.dot_general(
        left, right, (((0,), (0,)), ((), ())), preferred_element_type=jnp.float32
    )


def per_device(
    paths, deltas, payoffs, counts, w_first, w_second, w_out, mom_first, mom_second, mom_out,
    n_blk,
):
    chips, snake, place, cw, ccw, partner = ring_plan(n_blk)
    position = lax.axis_index("blk")
    core = position % 2
    rows_dev = paths.shape[0]
    r_one, r_two = w_first.shape[0], w_second.shape[0]
    hidden = w_first.shape[1]
    gathered = ring_all_gather(jnp.concatenate([w_first, w_second], axis=0), n_blk)
    w_one = gathered[:, :r_one].reshape(n_blk * r_one, hidden)
    w_two = gathered[:, r_one:].reshape(n_blk * r_two, hidden)
    sending = lax.dynamic_index_in_dim(counts, position, 0, keepdims=False)
    x_rows, z_rows, y_rows = (paths, deltas, payoffs)
    total = jnp.sum(sending)
    mask = (jnp.arange(rows_dev, dtype=jnp.int32) < total).astype(jnp.float32)
    e_slope, g_one, e_aone, e_cone, g_two, h_one, e_atwo, grad_three = twin_terms(
        x_rows, z_rows, y_rows, mask, w_one, w_two, w_out
    )
    chip = position // 2
    spot = jnp.asarray(place, jnp.int32)[chip]
    ring_chips = jnp.asarray(snake, jnp.int32)[(spot + jnp.arange(chips, dtype=jnp.int32)) % chips]

    def split_cols(f, width):
        f = jnp.take(f.reshape(rows_dev, chips, 2, width), ring_chips, axis=1)
        keep = lax.dynamic_index_in_dim(f, core, 2, keepdims=False)
        give = lax.dynamic_index_in_dim(f, 1 - core, 2, keepdims=False)
        return keep, lax.ppermute(give, "blk", partner)

    def swap(f):
        return lax.ppermute(f, "blk", partner)

    x_keep, x_got = split_cols(x_rows, r_one)
    h_keep, h_got = split_cols(h_one, r_two)
    g2_got = swap(g_two)
    g1_got = swap(g_one)
    ed_keep, ed_got = split_cols(e_slope, r_one)
    ec_keep, ec_got = split_cols(e_cone, r_two)
    ea2_got = swap(e_atwo)
    ea1_got = swap(e_aone)
    chip_out = grad_three + swap(grad_three)
    part_two = (
        slots_product(ec_keep, g_two) + slots_product(ec_got, g2_got)
        + slots_product(h_keep, e_atwo) + slots_product(h_got, ea2_got)
    )
    part_one = (
        slots_product(ed_keep, g_one) + slots_product(ed_got, g1_got)
        + slots_product(x_keep, e_aone) + slots_product(x_got, ea1_got)
    )
    own_row = jnp.arange(chips, dtype=jnp.int32)[:, None] == chip
    outs = jnp.where(own_row, chip_out[None, :], 0.0)
    summed = jnp.concatenate(
        [part_two, jnp.broadcast_to(outs, (chips,) + outs.shape), part_one], axis=1
    )
    reduced = ring_reduce_scatter(summed, n_blk)
    grad_two = reduced[:r_two]
    grad_out = jnp.sum(reduced[r_two:r_two + chips], axis=0)
    grad_one = reduced[r_two + chips:]
    new_first = 0.8 * mom_first + 0.2 * normalized(grad_one)
    new_second = 0.8 * mom_second + 0.2 * normalized(grad_two)
    new_out = 0.8 * mom_out + 0.2 * normalized(grad_out)
    return (new_first, new_second, new_out)


def solution(mesh):
    in_specs = (
        P(("groups", "blk"), None),
        P(("groups", "blk"), None),
        P(("groups", "blk")),
        P("groups", None),
        P(("groups", "blk"), None),
        P(("groups", "blk"), None),
        P("groups"),
        P(("groups", "blk"), None),
        P(("groups", "blk"), None),
        P("groups"),
    )
    out_specs = (P(("groups", "blk"), None), P(("groups", "blk"), None), P("groups"))
    return jax.shard_map(
        functools.partial(per_device, n_blk=mesh.shape["blk"]),
        mesh=mesh, in_specs=in_specs, out_specs=out_specs, check_vma=False,
    )
```

```python
import functools

import jax
import jax.numpy as jnp
from jax import lax
from jax.experimental import pallas as pl
from jax.experimental.pallas import tpu as pltpu
from jax.sharding import PartitionSpec as P


def rows_product(left, right):
    return lax.dot_general(
        left, right, (((0,), (0,)), ((), ())), preferred_element_type=jnp.float32
    )


def twin_terms(x_rows, z_rows, y_rows, mask, w_one, w_two, w_three):
    w_outf = w_three.astype(jnp.float32)
    a_one = jnp.dot(x_rows, w_one, preferred_element_type=jnp.float32)
    s_one = jax.nn.sigmoid(a_one)
    h_one = jax.nn.softplus(a_one).astype(jnp.bfloat16)
    a_two = jnp.dot(h_one, w_two, preferred_element_type=jnp.float32)
    s_two = jax.nn.sigmoid(a_two)
    h_two = jax.nn.softplus(a_two)
    value = jnp.sum(h_two * w_outf[None, :], axis=1)
    g_two = (s_two * w_outf[None, :]).astype(jnp.bfloat16)
    c_one = lax.dot_general(
        g_two, w_two, (((1,), (1,)), ((), ())), preferred_element_type=jnp.float32
    )
    g_one = (c_one * s_one).astype(jnp.bfloat16)
    slope = lax.dot_general(
        g_one, w_one, (((1,), (1,)), ((), ())), preferred_element_type=jnp.float32
    )
    e_value = 2.0 * mask * (value - y_rows.astype(jnp.float32))
    e_slope = (2.0 * mask[:, None] * (slope - z_rows.astype(jnp.float32))).astype(jnp.bfloat16)
    e_gone = jnp.dot(e_slope, w_one, preferred_element_type=jnp.float32)
    e_cone = (e_gone * s_one).astype(jnp.bfloat16)
    e_sone = e_gone * c_one
    e_gtwo = jnp.dot(e_cone, w_two, preferred_element_type=jnp.float32)
    grad_three = jnp.sum(e_gtwo * s_two + e_value[:, None] * h_two, axis=0)
    e_atwo = (
        e_gtwo * w_outf[None, :] * s_two * (1.0 - s_two)
        + e_value[:, None] * w_outf[None, :] * s_two
    ).astype(jnp.bfloat16)
    e_hone = lax.dot_general(
        e_atwo, w_two, (((1,), (1,)), ((), ())), preferred_element_type=jnp.float32
    )
    e_aone = (e_sone * s_one * (1.0 - s_one) + e_hone * s_one).astype(jnp.bfloat16)
    return (e_slope, g_one, e_aone, e_cone, g_two, h_one, e_atwo, grad_three)


def _nt(left, right):
    return lax.dot_general(left, right, (((1,), (1,)), ((), ())), preferred_element_type=jnp.float32)


def _sigmoid(a):
    return 1.0 / (1.0 + jnp.exp(-a))


def _softplus(a):
    return jnp.maximum(a, 0.0) + jnp.log1p(jnp.exp(-jnp.abs(a)))


def twin_body(x_ref, z_ref, y_ref, m_ref, w1_ref, w2_ref, wo_ref,
              es_ref, g1_ref, ea1_ref, ec1_ref, g2_ref, h1_ref, ea2_ref, g3_ref):
    w1 = w1_ref[...]
    w2 = w2_ref[...]
    wo = wo_ref[...]
    mask = m_ref[...]
    a1 = jnp.dot(x_ref[...], w1, preferred_element_type=jnp.float32)
    s1 = _sigmoid(a1)
    h1 = _softplus(a1).astype(jnp.bfloat16)
    a2 = jnp.dot(h1, w2, preferred_element_type=jnp.float32)
    s2 = _sigmoid(a2)
    h2 = _softplus(a2)
    value = jnp.sum(h2 * wo, axis=1, keepdims=True)
    g2 = (s2 * wo).astype(jnp.bfloat16)
    c1 = _nt(g2, w2)
    g1 = (c1 * s1).astype(jnp.bfloat16)
    slope = _nt(g1, w1)
    ev = 2.0 * mask * (value - y_ref[...])
    ed = (2.0 * mask * (slope - z_ref[...].astype(jnp.float32))).astype(jnp.bfloat16)
    eg1 = jnp.dot(ed, w1, preferred_element_type=jnp.float32)
    ec1 = (eg1 * s1).astype(jnp.bfloat16)
    es1 = eg1 * c1
    eg2 = jnp.dot(ec1, w2, preferred_element_type=jnp.float32)
    g3_ref[...] = jnp.sum(eg2 * s2 + ev * h2, axis=0, keepdims=True)
    ea2 = (eg2 * wo * s2 * (1.0 - s2) + ev * wo * s2).astype(jnp.bfloat16)
    eh1 = _nt(ea2, w2)
    ea1 = (es1 * s1 * (1.0 - s1) + eh1 * s1).astype(jnp.bfloat16)
    es_ref[...] = ed
    g1_ref[...] = g1
    ea1_ref[...] = ea1
    ec1_ref[...] = ec1
    g2_ref[...] = g2
    h1_ref[...] = h1
    ea2_ref[...] = ea2


def twin_fused(x_rows, z_rows, y_rows, mask, w_one, w_two, w_three):
    rows, assets = x_rows.shape
    hidden = w_one.shape[1]
    bf, f32 = jnp.bfloat16, jnp.float32
    shapes = (
        jax.ShapeDtypeStruct((rows, assets), bf),
        jax.ShapeDtypeStruct((rows, hidden), bf),
        jax.ShapeDtypeStruct((rows, hidden), bf),
        jax.ShapeDtypeStruct((rows, hidden), bf),
        jax.ShapeDtypeStruct((rows, hidden), bf),
        jax.ShapeDtypeStruct((rows, hidden), bf),
        jax.ShapeDtypeStruct((rows, hidden), bf),
        jax.ShapeDtypeStruct((1, hidden), f32),
    )
    vmem = pl.BlockSpec(memory_space=pltpu.VMEM)
    flops = 2 * rows * hidden * (3 * assets + 4 * hidden)
    e_slope, g_one, e_aone, e_cone, g_two, h_one, e_atwo, grad_three = pl.pallas_call(
        twin_body,
        out_shape=shapes,
        in_specs=[vmem] * 7,
        out_specs=[vmem] * 8,
        cost_estimate=pl.CostEstimate(
            flops=flops, transcendentals=6 * rows * hidden,
            bytes_accessed=2 * (assets + 2 * hidden) * hidden + 16 * rows * hidden),
    )(x_rows, z_rows, y_rows.astype(f32)[:, None], mask[:, None], w_one, w_two,
      w_three.astype(f32)[None, :])
    return (e_slope, g_one, e_aone, e_cone, g_two, h_one, e_atwo, grad_three[0])


def normalized(grad):
    return grad / jnp.sqrt(jnp.mean(grad * grad, axis=-1, keepdims=True) + 1e-06)


def ring_plan(n_blk):
    chips = n_blk // 2
    snake = list(range(0, chips, 2)) + list(range(chips - 1, 0, -2))
    place = [0] * chips
    for p, q in enumerate(snake):
        place[q] = p
    cw = [(2 * snake[p] + c, 2 * snake[(p + 1) % chips] + c) for p in range(chips) for c in range(2)]
    ccw = [(b, a) for a, b in cw]
    partner = [(b, b ^ 1) for b in range(n_blk)]
    return chips, snake, place, cw, ccw, partner


def ring_all_gather(x, n_blk):
    chips, snake, place, cw, ccw, partner = ring_plan(n_blk)
    ahead = chips // 2
    behind = chips - 1 - ahead
    position = lax.axis_index("blk")
    core, chip = position % 2, position // 2
    spot = jnp.asarray(place, jnp.int32)[chip]
    rel = [None] * chips
    rel[0] = x
    left = right = x
    for s in range(1, ahead + 1):
        left = lax.ppermute(left, "blk", cw)
        rel[chips - s] = left
        if s <= behind:
            right = lax.ppermute(right, "blk", ccw)
            rel[s] = right
    mine = jnp.stack(rel)
    other = lax.ppermute(mine, "blk", partner)
    both = jnp.concatenate([mine, other], axis=0)
    dest = jnp.arange(n_blk, dtype=jnp.int32)
    dest_chip, dest_core = dest // 2, dest % 2
    k = (jnp.asarray(place, jnp.int32)[dest_chip] - spot) % chips
    index = jnp.where(dest_core == core, 0, chips) + k
    return jnp.take(both, index, axis=0)


def ring_reduce_scatter(summed, n_blk):
    chips, snake, place, cw, ccw, partner = ring_plan(n_blk)
    ahead = chips // 2
    behind = chips - 1 - ahead
    rows = summed.shape[1]
    split = (rows // 16) * 8

    def forward(part, window):
        acc = part[window % chips]
        for s in range(1, window + 1):
            acc = lax.ppermute(acc, "blk", cw) + part[(window - s) % chips]
        return acc

    def backward(part, window):
        acc = part[chips - window]
        for s in range(1, window + 1):
            acc = lax.ppermute(acc, "blk", ccw)
            if s < window:
                acc = acc + part[chips - window + s]
        return acc

    def both_ways(part, one, other):
        total = forward(part, one)
        if other:
            total = total + backward(part, other)
        return total

    if split == 0 or behind == ahead:
        return both_ways(summed, ahead, behind)
    first = both_ways(summed[:, :split], ahead, behind)
    second = both_ways(summed[:, split:], behind, ahead)
    return jnp.concatenate([first, second], axis=0)


def slots_product(left, right):
    return lax.dot_general(
        left, right, (((0,), (0,)), ((), ())), preferred_element_type=jnp.float32
    )


def per_device(
    paths, deltas, payoffs, counts, w_first, w_second, w_out, mom_first, mom_second, mom_out,
    n_blk,
):
    chips, snake, place, cw, ccw, partner = ring_plan(n_blk)
    position = lax.axis_index("blk")
    core = position % 2
    rows_dev = paths.shape[0]
    r_one, r_two = w_first.shape[0], w_second.shape[0]
    hidden = w_first.shape[1]
    gathered = ring_all_gather(jnp.concatenate([w_first, w_second], axis=0), n_blk)
    w_one = gathered[:, :r_one].reshape(n_blk * r_one, hidden)
    w_two = gathered[:, r_one:].reshape(n_blk * r_two, hidden)
    sending = lax.dynamic_index_in_dim(counts, position, 0, keepdims=False)
    x_rows, z_rows, y_rows = (paths, deltas, payoffs)
    total = jnp.sum(sending)
    mask = (jnp.arange(rows_dev, dtype=jnp.int32) < total).astype(jnp.float32)
    e_slope, g_one, e_aone, e_cone, g_two, h_one, e_atwo, grad_three = twin_fused(
        x_rows, z_rows, y_rows, mask, w_one, w_two, w_out
    )
    chip = position // 2
    spot = jnp.asarray(place, jnp.int32)[chip]
    ring_chips = jnp.asarray(snake, jnp.int32)[(spot + jnp.arange(chips, dtype=jnp.int32)) % chips]

    def split_cols(f, width):
        f = jnp.take(f.reshape(rows_dev, chips, 2, width), ring_chips, axis=1)
        keep = lax.dynamic_index_in_dim(f, core, 2, keepdims=False)
        give = lax.dynamic_index_in_dim(f, 1 - core, 2, keepdims=False)
        return keep, lax.ppermute(give, "blk", partner)

    def swap(f):
        return lax.ppermute(f, "blk", partner)

    x_keep, x_got = split_cols(x_rows, r_one)
    h_keep, h_got = split_cols(h_one, r_two)
    g2_got = swap(g_two)
    g1_got = swap(g_one)
    ed_keep, ed_got = split_cols(e_slope, r_one)
    ec_keep, ec_got = split_cols(e_cone, r_two)
    ea2_got = swap(e_atwo)
    ea1_got = swap(e_aone)
    chip_out = grad_three + swap(grad_three)
    part_two = (
        slots_product(ec_keep, g_two) + slots_product(ec_got, g2_got)
        + slots_product(h_keep, e_atwo) + slots_product(h_got, ea2_got)
    )
    part_one = (
        slots_product(ed_keep, g_one) + slots_product(ed_got, g1_got)
        + slots_product(x_keep, e_aone) + slots_product(x_got, ea1_got)
    )
    own_row = jnp.arange(chips, dtype=jnp.int32)[:, None] == chip
    outs = jnp.where(own_row, chip_out[None, :], 0.0)
    summed = jnp.concatenate(
        [part_two, jnp.broadcast_to(outs, (chips,) + outs.shape), part_one], axis=1
    )
    reduced = ring_reduce_scatter(summed, n_blk)
    grad_two = reduced[:r_two]
    grad_out = jnp.sum(reduced[r_two:r_two + chips], axis=0)
    grad_one = reduced[r_two + chips:]
    new_first = 0.8 * mom_first + 0.2 * normalized(grad_one)
    new_second = 0.8 * mom_second + 0.2 * normalized(grad_two)
    new_out = 0.8 * mom_out + 0.2 * normalized(grad_out)
    return (new_first, new_second, new_out)


def solution(mesh):
    in_specs = (
        P(("groups", "blk"), None),
        P(("groups", "blk"), None),
        P(("groups", "blk")),
        P("groups", None),
        P(("groups", "blk"), None),
        P(("groups", "blk"), None),
        P("groups"),
        P(("groups", "blk"), None),
        P(("groups", "blk"), None),
        P("groups"),
    )
    out_specs = (P(("groups", "blk"), None), P(("groups", "blk"), None), P("groups"))
    return jax.shard_map(
        functools.partial(per_device, n_blk=mesh.shape["blk"]),
        mesh=mesh, in_specs=in_specs, out_specs=out_specs, check_vma=False,
    )
```

```python
import functools

import jax
import jax.numpy as jnp
from jax import lax
from jax.experimental import pallas as pl
from jax.experimental.pallas import tpu as pltpu
from jax.sharding import PartitionSpec as P


def rows_product(left, right):
    return lax.dot_general(
        left, right, (((0,), (0,)), ((), ())), preferred_element_type=jnp.float32
    )


def twin_terms(x_rows, z_rows, y_rows, mask, w_one, w_two, w_three):
    w_outf = w_three.astype(jnp.float32)
    a_one = jnp.dot(x_rows, w_one, preferred_element_type=jnp.float32)
    s_one = jax.nn.sigmoid(a_one)
    h_one = jax.nn.softplus(a_one).astype(jnp.bfloat16)
    a_two = jnp.dot(h_one, w_two, preferred_element_type=jnp.float32)
    s_two = jax.nn.sigmoid(a_two)
    h_two = jax.nn.softplus(a_two)
    value = jnp.sum(h_two * w_outf[None, :], axis=1)
    g_two = (s_two * w_outf[None, :]).astype(jnp.bfloat16)
    c_one = lax.dot_general(
        g_two, w_two, (((1,), (1,)), ((), ())), preferred_element_type=jnp.float32
    )
    g_one = (c_one * s_one).astype(jnp.bfloat16)
    slope = lax.dot_general(
        g_one, w_one, (((1,), (1,)), ((), ())), preferred_element_type=jnp.float32
    )
    e_value = 2.0 * mask * (value - y_rows.astype(jnp.float32))
    e_slope = (2.0 * mask[:, None] * (slope - z_rows.astype(jnp.float32))).astype(jnp.bfloat16)
    e_gone = jnp.dot(e_slope, w_one, preferred_element_type=jnp.float32)
    e_cone = (e_gone * s_one).astype(jnp.bfloat16)
    e_sone = e_gone * c_one
    e_gtwo = jnp.dot(e_cone, w_two, preferred_element_type=jnp.float32)
    grad_three = jnp.sum(e_gtwo * s_two + e_value[:, None] * h_two, axis=0)
    e_atwo = (
        e_gtwo * w_outf[None, :] * s_two * (1.0 - s_two)
        + e_value[:, None] * w_outf[None, :] * s_two
    ).astype(jnp.bfloat16)
    e_hone = lax.dot_general(
        e_atwo, w_two, (((1,), (1,)), ((), ())), preferred_element_type=jnp.float32
    )
    e_aone = (e_sone * s_one * (1.0 - s_one) + e_hone * s_one).astype(jnp.bfloat16)
    return (e_slope, g_one, e_aone, e_cone, g_two, h_one, e_atwo, grad_three)


def _nt(left, right):
    return lax.dot_general(left, right, (((1,), (1,)), ((), ())), preferred_element_type=jnp.float32)


def _sigmoid(a):
    return 1.0 / (1.0 + jnp.exp(-a))


def _softplus(a):
    return jnp.maximum(a, 0.0) + jnp.log1p(jnp.exp(-jnp.abs(a)))


def twin_body(r_one, x_ref, z_ref, y_ref, m_ref, w_ref, wo_ref,
              es_ref, g1_ref, ea1_ref, ec1_ref, g2_ref, h1_ref, ea2_ref, g3_ref):
    blocks, width, hidden = w_ref.shape
    w1 = w_ref[:, :r_one, :].reshape(blocks * r_one, hidden)
    w2 = w_ref[:, r_one:, :].reshape(blocks * (width - r_one), hidden)
    wo = wo_ref[...]
    mask = m_ref[...]
    a1 = jnp.dot(x_ref[...], w1, preferred_element_type=jnp.float32)
    s1 = _sigmoid(a1)
    h1 = _softplus(a1).astype(jnp.bfloat16)
    a2 = jnp.dot(h1, w2, preferred_element_type=jnp.float32)
    s2 = _sigmoid(a2)
    h2 = _softplus(a2)
    value = jnp.sum(h2 * wo, axis=1, keepdims=True)
    g2 = (s2 * wo).astype(jnp.bfloat16)
    c1 = _nt(g2, w2)
    g1 = (c1 * s1).astype(jnp.bfloat16)
    slope = _nt(g1, w1)
    ev = 2.0 * mask * (value - y_ref[...])
    ed = (2.0 * mask * (slope - z_ref[...].astype(jnp.float32))).astype(jnp.bfloat16)
    eg1 = jnp.dot(ed, w1, preferred_element_type=jnp.float32)
    ec1 = (eg1 * s1).astype(jnp.bfloat16)
    es1 = eg1 * c1
    eg2 = jnp.dot(ec1, w2, preferred_element_type=jnp.float32)
    g3_ref[...] = jnp.sum(eg2 * s2 + ev * h2, axis=0, keepdims=True)
    ea2 = (eg2 * wo * s2 * (1.0 - s2) + ev * wo * s2).astype(jnp.bfloat16)
    eh1 = _nt(ea2, w2)
    ea1 = (es1 * s1 * (1.0 - s1) + eh1 * s1).astype(jnp.bfloat16)
    es_ref[...] = ed
    g1_ref[...] = g1
    ea1_ref[...] = ea1
    ec1_ref[...] = ec1
    g2_ref[...] = g2
    h1_ref[...] = h1
    ea2_ref[...] = ea2


def twin_fused(x_rows, z_rows, y_rows, mask, w_blocks, r_one, w_three):
    rows, assets = x_rows.shape
    blocks, width, hidden = w_blocks.shape
    bf, f32 = jnp.bfloat16, jnp.float32
    shapes = (
        jax.ShapeDtypeStruct((rows, assets), bf),
        jax.ShapeDtypeStruct((rows, hidden), bf),
        jax.ShapeDtypeStruct((rows, hidden), bf),
        jax.ShapeDtypeStruct((rows, hidden), bf),
        jax.ShapeDtypeStruct((rows, hidden), bf),
        jax.ShapeDtypeStruct((rows, hidden), bf),
        jax.ShapeDtypeStruct((rows, hidden), bf),
        jax.ShapeDtypeStruct((1, hidden), f32),
    )
    vmem = pl.BlockSpec(memory_space=pltpu.VMEM)
    flops = 2 * rows * hidden * (3 * assets + 4 * hidden)
    e_slope, g_one, e_aone, e_cone, g_two, h_one, e_atwo, grad_three = pl.pallas_call(
        functools.partial(twin_body, r_one),
        out_shape=shapes,
        in_specs=[vmem] * 6,
        out_specs=[vmem] * 8,
        cost_estimate=pl.CostEstimate(
            flops=flops, transcendentals=6 * rows * hidden,
            bytes_accessed=2 * blocks * width * hidden + 16 * rows * hidden),
    )(x_rows, z_rows, y_rows.astype(f32)[:, None], mask[:, None], w_blocks,
      w_three.astype(f32)[None, :])
    return (e_slope, g_one, e_aone, e_cone, g_two, h_one, e_atwo, grad_three[0])


def normalized(grad):
    return grad / jnp.sqrt(jnp.mean(grad * grad, axis=-1, keepdims=True) + 1e-06)


def ring_plan(n_blk):
    chips = n_blk // 2
    snake = list(range(0, chips, 2)) + list(range(chips - 1, 0, -2))
    place = [0] * chips
    for p, q in enumerate(snake):
        place[q] = p
    cw = [(2 * snake[p] + c, 2 * snake[(p + 1) % chips] + c) for p in range(chips) for c in range(2)]
    ccw = [(b, a) for a, b in cw]
    partner = [(b, b ^ 1) for b in range(n_blk)]
    return chips, snake, place, cw, ccw, partner


def ring_all_gather(x, n_blk):
    chips, snake, place, cw, ccw, partner = ring_plan(n_blk)
    ahead = chips // 2
    behind = chips - 1 - ahead
    position = lax.axis_index("blk")
    core, chip = position % 2, position // 2
    spot = jnp.asarray(place, jnp.int32)[chip]
    rel = [None] * chips
    rel[0] = x
    left = right = x
    for s in range(1, ahead + 1):
        left = lax.ppermute(left, "blk", cw)
        rel[chips - s] = left
        if s <= behind:
            right = lax.ppermute(right, "blk", ccw)
            rel[s] = right
    mine = jnp.stack(rel)
    other = lax.ppermute(mine, "blk", partner)
    both = jnp.concatenate([mine, other], axis=0)
    dest = jnp.arange(n_blk, dtype=jnp.int32)
    dest_chip, dest_core = dest // 2, dest % 2
    k = (jnp.asarray(place, jnp.int32)[dest_chip] - spot) % chips
    index = jnp.where(dest_core == core, 0, chips) + k
    return jnp.take(both, index, axis=0)


def ring_reduce_scatter(summed, n_blk):
    chips, snake, place, cw, ccw, partner = ring_plan(n_blk)
    ahead = chips // 2
    behind = chips - 1 - ahead
    rows = summed.shape[1]
    split = (rows // 16) * 8

    def forward(part, window):
        acc = part[window % chips]
        for s in range(1, window + 1):
            acc = lax.ppermute(acc, "blk", cw) + part[(window - s) % chips]
        return acc

    def backward(part, window):
        acc = part[chips - window]
        for s in range(1, window + 1):
            acc = lax.ppermute(acc, "blk", ccw)
            if s < window:
                acc = acc + part[chips - window + s]
        return acc

    def both_ways(part, one, other):
        total = forward(part, one)
        if other:
            total = total + backward(part, other)
        return total

    if split == 0 or behind == ahead:
        return both_ways(summed, ahead, behind)
    first = both_ways(summed[:, :split], ahead, behind)
    second = both_ways(summed[:, split:], behind, ahead)
    return jnp.concatenate([first, second], axis=0)


def slots_product(left, right):
    return lax.dot_general(
        left, right, (((0,), (0,)), ((), ())), preferred_element_type=jnp.float32
    )


def per_device(
    paths, deltas, payoffs, counts, w_first, w_second, w_out, mom_first, mom_second, mom_out,
    n_blk,
):
    chips, snake, place, cw, ccw, partner = ring_plan(n_blk)
    position = lax.axis_index("blk")
    core = position % 2
    rows_dev = paths.shape[0]
    r_one, r_two = w_first.shape[0], w_second.shape[0]
    hidden = w_first.shape[1]
    gathered = ring_all_gather(jnp.concatenate([w_first, w_second], axis=0), n_blk)
    if r_one % 16 or r_two % 16:
        gathered = jnp.concatenate(
            [gathered[:, :r_one].reshape(1, n_blk * r_one, hidden),
             gathered[:, r_one:].reshape(1, n_blk * r_two, hidden)], axis=1)
        split_at = n_blk * r_one
    else:
        split_at = r_one
    sending = lax.dynamic_index_in_dim(counts, position, 0, keepdims=False)
    x_rows, z_rows, y_rows = (paths, deltas, payoffs)
    total = jnp.sum(sending)
    mask = (jnp.arange(rows_dev, dtype=jnp.int32) < total).astype(jnp.float32)
    e_slope, g_one, e_aone, e_cone, g_two, h_one, e_atwo, grad_three = twin_fused(
        x_rows, z_rows, y_rows, mask, gathered, split_at, w_out
    )
    chip = position // 2
    spot = jnp.asarray(place, jnp.int32)[chip]
    ring_chips = jnp.asarray(snake, jnp.int32)[(spot + jnp.arange(chips, dtype=jnp.int32)) % chips]

    def split_cols(f, width):
        f = jnp.take(f.reshape(rows_dev, chips, 2, width), ring_chips, axis=1)
        keep = lax.dynamic_index_in_dim(f, core, 2, keepdims=False)
        give = lax.dynamic_index_in_dim(f, 1 - core, 2, keepdims=False)
        return keep, lax.ppermute(give, "blk", partner)

    def swap(f):
        return lax.ppermute(f, "blk", partner)

    x_keep, x_got = split_cols(x_rows, r_one)
    h_keep, h_got = split_cols(h_one, r_two)
    g2_got = swap(g_two)
    g1_got = swap(g_one)
    ed_keep, ed_got = split_cols(e_slope, r_one)
    ec_keep, ec_got = split_cols(e_cone, r_two)
    ea2_got = swap(e_atwo)
    ea1_got = swap(e_aone)
    chip_out = grad_three + swap(grad_three)
    part_two = (
        slots_product(ec_keep, g_two) + slots_product(ec_got, g2_got)
        + slots_product(h_keep, e_atwo) + slots_product(h_got, ea2_got)
    )
    part_one = (
        slots_product(ed_keep, g_one) + slots_product(ed_got, g1_got)
        + slots_product(x_keep, e_aone) + slots_product(x_got, ea1_got)
    )
    own_row = jnp.arange(chips, dtype=jnp.int32)[:, None] == chip
    outs = jnp.where(own_row, chip_out[None, :], 0.0)
    summed = jnp.concatenate(
        [part_two, jnp.broadcast_to(outs, (chips,) + outs.shape), part_one], axis=1
    )
    reduced = ring_reduce_scatter(summed, n_blk)
    grad_two = reduced[:r_two]
    grad_out = jnp.sum(reduced[r_two:r_two + chips], axis=0)
    grad_one = reduced[r_two + chips:]
    new_first = 0.8 * mom_first + 0.2 * normalized(grad_one)
    new_second = 0.8 * mom_second + 0.2 * normalized(grad_two)
    new_out = 0.8 * mom_out + 0.2 * normalized(grad_out)
    return (new_first, new_second, new_out)


def solution(mesh):
    in_specs = (
        P(("groups", "blk"), None),
        P(("groups", "blk"), None),
        P(("groups", "blk")),
        P("groups", None),
        P(("groups", "blk"), None),
        P(("groups", "blk"), None),
        P("groups"),
        P(("groups", "blk"), None),
        P(("groups", "blk"), None),
        P("groups"),
    )
    out_specs = (P(("groups", "blk"), None), P(("groups", "blk"), None), P("groups"))
    return jax.shard_map(
        functools.partial(per_device, n_blk=mesh.shape["blk"]),
        mesh=mesh, in_specs=in_specs, out_specs=out_specs, check_vma=False,
    )
```

```python
import functools

import jax
import jax.numpy as jnp
from jax import lax
from jax.experimental import pallas as pl
from jax.experimental.pallas import tpu as pltpu
from jax.sharding import PartitionSpec as P


def rows_product(left, right):
    return lax.dot_general(
        left, right, (((0,), (0,)), ((), ())), preferred_element_type=jnp.float32
    )


def twin_terms(x_rows, z_rows, y_rows, mask, w_one, w_two, w_three):
    w_outf = w_three.astype(jnp.float32)
    a_one = jnp.dot(x_rows, w_one, preferred_element_type=jnp.float32)
    s_one = jax.nn.sigmoid(a_one)
    h_one = jax.nn.softplus(a_one).astype(jnp.bfloat16)
    a_two = jnp.dot(h_one, w_two, preferred_element_type=jnp.float32)
    s_two = jax.nn.sigmoid(a_two)
    h_two = jax.nn.softplus(a_two)
    value = jnp.sum(h_two * w_outf[None, :], axis=1)
    g_two = (s_two * w_outf[None, :]).astype(jnp.bfloat16)
    c_one = lax.dot_general(
        g_two, w_two, (((1,), (1,)), ((), ())), preferred_element_type=jnp.float32
    )
    g_one = (c_one * s_one).astype(jnp.bfloat16)
    slope = lax.dot_general(
        g_one, w_one, (((1,), (1,)), ((), ())), preferred_element_type=jnp.float32
    )
    e_value = 2.0 * mask * (value - y_rows.astype(jnp.float32))
    e_slope = (2.0 * mask[:, None] * (slope - z_rows.astype(jnp.float32))).astype(jnp.bfloat16)
    e_gone = jnp.dot(e_slope, w_one, preferred_element_type=jnp.float32)
    e_cone = (e_gone * s_one).astype(jnp.bfloat16)
    e_sone = e_gone * c_one
    e_gtwo = jnp.dot(e_cone, w_two, preferred_element_type=jnp.float32)
    grad_three = jnp.sum(e_gtwo * s_two + e_value[:, None] * h_two, axis=0)
    e_atwo = (
        e_gtwo * w_outf[None, :] * s_two * (1.0 - s_two)
        + e_value[:, None] * w_outf[None, :] * s_two
    ).astype(jnp.bfloat16)
    e_hone = lax.dot_general(
        e_atwo, w_two, (((1,), (1,)), ((), ())), preferred_element_type=jnp.float32
    )
    e_aone = (e_sone * s_one * (1.0 - s_one) + e_hone * s_one).astype(jnp.bfloat16)
    return (e_slope, g_one, e_aone, e_cone, g_two, h_one, e_atwo, grad_three)


def _nt(left, right):
    return lax.dot_general(left, right, (((1,), (1,)), ((), ())), preferred_element_type=jnp.float32)


def _sigmoid(a):
    return 1.0 / (1.0 + jnp.exp(-a))


def _softplus(a):
    return jnp.maximum(a, 0.0) + jnp.log1p(jnp.exp(-jnp.abs(a)))


def twin_body(r_one, x_ref, z_ref, y_ref, m_ref, w_ref, wo_ref,
              es_ref, g1_ref, ea1_ref, ec1_ref, g2_ref, h1_ref, ea2_ref, g3_ref):
    blocks, width, hidden = w_ref.shape
    w1 = w_ref[:, :r_one, :].reshape(blocks * r_one, hidden)
    w2 = w_ref[:, r_one:, :].reshape(blocks * (width - r_one), hidden)
    wo = wo_ref[...]
    mask = m_ref[...]
    a1 = jnp.dot(x_ref[...], w1, preferred_element_type=jnp.float32)
    s1 = _sigmoid(a1)
    h1 = _softplus(a1).astype(jnp.bfloat16)
    a2 = jnp.dot(h1, w2, preferred_element_type=jnp.float32)
    s2 = _sigmoid(a2)
    h2 = _softplus(a2)
    value = jnp.sum(h2 * wo, axis=1, keepdims=True)
    g2 = (s2 * wo).astype(jnp.bfloat16)
    c1 = _nt(g2, w2)
    g1 = (c1 * s1).astype(jnp.bfloat16)
    slope = _nt(g1, w1)
    ev = 2.0 * mask * (value - y_ref[...])
    ed = (2.0 * mask * (slope - z_ref[...].astype(jnp.float32))).astype(jnp.bfloat16)
    eg1 = jnp.dot(ed, w1, preferred_element_type=jnp.float32)
    ec1 = (eg1 * s1).astype(jnp.bfloat16)
    es1 = eg1 * c1
    eg2 = jnp.dot(ec1, w2, preferred_element_type=jnp.float32)
    g3_ref[...] = jnp.sum(eg2 * s2 + ev * h2, axis=0, keepdims=True)
    ea2 = (eg2 * wo * s2 * (1.0 - s2) + ev * wo * s2).astype(jnp.bfloat16)
    eh1 = _nt(ea2, w2)
    ea1 = (es1 * s1 * (1.0 - s1) + eh1 * s1).astype(jnp.bfloat16)
    es_ref[...] = ed
    g1_ref[...] = g1
    ea1_ref[...] = ea1
    ec1_ref[...] = ec1
    g2_ref[...] = g2
    h1_ref[...] = h1
    ea2_ref[...] = ea2


def twin_fused(x_rows, z_rows, y_rows, mask, w_blocks, r_one, w_three):
    rows, assets = x_rows.shape
    blocks, width, hidden = w_blocks.shape
    bf, f32 = jnp.bfloat16, jnp.float32
    shapes = (
        jax.ShapeDtypeStruct((rows, assets), bf),
        jax.ShapeDtypeStruct((rows, hidden), bf),
        jax.ShapeDtypeStruct((rows, hidden), bf),
        jax.ShapeDtypeStruct((rows, hidden), bf),
        jax.ShapeDtypeStruct((rows, hidden), bf),
        jax.ShapeDtypeStruct((rows, hidden), bf),
        jax.ShapeDtypeStruct((rows, hidden), bf),
        jax.ShapeDtypeStruct((1, hidden), f32),
    )
    vmem = pl.BlockSpec(memory_space=pltpu.VMEM)
    flops = 2 * rows * hidden * (3 * assets + 4 * hidden)
    e_slope, g_one, e_aone, e_cone, g_two, h_one, e_atwo, grad_three = pl.pallas_call(
        functools.partial(twin_body, r_one),
        out_shape=shapes,
        in_specs=[vmem] * 6,
        out_specs=[vmem] * 8,
        cost_estimate=pl.CostEstimate(
            flops=flops, transcendentals=6 * rows * hidden,
            bytes_accessed=2 * blocks * width * hidden + 16 * rows * hidden),
    )(x_rows, z_rows, y_rows.astype(f32)[:, None], mask[:, None], w_blocks,
      w_three.astype(f32)[None, :])
    return (e_slope, g_one, e_aone, e_cone, g_two, h_one, e_atwo, grad_three[0])


def normalized(grad):
    return grad / jnp.sqrt(jnp.mean(grad * grad, axis=-1, keepdims=True) + 1e-06)


def ring_plan(n_blk):
    chips = n_blk // 2
    snake = list(range(0, chips, 2)) + list(range(chips - 1, 0, -2))
    place = [0] * chips
    for p, q in enumerate(snake):
        place[q] = p
    cw = [(2 * snake[p] + c, 2 * snake[(p + 1) % chips] + c) for p in range(chips) for c in range(2)]
    ccw = [(b, a) for a, b in cw]
    partner = [(b, b ^ 1) for b in range(n_blk)]
    return chips, snake, place, cw, ccw, partner


def ring_all_gather(x, n_blk):
    chips, snake, place, cw, ccw, partner = ring_plan(n_blk)
    ahead = chips // 2
    behind = chips - 1 - ahead
    position = lax.axis_index("blk")
    core, chip = position % 2, position // 2
    spot = jnp.asarray(place, jnp.int32)[chip]
    rel = [None] * chips
    rel[0] = x
    left = right = x
    for s in range(1, ahead + 1):
        left = lax.ppermute(left, "blk", cw)
        rel[chips - s] = left
        if s <= behind:
            right = lax.ppermute(right, "blk", ccw)
            rel[s] = right
    mine = jnp.stack(rel)
    other = lax.ppermute(mine, "blk", partner)
    both = jnp.concatenate([mine, other], axis=0)
    dest = jnp.arange(n_blk, dtype=jnp.int32)
    dest_chip, dest_core = dest // 2, dest % 2
    k = (jnp.asarray(place, jnp.int32)[dest_chip] - spot) % chips
    index = jnp.where(dest_core == core, 0, chips) + k
    return jnp.take(both, index, axis=0, mode="clip")


def ring_reduce_scatter(summed, n_blk):
    chips, snake, place, cw, ccw, partner = ring_plan(n_blk)
    ahead = chips // 2
    behind = chips - 1 - ahead
    rows = summed.shape[1]
    split = (rows // 16) * 8

    def forward(part, window):
        acc = part[window % chips]
        for s in range(1, window + 1):
            acc = lax.ppermute(acc, "blk", cw) + part[(window - s) % chips]
        return acc

    def backward(part, window):
        acc = part[chips - window]
        for s in range(1, window + 1):
            acc = lax.ppermute(acc, "blk", ccw)
            if s < window:
                acc = acc + part[chips - window + s]
        return acc

    def both_ways(part, one, other):
        total = forward(part, one)
        if other:
            total = total + backward(part, other)
        return total

    if split == 0 or behind == ahead:
        return both_ways(summed, ahead, behind)
    first = both_ways(summed[:, :split], ahead, behind)
    second = both_ways(summed[:, split:], behind, ahead)
    return jnp.concatenate([first, second], axis=0)


def slots_product(left, right):
    return lax.dot_general(
        left, right, (((0,), (0,)), ((), ())), preferred_element_type=jnp.float32
    )


def per_device(
    paths, deltas, payoffs, counts, w_first, w_second, w_out, mom_first, mom_second, mom_out,
    n_blk,
):
    chips, snake, place, cw, ccw, partner = ring_plan(n_blk)
    position = lax.axis_index("blk")
    core = position % 2
    rows_dev = paths.shape[0]
    r_one, r_two = w_first.shape[0], w_second.shape[0]
    hidden = w_first.shape[1]
    gathered = ring_all_gather(jnp.concatenate([w_first, w_second], axis=0), n_blk)
    if r_one % 16 or r_two % 16:
        gathered = jnp.concatenate(
            [gathered[:, :r_one].reshape(1, n_blk * r_one, hidden),
             gathered[:, r_one:].reshape(1, n_blk * r_two, hidden)], axis=1)
        split_at = n_blk * r_one
    else:
        split_at = r_one
    sending = lax.dynamic_index_in_dim(counts, position, 0, keepdims=False)
    x_rows, z_rows, y_rows = (paths, deltas, payoffs)
    total = jnp.sum(sending)
    mask = (jnp.arange(rows_dev, dtype=jnp.int32) < total).astype(jnp.float32)
    e_slope, g_one, e_aone, e_cone, g_two, h_one, e_atwo, grad_three = twin_fused(
        x_rows, z_rows, y_rows, mask, gathered, split_at, w_out
    )
    chip = position // 2
    spot = jnp.asarray(place, jnp.int32)[chip]
    ring_chips = jnp.asarray(snake, jnp.int32)[(spot + jnp.arange(chips, dtype=jnp.int32)) % chips]

    def split_cols(f, width):
        f = jnp.take(
            f.reshape(rows_dev, chips, 2, width), ring_chips, axis=1, mode="clip"
        )
        keep = lax.dynamic_index_in_dim(f, core, 2, keepdims=False)
        give = lax.dynamic_index_in_dim(f, 1 - core, 2, keepdims=False)
        return keep, lax.ppermute(give, "blk", partner)

    def swap(f):
        return lax.ppermute(f, "blk", partner)

    x_keep, x_got = split_cols(x_rows, r_one)
    h_keep, h_got = split_cols(h_one, r_two)
    g2_got = swap(g_two)
    g1_got = swap(g_one)
    ed_keep, ed_got = split_cols(e_slope, r_one)
    ec_keep, ec_got = split_cols(e_cone, r_two)
    ea2_got = swap(e_atwo)
    ea1_got = swap(e_aone)
    chip_out = grad_three + swap(grad_three)
    part_two = (
        slots_product(ec_keep, g_two) + slots_product(ec_got, g2_got)
        + slots_product(h_keep, e_atwo) + slots_product(h_got, ea2_got)
    )
    part_one = (
        slots_product(ed_keep, g_one) + slots_product(ed_got, g1_got)
        + slots_product(x_keep, e_aone) + slots_product(x_got, ea1_got)
    )
    own_row = jnp.arange(chips, dtype=jnp.int32)[:, None] == chip
    outs = jnp.where(own_row, chip_out[None, :], 0.0)
    summed = jnp.concatenate(
        [part_two, jnp.broadcast_to(outs, (chips,) + outs.shape), part_one], axis=1
    )
    reduced = ring_reduce_scatter(summed, n_blk)
    grad_two = reduced[:r_two]
    grad_out = jnp.sum(reduced[r_two:r_two + chips], axis=0)
    grad_one = reduced[r_two + chips:]
    new_first = 0.8 * mom_first + 0.2 * normalized(grad_one)
    new_second = 0.8 * mom_second + 0.2 * normalized(grad_two)
    new_out = 0.8 * mom_out + 0.2 * normalized(grad_out)
    return (new_first, new_second, new_out)


def solution(mesh):
    in_specs = (
        P(("groups", "blk"), None),
        P(("groups", "blk"), None),
        P(("groups", "blk")),
        P("groups", None),
        P(("groups", "blk"), None),
        P(("groups", "blk"), None),
        P("groups"),
        P(("groups", "blk"), None),
        P(("groups", "blk"), None),
        P("groups"),
    )
    out_specs = (P(("groups", "blk"), None), P(("groups", "blk"), None), P("groups"))
    return jax.shard_map(
        functools.partial(per_device, n_blk=mesh.shape["blk"]),
        mesh=mesh, in_specs=in_specs, out_specs=out_specs, check_vma=False,
    )
```

```python
import functools

import jax
import jax.numpy as jnp
from jax import lax
from jax.experimental import pallas as pl
from jax.experimental.pallas import tpu as pltpu
from jax.sharding import PartitionSpec as P


def rows_product(left, right):
    return lax.dot_general(
        left, right, (((0,), (0,)), ((), ())), preferred_element_type=jnp.float32
    )


def twin_terms(x_rows, z_rows, y_rows, mask, w_one, w_two, w_three):
    w_outf = w_three.astype(jnp.float32)
    a_one = jnp.dot(x_rows, w_one, preferred_element_type=jnp.float32)
    s_one = jax.nn.sigmoid(a_one)
    h_one = jax.nn.softplus(a_one).astype(jnp.bfloat16)
    a_two = jnp.dot(h_one, w_two, preferred_element_type=jnp.float32)
    s_two = jax.nn.sigmoid(a_two)
    h_two = jax.nn.softplus(a_two)
    value = jnp.sum(h_two * w_outf[None, :], axis=1)
    g_two = (s_two * w_outf[None, :]).astype(jnp.bfloat16)
    c_one = lax.dot_general(
        g_two, w_two, (((1,), (1,)), ((), ())), preferred_element_type=jnp.float32
    )
    g_one = (c_one * s_one).astype(jnp.bfloat16)
    slope = lax.dot_general(
        g_one, w_one, (((1,), (1,)), ((), ())), preferred_element_type=jnp.float32
    )
    e_value = 2.0 * mask * (value - y_rows.astype(jnp.float32))
    e_slope = (2.0 * mask[:, None] * (slope - z_rows.astype(jnp.float32))).astype(jnp.bfloat16)
    e_gone = jnp.dot(e_slope, w_one, preferred_element_type=jnp.float32)
    e_cone = (e_gone * s_one).astype(jnp.bfloat16)
    e_sone = e_gone * c_one
    e_gtwo = jnp.dot(e_cone, w_two, preferred_element_type=jnp.float32)
    grad_three = jnp.sum(e_gtwo * s_two + e_value[:, None] * h_two, axis=0)
    e_atwo = (
        e_gtwo * w_outf[None, :] * s_two * (1.0 - s_two)
        + e_value[:, None] * w_outf[None, :] * s_two
    ).astype(jnp.bfloat16)
    e_hone = lax.dot_general(
        e_atwo, w_two, (((1,), (1,)), ((), ())), preferred_element_type=jnp.float32
    )
    e_aone = (e_sone * s_one * (1.0 - s_one) + e_hone * s_one).astype(jnp.bfloat16)
    return (e_slope, g_one, e_aone, e_cone, g_two, h_one, e_atwo, grad_three)


def _nt(left, right):
    return lax.dot_general(left, right, (((1,), (1,)), ((), ())), preferred_element_type=jnp.float32)


def _sigmoid(a):
    return 1.0 / (1.0 + jnp.exp(-a))


def _softplus(a):
    return jnp.maximum(a, 0.0) + jnp.log1p(jnp.exp(-jnp.abs(a)))


def twin_body(r_one, sel_ref, x_ref, z_ref, y_ref, m_ref, mine_ref, other_ref, wo_ref,
              es_ref, g1_ref, ea1_ref, ec1_ref, g2_ref, h1_ref, ea2_ref, g3_ref):
    chips = mine_ref.shape[0]
    ones, twos = [], []
    for b in range(sel_ref.shape[0]):
        i = sel_ref[b]
        block = jnp.where(i < chips, mine_ref[i % chips], other_ref[i % chips])
        ones.append(block[:r_one])
        twos.append(block[r_one:])
    w1 = jnp.concatenate(ones, axis=0)
    w2 = jnp.concatenate(twos, axis=0)
    wo = wo_ref[...]
    mask = m_ref[...]
    a1 = jnp.dot(x_ref[...], w1, preferred_element_type=jnp.float32)
    s1 = _sigmoid(a1)
    h1 = _softplus(a1).astype(jnp.bfloat16)
    a2 = jnp.dot(h1, w2, preferred_element_type=jnp.float32)
    s2 = _sigmoid(a2)
    h2 = _softplus(a2)
    value = jnp.sum(h2 * wo, axis=1, keepdims=True)
    g2 = (s2 * wo).astype(jnp.bfloat16)
    c1 = _nt(g2, w2)
    g1 = (c1 * s1).astype(jnp.bfloat16)
    slope = _nt(g1, w1)
    ev = 2.0 * mask * (value - y_ref[...])
    ed = (2.0 * mask * (slope - z_ref[...].astype(jnp.float32))).astype(jnp.bfloat16)
    eg1 = jnp.dot(ed, w1, preferred_element_type=jnp.float32)
    ec1 = (eg1 * s1).astype(jnp.bfloat16)
    es1 = eg1 * c1
    eg2 = jnp.dot(ec1, w2, preferred_element_type=jnp.float32)
    g3_ref[...] = jnp.sum(eg2 * s2 + ev * h2, axis=0, keepdims=True)
    ea2 = (eg2 * wo * s2 * (1.0 - s2) + ev * wo * s2).astype(jnp.bfloat16)
    eh1 = _nt(ea2, w2)
    ea1 = (es1 * s1 * (1.0 - s1) + eh1 * s1).astype(jnp.bfloat16)
    es_ref[...] = ed
    g1_ref[...] = g1
    ea1_ref[...] = ea1
    ec1_ref[...] = ec1
    g2_ref[...] = g2
    h1_ref[...] = h1
    ea2_ref[...] = ea2


def twin_fused(x_rows, z_rows, y_rows, mask, mine, other, sel, r_one, w_three):
    rows, assets = x_rows.shape
    chips, width, hidden = mine.shape
    bf, f32 = jnp.bfloat16, jnp.float32
    shapes = (
        jax.ShapeDtypeStruct((rows, assets), bf),
        jax.ShapeDtypeStruct((rows, hidden), bf),
        jax.ShapeDtypeStruct((rows, hidden), bf),
        jax.ShapeDtypeStruct((rows, hidden), bf),
        jax.ShapeDtypeStruct((rows, hidden), bf),
        jax.ShapeDtypeStruct((rows, hidden), bf),
        jax.ShapeDtypeStruct((rows, hidden), bf),
        jax.ShapeDtypeStruct((1, hidden), f32),
    )
    vmem = pl.BlockSpec(memory_space=pltpu.VMEM)
    smem = pl.BlockSpec(memory_space=pltpu.SMEM)
    flops = 2 * rows * hidden * (3 * assets + 4 * hidden)
    e_slope, g_one, e_aone, e_cone, g_two, h_one, e_atwo, grad_three = pl.pallas_call(
        functools.partial(twin_body, r_one),
        out_shape=shapes,
        in_specs=[smem] + [vmem] * 7,
        out_specs=[vmem] * 8,
        cost_estimate=pl.CostEstimate(
            flops=flops, transcendentals=6 * rows * hidden,
            bytes_accessed=4 * chips * width * hidden + 16 * rows * hidden),
    )(sel, x_rows, z_rows, y_rows.astype(f32)[:, None], mask[:, None], mine, other,
      w_three.astype(f32)[None, :])
    return (e_slope, g_one, e_aone, e_cone, g_two, h_one, e_atwo, grad_three[0])


def normalized(grad):
    return grad / jnp.sqrt(jnp.mean(grad * grad, axis=-1, keepdims=True) + 1e-06)


def ring_plan(n_blk):
    chips = n_blk // 2
    snake = list(range(0, chips, 2)) + list(range(chips - 1, 0, -2))
    place = [0] * chips
    for p, q in enumerate(snake):
        place[q] = p
    cw = [(2 * snake[p] + c, 2 * snake[(p + 1) % chips] + c) for p in range(chips) for c in range(2)]
    ccw = [(b, a) for a, b in cw]
    partner = [(b, b ^ 1) for b in range(n_blk)]
    return chips, snake, place, cw, ccw, partner


def ring_all_gather(x, n_blk):
    chips, snake, place, cw, ccw, partner = ring_plan(n_blk)
    ahead = chips // 2
    behind = chips - 1 - ahead
    position = lax.axis_index("blk")
    core, chip = position % 2, position // 2
    spot = jnp.asarray(place, jnp.int32)[chip]
    rel = [None] * chips
    rel[0] = x
    left = right = x
    for s in range(1, ahead + 1):
        left = lax.ppermute(left, "blk", cw)
        rel[chips - s] = left
        if s <= behind:
            right = lax.ppermute(right, "blk", ccw)
            rel[s] = right
    mine = jnp.stack(rel)
    other = lax.ppermute(mine, "blk", partner)
    dest = jnp.arange(n_blk, dtype=jnp.int32)
    dest_chip, dest_core = dest // 2, dest % 2
    k = (jnp.asarray(place, jnp.int32)[dest_chip] - spot) % chips
    index = jnp.where(dest_core == core, 0, chips) + k
    return mine, other, index


def ring_reduce_scatter(summed, n_blk):
    chips, snake, place, cw, ccw, partner = ring_plan(n_blk)
    ahead = chips // 2
    behind = chips - 1 - ahead
    rows = summed.shape[1]
    split = (rows // 16) * 8

    def forward(part, window):
        acc = part[window % chips]
        for s in range(1, window + 1):
            acc = lax.ppermute(acc, "blk", cw) + part[(window - s) % chips]
        return acc

    def backward(part, window):
        acc = part[chips - window]
        for s in range(1, window + 1):
            acc = lax.ppermute(acc, "blk", ccw)
            if s < window:
                acc = acc + part[chips - window + s]
        return acc

    def both_ways(part, one, other):
        total = forward(part, one)
        if other:
            total = total + backward(part, other)
        return total

    if split == 0 or behind == ahead:
        return both_ways(summed, ahead, behind)
    first = both_ways(summed[:, :split], ahead, behind)
    second = both_ways(summed[:, split:], behind, ahead)
    return jnp.concatenate([first, second], axis=0)


def slots_product(left, right):
    return lax.dot_general(
        left, right, (((0,), (0,)), ((), ())), preferred_element_type=jnp.float32
    )


def per_device(
    paths, deltas, payoffs, counts, w_first, w_second, w_out, mom_first, mom_second, mom_out,
    n_blk,
):
    chips, snake, place, cw, ccw, partner = ring_plan(n_blk)
    position = lax.axis_index("blk")
    core = position % 2
    rows_dev = paths.shape[0]
    r_one, r_two = w_first.shape[0], w_second.shape[0]
    hidden = w_first.shape[1]
    mine, other, index = ring_all_gather(jnp.concatenate([w_first, w_second], axis=0), n_blk)
    fused = r_one % 16 == 0 and r_two % 16 == 0
    if not fused:
        gathered = jnp.take(
            jnp.concatenate([mine, other], axis=0), index, axis=0, mode="clip"
        )
        w_one = gathered[:, :r_one].reshape(n_blk * r_one, hidden)
        w_two = gathered[:, r_one:].reshape(n_blk * r_two, hidden)
    sending = lax.dynamic_index_in_dim(counts, position, 0, keepdims=False)
    x_rows, z_rows, y_rows = (paths, deltas, payoffs)
    total = jnp.sum(sending)
    mask = (jnp.arange(rows_dev, dtype=jnp.int32) < total).astype(jnp.float32)
    if fused:
        terms = twin_fused(x_rows, z_rows, y_rows, mask, mine, other, index, r_one, w_out)
    else:
        terms = twin_terms(x_rows, z_rows, y_rows, mask, w_one, w_two, w_out)
    e_slope, g_one, e_aone, e_cone, g_two, h_one, e_atwo, grad_three = terms
    chip = position // 2
    spot = jnp.asarray(place, jnp.int32)[chip]
    ring_chips = jnp.asarray(snake, jnp.int32)[(spot + jnp.arange(chips, dtype=jnp.int32)) % chips]

    def split_cols(f, width):
        f = jnp.take(
            f.reshape(rows_dev, chips, 2, width), ring_chips, axis=1, mode="clip"
        )
        keep = lax.dynamic_index_in_dim(f, core, 2, keepdims=False)
        give = lax.dynamic_index_in_dim(f, 1 - core, 2, keepdims=False)
        return keep, lax.ppermute(give, "blk", partner)

    def swap(f):
        return lax.ppermute(f, "blk", partner)

    x_keep, x_got = split_cols(x_rows, r_one)
    h_keep, h_got = split_cols(h_one, r_two)
    g2_got = swap(g_two)
    g1_got = swap(g_one)
    ed_keep, ed_got = split_cols(e_slope, r_one)
    ec_keep, ec_got = split_cols(e_cone, r_two)
    ea2_got = swap(e_atwo)
    ea1_got = swap(e_aone)
    chip_out = grad_three + swap(grad_three)
    part_two = (
        slots_product(ec_keep, g_two) + slots_product(ec_got, g2_got)
        + slots_product(h_keep, e_atwo) + slots_product(h_got, ea2_got)
    )
    part_one = (
        slots_product(ed_keep, g_one) + slots_product(ed_got, g1_got)
        + slots_product(x_keep, e_aone) + slots_product(x_got, ea1_got)
    )
    own_row = jnp.arange(chips, dtype=jnp.int32)[:, None] == chip
    outs = jnp.where(own_row, chip_out[None, :], 0.0)
    summed = jnp.concatenate(
        [part_two, jnp.broadcast_to(outs, (chips,) + outs.shape), part_one], axis=1
    )
    reduced = ring_reduce_scatter(summed, n_blk)
    grad_two = reduced[:r_two]
    grad_out = jnp.sum(reduced[r_two:r_two + chips], axis=0)
    grad_one = reduced[r_two + chips:]
    new_first = 0.8 * mom_first + 0.2 * normalized(grad_one)
    new_second = 0.8 * mom_second + 0.2 * normalized(grad_two)
    new_out = 0.8 * mom_out + 0.2 * normalized(grad_out)
    return (new_first, new_second, new_out)


def solution(mesh):
    in_specs = (
        P(("groups", "blk"), None),
        P(("groups", "blk"), None),
        P(("groups", "blk")),
        P("groups", None),
        P(("groups", "blk"), None),
        P(("groups", "blk"), None),
        P("groups"),
        P(("groups", "blk"), None),
        P(("groups", "blk"), None),
        P("groups"),
    )
    out_specs = (P(("groups", "blk"), None), P(("groups", "blk"), None), P("groups"))
    return jax.shard_map(
        functools.partial(per_device, n_blk=mesh.shape["blk"]),
        mesh=mesh, in_specs=in_specs, out_specs=out_specs, check_vma=False,
    )
```

```python
import functools

import jax
import jax.numpy as jnp
from jax import lax
from jax.experimental import pallas as pl
from jax.experimental.pallas import tpu as pltpu
from jax.sharding import PartitionSpec as P


def rows_product(left, right):
    return lax.dot_general(
        left, right, (((0,), (0,)), ((), ())), preferred_element_type=jnp.float32
    )


def twin_terms(x_rows, z_rows, y_rows, mask, w_one, w_two, w_three):
    w_outf = w_three.astype(jnp.float32)
    a_one = jnp.dot(x_rows, w_one, preferred_element_type=jnp.float32)
    s_one = jax.nn.sigmoid(a_one)
    h_one = jax.nn.softplus(a_one).astype(jnp.bfloat16)
    a_two = jnp.dot(h_one, w_two, preferred_element_type=jnp.float32)
    s_two = jax.nn.sigmoid(a_two)
    h_two = jax.nn.softplus(a_two)
    value = jnp.sum(h_two * w_outf[None, :], axis=1)
    g_two = (s_two * w_outf[None, :]).astype(jnp.bfloat16)
    c_one = lax.dot_general(
        g_two, w_two, (((1,), (1,)), ((), ())), preferred_element_type=jnp.float32
    )
    g_one = (c_one * s_one).astype(jnp.bfloat16)
    slope = lax.dot_general(
        g_one, w_one, (((1,), (1,)), ((), ())), preferred_element_type=jnp.float32
    )
    e_value = 2.0 * mask * (value - y_rows.astype(jnp.float32))
    e_slope = (2.0 * mask[:, None] * (slope - z_rows.astype(jnp.float32))).astype(jnp.bfloat16)
    e_gone = jnp.dot(e_slope, w_one, preferred_element_type=jnp.float32)
    e_cone = (e_gone * s_one).astype(jnp.bfloat16)
    e_sone = e_gone * c_one
    e_gtwo = jnp.dot(e_cone, w_two, preferred_element_type=jnp.float32)
    grad_three = jnp.sum(e_gtwo * s_two + e_value[:, None] * h_two, axis=0)
    e_atwo = (
        e_gtwo * w_outf[None, :] * s_two * (1.0 - s_two)
        + e_value[:, None] * w_outf[None, :] * s_two
    ).astype(jnp.bfloat16)
    e_hone = lax.dot_general(
        e_atwo, w_two, (((1,), (1,)), ((), ())), preferred_element_type=jnp.float32
    )
    e_aone = (e_sone * s_one * (1.0 - s_one) + e_hone * s_one).astype(jnp.bfloat16)
    return (e_slope, g_one, e_aone, e_cone, g_two, h_one, e_atwo, grad_three)


def _nt(left, right):
    return lax.dot_general(left, right, (((1,), (1,)), ((), ())), preferred_element_type=jnp.float32)


def _sigmoid(a):
    return 1.0 / (1.0 + jnp.exp(-a))


def _softplus(a):
    return jnp.maximum(a, 0.0) + jnp.log1p(jnp.exp(-jnp.abs(a)))


def twin_body(r_one, sel_ref, x_ref, z_ref, y_ref, m_ref, mine_ref, other_ref, wo_ref,
              es_ref, g1_ref, ea1_ref, ec1_ref, g2_ref, h1_ref, ea2_ref, g3_ref):
    chips = mine_ref.shape[0]
    ones, twos = [], []
    for b in range(sel_ref.shape[0]):
        i = sel_ref[b]
        block = jnp.where(i < chips, mine_ref[i % chips], other_ref[i % chips])
        ones.append(block[:r_one])
        twos.append(block[r_one:])
    w1 = jnp.concatenate(ones, axis=0)
    w2 = jnp.concatenate(twos, axis=0)
    wo = wo_ref[...]
    mask = m_ref[...]
    a1 = jnp.dot(x_ref[...], w1, preferred_element_type=jnp.float32)
    s1 = _sigmoid(a1)
    h1 = _softplus(a1).astype(jnp.bfloat16)
    a2 = jnp.dot(h1, w2, preferred_element_type=jnp.float32)
    s2 = _sigmoid(a2)
    h2 = _softplus(a2)
    value = jnp.sum(h2 * wo, axis=1, keepdims=True)
    g2 = (s2 * wo).astype(jnp.bfloat16)
    c1 = _nt(g2, w2)
    g1 = (c1 * s1).astype(jnp.bfloat16)
    slope = _nt(g1, w1)
    ev = 2.0 * mask * (value - y_ref[...])
    ed = (2.0 * mask * (slope - z_ref[...].astype(jnp.float32))).astype(jnp.bfloat16)
    eg1 = jnp.dot(ed, w1, preferred_element_type=jnp.float32)
    ec1 = (eg1 * s1).astype(jnp.bfloat16)
    es1 = eg1 * c1
    eg2 = jnp.dot(ec1, w2, preferred_element_type=jnp.float32)
    g3_ref[...] = jnp.sum(eg2 * s2 + ev * h2, axis=0, keepdims=True)
    ea2 = (eg2 * wo * s2 * (1.0 - s2) + ev * wo * s2).astype(jnp.bfloat16)
    eh1 = _nt(ea2, w2)
    ea1 = (es1 * s1 * (1.0 - s1) + eh1 * s1).astype(jnp.bfloat16)
    es_ref[...] = ed
    g1_ref[...] = g1
    ea1_ref[...] = ea1
    ec1_ref[...] = ec1.astype(jnp.float32).T.astype(jnp.bfloat16)
    g2_ref[...] = g2
    h1_ref[...] = h1.astype(jnp.float32).T.astype(jnp.bfloat16)
    ea2_ref[...] = ea2


def twin_fused(x_rows, z_rows, y_rows, mask, mine, other, sel, r_one, w_three):
    rows, assets = x_rows.shape
    chips, width, hidden = mine.shape
    bf, f32 = jnp.bfloat16, jnp.float32
    shapes = (
        jax.ShapeDtypeStruct((rows, assets), bf),
        jax.ShapeDtypeStruct((rows, hidden), bf),
        jax.ShapeDtypeStruct((rows, hidden), bf),
        jax.ShapeDtypeStruct((hidden, rows), bf),
        jax.ShapeDtypeStruct((rows, hidden), bf),
        jax.ShapeDtypeStruct((hidden, rows), bf),
        jax.ShapeDtypeStruct((rows, hidden), bf),
        jax.ShapeDtypeStruct((1, hidden), f32),
    )
    vmem = pl.BlockSpec(memory_space=pltpu.VMEM)
    smem = pl.BlockSpec(memory_space=pltpu.SMEM)
    flops = 2 * rows * hidden * (3 * assets + 4 * hidden)
    e_slope, g_one, e_aone, e_cone, g_two, h_one, e_atwo, grad_three = pl.pallas_call(
        functools.partial(twin_body, r_one),
        out_shape=shapes,
        in_specs=[smem] + [vmem] * 7,
        out_specs=[vmem] * 8,
        cost_estimate=pl.CostEstimate(
            flops=flops, transcendentals=6 * rows * hidden,
            bytes_accessed=4 * chips * width * hidden + 16 * rows * hidden),
    )(sel, x_rows, z_rows, y_rows.astype(f32)[:, None], mask[:, None], mine, other,
      w_three.astype(f32)[None, :])
    return (e_slope, g_one, e_aone, e_cone, g_two, h_one, e_atwo, grad_three[0])


def normalized(grad):
    return grad / jnp.sqrt(jnp.mean(grad * grad, axis=-1, keepdims=True) + 1e-06)


def ring_plan(n_blk):
    chips = n_blk // 2
    snake = list(range(0, chips, 2)) + list(range(chips - 1, 0, -2))
    place = [0] * chips
    for p, q in enumerate(snake):
        place[q] = p
    cw = [(2 * snake[p] + c, 2 * snake[(p + 1) % chips] + c) for p in range(chips) for c in range(2)]
    ccw = [(b, a) for a, b in cw]
    partner = [(b, b ^ 1) for b in range(n_blk)]
    return chips, snake, place, cw, ccw, partner


def ring_all_gather(x, n_blk):
    chips, snake, place, cw, ccw, partner = ring_plan(n_blk)
    ahead = chips // 2
    behind = chips - 1 - ahead
    position = lax.axis_index("blk")
    core, chip = position % 2, position // 2
    spot = jnp.asarray(place, jnp.int32)[chip]
    rel = [None] * chips
    rel[0] = x
    left = right = x
    for s in range(1, ahead + 1):
        left = lax.ppermute(left, "blk", cw)
        rel[chips - s] = left
        if s <= behind:
            right = lax.ppermute(right, "blk", ccw)
            rel[s] = right
    mine = jnp.stack(rel)
    other = lax.ppermute(mine, "blk", partner)
    dest = jnp.arange(n_blk, dtype=jnp.int32)
    dest_chip, dest_core = dest // 2, dest % 2
    k = (jnp.asarray(place, jnp.int32)[dest_chip] - spot) % chips
    index = jnp.where(dest_core == core, 0, chips) + k
    return mine, other, index


def ring_reduce_scatter(summed, n_blk):
    chips, snake, place, cw, ccw, partner = ring_plan(n_blk)
    ahead = chips // 2
    behind = chips - 1 - ahead
    rows = summed.shape[1]
    split = (rows // 16) * 8

    def forward(part, window):
        acc = part[window % chips]
        for s in range(1, window + 1):
            acc = lax.ppermute(acc, "blk", cw) + part[(window - s) % chips]
        return acc

    def backward(part, window):
        acc = part[chips - window]
        for s in range(1, window + 1):
            acc = lax.ppermute(acc, "blk", ccw)
            if s < window:
                acc = acc + part[chips - window + s]
        return acc

    def both_ways(part, one, other):
        total = forward(part, one)
        if other:
            total = total + backward(part, other)
        return total

    if split == 0 or behind == ahead:
        return both_ways(summed, ahead, behind)
    first = both_ways(summed[:, :split], ahead, behind)
    second = both_ways(summed[:, split:], behind, ahead)
    return jnp.concatenate([first, second], axis=0)


def slots_product(left, right):
    return lax.dot_general(
        left, right, (((0,), (0,)), ((), ())), preferred_element_type=jnp.float32
    )


def per_device(
    paths, deltas, payoffs, counts, w_first, w_second, w_out, mom_first, mom_second, mom_out,
    n_blk,
):
    chips, snake, place, cw, ccw, partner = ring_plan(n_blk)
    position = lax.axis_index("blk")
    core = position % 2
    rows_dev = paths.shape[0]
    r_one, r_two = w_first.shape[0], w_second.shape[0]
    hidden = w_first.shape[1]
    mine, other, index = ring_all_gather(jnp.concatenate([w_first, w_second], axis=0), n_blk)
    fused = r_one % 16 == 0 and r_two % 16 == 0
    if not fused:
        gathered = jnp.take(
            jnp.concatenate([mine, other], axis=0), index, axis=0, mode="clip"
        )
        w_one = gathered[:, :r_one].reshape(n_blk * r_one, hidden)
        w_two = gathered[:, r_one:].reshape(n_blk * r_two, hidden)
    sending = lax.dynamic_index_in_dim(counts, position, 0, keepdims=False)
    x_rows, z_rows, y_rows = (paths, deltas, payoffs)
    total = jnp.sum(sending)
    mask = (jnp.arange(rows_dev, dtype=jnp.int32) < total).astype(jnp.float32)
    if fused:
        terms = twin_fused(x_rows, z_rows, y_rows, mask, mine, other, index, r_one, w_out)
    else:
        terms = twin_terms(x_rows, z_rows, y_rows, mask, w_one, w_two, w_out)
    e_slope, g_one, e_aone, e_cone, g_two, h_one, e_atwo, grad_three = terms
    if not fused:
        e_cone, h_one = e_cone.T, h_one.T
    chip = position // 2
    spot = jnp.asarray(place, jnp.int32)[chip]
    ring_chips = jnp.asarray(snake, jnp.int32)[(spot + jnp.arange(chips, dtype=jnp.int32)) % chips]

    def split_cols(f, width):
        f = jnp.take(
            f.reshape(rows_dev, chips, 2, width), ring_chips, axis=1, mode="clip"
        )
        keep = lax.dynamic_index_in_dim(f, core, 2, keepdims=False)
        give = lax.dynamic_index_in_dim(f, 1 - core, 2, keepdims=False)
        return keep, lax.ppermute(give, "blk", partner)

    def swap(f):
        return lax.ppermute(f, "blk", partner)

    def split_rows(f, width):
        f = jnp.take(f.reshape(chips, 2, width, rows_dev), ring_chips, axis=0, mode="clip")
        keep = lax.dynamic_index_in_dim(f, core, 1, keepdims=False)
        give = lax.dynamic_index_in_dim(f, 1 - core, 1, keepdims=False)
        return keep, lax.ppermute(give, "blk", partner)

    def rows_first(left, right):
        return lax.dot_general(
            left, right, (((2,), (0,)), ((), ())), preferred_element_type=jnp.float32
        )

    x_keep, x_got = split_cols(x_rows, r_one)
    h_keep, h_got = split_rows(h_one, r_two)
    g2_got = swap(g_two)
    g1_got = swap(g_one)
    ed_keep, ed_got = split_cols(e_slope, r_one)
    ec_keep, ec_got = split_rows(e_cone, r_two)
    ea2_got = swap(e_atwo)
    ea1_got = swap(e_aone)
    chip_out = grad_three + swap(grad_three)
    part_two = (
        rows_first(ec_keep, g_two) + rows_first(ec_got, g2_got)
        + rows_first(h_keep, e_atwo) + rows_first(h_got, ea2_got)
    )
    part_one = (
        slots_product(ed_keep, g_one) + slots_product(ed_got, g1_got)
        + slots_product(x_keep, e_aone) + slots_product(x_got, ea1_got)
    )
    own_row = jnp.arange(chips, dtype=jnp.int32)[:, None] == chip
    outs = jnp.where(own_row, chip_out[None, :], 0.0)
    summed = jnp.concatenate(
        [part_two, jnp.broadcast_to(outs, (chips,) + outs.shape), part_one], axis=1
    )
    reduced = ring_reduce_scatter(summed, n_blk)
    grad_two = reduced[:r_two]
    grad_out = jnp.sum(reduced[r_two:r_two + chips], axis=0)
    grad_one = reduced[r_two + chips:]
    new_first = 0.8 * mom_first + 0.2 * normalized(grad_one)
    new_second = 0.8 * mom_second + 0.2 * normalized(grad_two)
    new_out = 0.8 * mom_out + 0.2 * normalized(grad_out)
    return (new_first, new_second, new_out)


def solution(mesh):
    in_specs = (
        P(("groups", "blk"), None),
        P(("groups", "blk"), None),
        P(("groups", "blk")),
        P("groups", None),
        P(("groups", "blk"), None),
        P(("groups", "blk"), None),
        P("groups"),
        P(("groups", "blk"), None),
        P(("groups", "blk"), None),
        P("groups"),
    )
    out_specs = (P(("groups", "blk"), None), P(("groups", "blk"), None), P("groups"))
    return jax.shard_map(
        functools.partial(per_device, n_blk=mesh.shape["blk"]),
        mesh=mesh, in_specs=in_specs, out_specs=out_specs, check_vma=False,
    )
```

```python
import functools

import jax
import jax.numpy as jnp
from jax import lax
from jax.experimental import pallas as pl
from jax.experimental.pallas import tpu as pltpu
from jax.sharding import PartitionSpec as P


def rows_product(left, right):
    return lax.dot_general(
        left, right, (((0,), (0,)), ((), ())), preferred_element_type=jnp.float32
    )


def twin_terms(x_rows, z_rows, y_rows, mask, w_one, w_two, w_three):
    w_outf = w_three.astype(jnp.float32)
    a_one = jnp.dot(x_rows, w_one, preferred_element_type=jnp.float32)
    s_one = jax.nn.sigmoid(a_one)
    h_one = jax.nn.softplus(a_one).astype(jnp.bfloat16)
    a_two = jnp.dot(h_one, w_two, preferred_element_type=jnp.float32)
    s_two = jax.nn.sigmoid(a_two)
    h_two = jax.nn.softplus(a_two)
    value = jnp.sum(h_two * w_outf[None, :], axis=1)
    g_two = (s_two * w_outf[None, :]).astype(jnp.bfloat16)
    c_one = lax.dot_general(
        g_two, w_two, (((1,), (1,)), ((), ())), preferred_element_type=jnp.float32
    )
    g_one = (c_one * s_one).astype(jnp.bfloat16)
    slope = lax.dot_general(
        g_one, w_one, (((1,), (1,)), ((), ())), preferred_element_type=jnp.float32
    )
    e_value = 2.0 * mask * (value - y_rows.astype(jnp.float32))
    e_slope = (2.0 * mask[:, None] * (slope - z_rows.astype(jnp.float32))).astype(jnp.bfloat16)
    e_gone = jnp.dot(e_slope, w_one, preferred_element_type=jnp.float32)
    e_cone = (e_gone * s_one).astype(jnp.bfloat16)
    e_sone = e_gone * c_one
    e_gtwo = jnp.dot(e_cone, w_two, preferred_element_type=jnp.float32)
    grad_three = jnp.sum(e_gtwo * s_two + e_value[:, None] * h_two, axis=0)
    e_atwo = (
        e_gtwo * w_outf[None, :] * s_two * (1.0 - s_two)
        + e_value[:, None] * w_outf[None, :] * s_two
    ).astype(jnp.bfloat16)
    e_hone = lax.dot_general(
        e_atwo, w_two, (((1,), (1,)), ((), ())), preferred_element_type=jnp.float32
    )
    e_aone = (e_sone * s_one * (1.0 - s_one) + e_hone * s_one).astype(jnp.bfloat16)
    return (e_slope, g_one, e_aone, e_cone, g_two, h_one, e_atwo, grad_three)


def _nt(left, right):
    return lax.dot_general(left, right, (((1,), (1,)), ((), ())), preferred_element_type=jnp.float32)


def _sigmoid(a):
    return 1.0 / (1.0 + jnp.exp(-a))


def _softplus(a):
    return jnp.maximum(a, 0.0) + jnp.log1p(jnp.exp(-jnp.abs(a)))


def twin_body(r_one, place, par_ref, x_ref, z_ref, y_ref, mine_ref, other_ref, wo_ref,
              es_ref, g1_ref, ea1_ref, ec1_ref, g2_ref, h1_ref, ea2_ref, g3_ref):
    chips = mine_ref.shape[0]
    total, core, spot = par_ref[0], par_ref[1], par_ref[2]
    rows = x_ref.shape[0]
    mask = (lax.broadcasted_iota(jnp.int32, (rows, 1), 0) < total).astype(jnp.float32)
    ones, twos = [], []
    for b in range(2 * chips):
        k = (place[b // 2] - spot + chips) % chips
        same = (b % 2) == core
        block = jnp.where(same, mine_ref[k], other_ref[k])
        ones.append(block[:r_one])
        twos.append(block[r_one:])
    w1 = jnp.concatenate(ones, axis=0)
    w2 = jnp.concatenate(twos, axis=0)
    wo = wo_ref[...]
    a1 = jnp.dot(x_ref[...], w1, preferred_element_type=jnp.float32)
    s1 = _sigmoid(a1)
    h1 = _softplus(a1).astype(jnp.bfloat16)
    a2 = jnp.dot(h1, w2, preferred_element_type=jnp.float32)
    s2 = _sigmoid(a2)
    h2 = _softplus(a2)
    value = jnp.sum(h2 * wo, axis=1, keepdims=True)
    g2 = (s2 * wo).astype(jnp.bfloat16)
    c1 = _nt(g2, w2)
    g1 = (c1 * s1).astype(jnp.bfloat16)
    slope = _nt(g1, w1)
    ev = 2.0 * mask * (value - y_ref[...])
    ed = (2.0 * mask * (slope - z_ref[...].astype(jnp.float32))).astype(jnp.bfloat16)
    eg1 = jnp.dot(ed, w1, preferred_element_type=jnp.float32)
    ec1 = (eg1 * s1).astype(jnp.bfloat16)
    es1 = eg1 * c1
    eg2 = jnp.dot(ec1, w2, preferred_element_type=jnp.float32)
    g3_ref[...] = jnp.sum(eg2 * s2 + ev * h2, axis=0, keepdims=True)
    ea2 = (eg2 * wo * s2 * (1.0 - s2) + ev * wo * s2).astype(jnp.bfloat16)
    eh1 = _nt(ea2, w2)
    ea1 = (es1 * s1 * (1.0 - s1) + eh1 * s1).astype(jnp.bfloat16)
    es_ref[...] = ed
    g1_ref[...] = g1
    ea1_ref[...] = ea1
    ec1_ref[...] = ec1.astype(jnp.float32).T.astype(jnp.bfloat16)
    g2_ref[...] = g2
    h1_ref[...] = h1.astype(jnp.float32).T.astype(jnp.bfloat16)
    ea2_ref[...] = ea2


def twin_fused(x_rows, z_rows, y_rows, params, place, mine, other, r_one, w_three):
    rows, assets = x_rows.shape
    chips, width, hidden = mine.shape
    bf, f32 = jnp.bfloat16, jnp.float32
    shapes = (
        jax.ShapeDtypeStruct((rows, assets), bf),
        jax.ShapeDtypeStruct((rows, hidden), bf),
        jax.ShapeDtypeStruct((rows, hidden), bf),
        jax.ShapeDtypeStruct((hidden, rows), bf),
        jax.ShapeDtypeStruct((rows, hidden), bf),
        jax.ShapeDtypeStruct((hidden, rows), bf),
        jax.ShapeDtypeStruct((rows, hidden), bf),
        jax.ShapeDtypeStruct((1, hidden), f32),
    )
    vmem = pl.BlockSpec(memory_space=pltpu.VMEM)
    smem = pl.BlockSpec(memory_space=pltpu.SMEM)
    flops = 2 * rows * hidden * (3 * assets + 4 * hidden)
    e_slope, g_one, e_aone, e_cone, g_two, h_one, e_atwo, grad_three = pl.pallas_call(
        functools.partial(twin_body, r_one, place),
        out_shape=shapes,
        in_specs=[smem] + [vmem] * 6,
        out_specs=[vmem] * 8,
        cost_estimate=pl.CostEstimate(
            flops=flops, transcendentals=6 * rows * hidden,
            bytes_accessed=4 * chips * width * hidden + 16 * rows * hidden),
    )(params, x_rows, z_rows, y_rows.astype(f32)[:, None], mine, other,
      w_three.astype(f32)[None, :])
    return (e_slope, g_one, e_aone, e_cone, g_two, h_one, e_atwo, grad_three[0])


def normalized(grad):
    return grad / jnp.sqrt(jnp.mean(grad * grad, axis=-1, keepdims=True) + 1e-06)


def ring_plan(n_blk):
    chips = n_blk // 2
    snake = list(range(0, chips, 2)) + list(range(chips - 1, 0, -2))
    place = [0] * chips
    for p, q in enumerate(snake):
        place[q] = p
    cw = [(2 * snake[p] + c, 2 * snake[(p + 1) % chips] + c) for p in range(chips) for c in range(2)]
    ccw = [(b, a) for a, b in cw]
    partner = [(b, b ^ 1) for b in range(n_blk)]
    return chips, snake, place, cw, ccw, partner


def ring_all_gather(x, n_blk):
    chips, snake, place, cw, ccw, partner = ring_plan(n_blk)
    ahead = chips // 2
    behind = chips - 1 - ahead
    position = lax.axis_index("blk")
    core, chip = position % 2, position // 2
    spot = jnp.asarray(place, jnp.int32)[chip]
    rel = [None] * chips
    rel[0] = x
    left = right = x
    for s in range(1, ahead + 1):
        left = lax.ppermute(left, "blk", cw)
        rel[chips - s] = left
        if s <= behind:
            right = lax.ppermute(right, "blk", ccw)
            rel[s] = right
    mine = jnp.stack(rel)
    other = lax.ppermute(mine, "blk", partner)
    dest = jnp.arange(n_blk, dtype=jnp.int32)
    dest_chip, dest_core = dest // 2, dest % 2
    k = (jnp.asarray(place, jnp.int32)[dest_chip] - spot) % chips
    index = jnp.where(dest_core == core, 0, chips) + k
    return mine, other, index


def ring_reduce_scatter(summed, n_blk):
    chips, snake, place, cw, ccw, partner = ring_plan(n_blk)
    ahead = chips // 2
    behind = chips - 1 - ahead
    rows = summed.shape[1]
    split = (rows // 16) * 8

    def forward(part, window):
        acc = part[window % chips]
        for s in range(1, window + 1):
            acc = lax.ppermute(acc, "blk", cw) + part[(window - s) % chips]
        return acc

    def backward(part, window):
        acc = part[chips - window]
        for s in range(1, window + 1):
            acc = lax.ppermute(acc, "blk", ccw)
            if s < window:
                acc = acc + part[chips - window + s]
        return acc

    def both_ways(part, one, other):
        total = forward(part, one)
        if other:
            total = total + backward(part, other)
        return total

    if split == 0 or behind == ahead:
        return both_ways(summed, ahead, behind)
    first = both_ways(summed[:, :split], ahead, behind)
    second = both_ways(summed[:, split:], behind, ahead)
    return jnp.concatenate([first, second], axis=0)


def slots_product(left, right):
    return lax.dot_general(
        left, right, (((0,), (0,)), ((), ())), preferred_element_type=jnp.float32
    )


def per_device(
    paths, deltas, payoffs, counts, w_first, w_second, w_out, mom_first, mom_second, mom_out,
    n_blk,
):
    chips, snake, place, cw, ccw, partner = ring_plan(n_blk)
    position = lax.axis_index("blk")
    core = position % 2
    rows_dev = paths.shape[0]
    r_one, r_two = w_first.shape[0], w_second.shape[0]
    hidden = w_first.shape[1]
    mine, other, index = ring_all_gather(jnp.concatenate([w_first, w_second], axis=0), n_blk)
    fused = r_one % 16 == 0 and r_two % 16 == 0
    if not fused:
        gathered = jnp.take(
            jnp.concatenate([mine, other], axis=0), index, axis=0, mode="clip"
        )
        w_one = gathered[:, :r_one].reshape(n_blk * r_one, hidden)
        w_two = gathered[:, r_one:].reshape(n_blk * r_two, hidden)
    sending = lax.dynamic_index_in_dim(counts, position, 0, keepdims=False)
    x_rows, z_rows, y_rows = (paths, deltas, payoffs)
    total = jnp.sum(sending)
    mask = (jnp.arange(rows_dev, dtype=jnp.int32) < total).astype(jnp.float32)
    if fused:
        spot = jnp.asarray(place, jnp.int32)[position // 2]
        params = jnp.stack([total, core, spot]).astype(jnp.int32)
        terms = twin_fused(x_rows, z_rows, y_rows, params, place, mine, other, r_one, w_out)
    else:
        terms = twin_terms(x_rows, z_rows, y_rows, mask, w_one, w_two, w_out)
    e_slope, g_one, e_aone, e_cone, g_two, h_one, e_atwo, grad_three = terms
    if not fused:
        e_cone, h_one = e_cone.T, h_one.T
    chip = position // 2
    spot = jnp.asarray(place, jnp.int32)[chip]
    ring_chips = jnp.asarray(snake, jnp.int32)[(spot + jnp.arange(chips, dtype=jnp.int32)) % chips]

    def split_cols(f, width):
        f = jnp.take(
            f.reshape(rows_dev, chips, 2, width), ring_chips, axis=1, mode="clip"
        )
        keep = lax.dynamic_index_in_dim(f, core, 2, keepdims=False)
        give = lax.dynamic_index_in_dim(f, 1 - core, 2, keepdims=False)
        return keep, lax.ppermute(give, "blk", partner)

    def swap(f):
        return lax.ppermute(f, "blk", partner)

    def split_rows(f, width):
        f = jnp.take(f.reshape(chips, 2, width, rows_dev), ring_chips, axis=0, mode="clip")
        keep = lax.dynamic_index_in_dim(f, core, 1, keepdims=False)
        give = lax.dynamic_index_in_dim(f, 1 - core, 1, keepdims=False)
        return keep, lax.ppermute(give, "blk", partner)

    def rows_first(left, right):
        return lax.dot_general(
            left, right, (((2,), (0,)), ((), ())), preferred_element_type=jnp.float32
        )

    x_keep, x_got = split_cols(x_rows, r_one)
    h_keep, h_got = split_rows(h_one, r_two)
    g2_got = swap(g_two)
    g1_got = swap(g_one)
    ed_keep, ed_got = split_cols(e_slope, r_one)
    ec_keep, ec_got = split_rows(e_cone, r_two)
    ea2_got = swap(e_atwo)
    ea1_got = swap(e_aone)
    chip_out = grad_three + swap(grad_three)
    part_two = (
        rows_first(ec_keep, g_two) + rows_first(ec_got, g2_got)
        + rows_first(h_keep, e_atwo) + rows_first(h_got, ea2_got)
    )
    part_one = (
        slots_product(ed_keep, g_one) + slots_product(ed_got, g1_got)
        + slots_product(x_keep, e_aone) + slots_product(x_got, ea1_got)
    )
    own_row = jnp.arange(chips, dtype=jnp.int32)[:, None] == chip
    outs = jnp.where(own_row, chip_out[None, :], 0.0)
    summed = jnp.concatenate(
        [part_two, jnp.broadcast_to(outs, (chips,) + outs.shape), part_one], axis=1
    )
    reduced = ring_reduce_scatter(summed, n_blk)
    grad_two = reduced[:r_two]
    grad_out = jnp.sum(reduced[r_two:r_two + chips], axis=0)
    grad_one = reduced[r_two + chips:]
    new_first = 0.8 * mom_first + 0.2 * normalized(grad_one)
    new_second = 0.8 * mom_second + 0.2 * normalized(grad_two)
    new_out = 0.8 * mom_out + 0.2 * normalized(grad_out)
    return (new_first, new_second, new_out)


def solution(mesh):
    in_specs = (
        P(("groups", "blk"), None),
        P(("groups", "blk"), None),
        P(("groups", "blk")),
        P("groups", None),
        P(("groups", "blk"), None),
        P(("groups", "blk"), None),
        P("groups"),
        P(("groups", "blk"), None),
        P(("groups", "blk"), None),
        P("groups"),
    )
    out_specs = (P(("groups", "blk"), None), P(("groups", "blk"), None), P("groups"))
    return jax.shard_map(
        functools.partial(per_device, n_blk=mesh.shape["blk"]),
        mesh=mesh, in_specs=in_specs, out_specs=out_specs, check_vma=False,
    )
```

```python
import functools

import jax
import jax.numpy as jnp
from jax import lax
from jax.experimental import pallas as pl
from jax.experimental.pallas import tpu as pltpu
from jax.sharding import PartitionSpec as P


def rows_product(left, right):
    return lax.dot_general(
        left, right, (((0,), (0,)), ((), ())), preferred_element_type=jnp.float32
    )


def twin_terms(x_rows, z_rows, y_rows, mask, w_one, w_two, w_three):
    w_outf = w_three.astype(jnp.float32)
    a_one = jnp.dot(x_rows, w_one, preferred_element_type=jnp.float32)
    s_one = jax.nn.sigmoid(a_one)
    h_one = jax.nn.softplus(a_one).astype(jnp.bfloat16)
    a_two = jnp.dot(h_one, w_two, preferred_element_type=jnp.float32)
    s_two = jax.nn.sigmoid(a_two)
    h_two = jax.nn.softplus(a_two)
    value = jnp.sum(h_two * w_outf[None, :], axis=1)
    g_two = (s_two * w_outf[None, :]).astype(jnp.bfloat16)
    c_one = lax.dot_general(
        g_two, w_two, (((1,), (1,)), ((), ())), preferred_element_type=jnp.float32
    )
    g_one = (c_one * s_one).astype(jnp.bfloat16)
    slope = lax.dot_general(
        g_one, w_one, (((1,), (1,)), ((), ())), preferred_element_type=jnp.float32
    )
    e_value = 2.0 * mask * (value - y_rows.astype(jnp.float32))
    e_slope = (2.0 * mask[:, None] * (slope - z_rows.astype(jnp.float32))).astype(jnp.bfloat16)
    e_gone = jnp.dot(e_slope, w_one, preferred_element_type=jnp.float32)
    e_cone = (e_gone * s_one).astype(jnp.bfloat16)
    e_sone = e_gone * c_one
    e_gtwo = jnp.dot(e_cone, w_two, preferred_element_type=jnp.float32)
    grad_three = jnp.sum(e_gtwo * s_two + e_value[:, None] * h_two, axis=0)
    e_atwo = (
        e_gtwo * w_outf[None, :] * s_two * (1.0 - s_two)
        + e_value[:, None] * w_outf[None, :] * s_two
    ).astype(jnp.bfloat16)
    e_hone = lax.dot_general(
        e_atwo, w_two, (((1,), (1,)), ((), ())), preferred_element_type=jnp.float32
    )
    e_aone = (e_sone * s_one * (1.0 - s_one) + e_hone * s_one).astype(jnp.bfloat16)
    return (e_slope, g_one, e_aone, e_cone, g_two, h_one, e_atwo, grad_three)


def _nt(left, right):
    return lax.dot_general(left, right, (((1,), (1,)), ((), ())), preferred_element_type=jnp.float32)


def _sigmoid(a):
    return 1.0 / (1.0 + jnp.exp(-a))


def _softplus(a):
    return jnp.maximum(a, 0.0) + jnp.log1p(jnp.exp(-jnp.abs(a)))


def twin_body(r_one, place, par_ref, x_ref, z_ref, y_ref, mine_ref, other_ref, wo_ref,
              es_ref, g1_ref, ea1_ref, ec1_ref, g2_ref, h1_ref, ea2_ref, g3_ref):
    chips = mine_ref.shape[0]
    total, core, spot = par_ref[0], par_ref[1], par_ref[2]
    rows = x_ref.shape[0]
    mask = (lax.broadcasted_iota(jnp.int32, (rows, 1), 0) < total).astype(jnp.float32)
    ones, twos = [], []
    for b in range(2 * chips):
        k = (place[b // 2] - spot + chips) % chips
        same = (b % 2) == core
        block = jnp.where(same, mine_ref[k], other_ref[k])
        ones.append(block[:r_one])
        twos.append(block[r_one:])
    w1 = jnp.concatenate(ones, axis=0)
    w2 = jnp.concatenate(twos, axis=0)
    wo = wo_ref[...]
    a1 = jnp.dot(x_ref[...], w1, preferred_element_type=jnp.float32)
    s1 = _sigmoid(a1)
    h1 = _softplus(a1).astype(jnp.bfloat16)
    a2 = jnp.dot(h1, w2, preferred_element_type=jnp.float32)
    s2 = _sigmoid(a2)
    h2 = _softplus(a2)
    value = jnp.sum(h2 * wo, axis=1, keepdims=True)
    g2 = (s2 * wo).astype(jnp.bfloat16)
    c1 = _nt(g2, w2)
    g1 = (c1 * s1).astype(jnp.bfloat16)
    slope = _nt(g1, w1)
    ev = 2.0 * mask * (value - y_ref[...])
    ed = (2.0 * mask * (slope - z_ref[...].astype(jnp.float32))).astype(jnp.bfloat16)
    eg1 = jnp.dot(ed, w1, preferred_element_type=jnp.float32)
    ec1 = (eg1 * s1).astype(jnp.bfloat16)
    es1 = eg1 * c1
    eg2 = jnp.dot(ec1, w2, preferred_element_type=jnp.float32)
    g3_ref[...] = jnp.sum(eg2 * s2 + ev * h2, axis=0, keepdims=True)
    ea2 = (eg2 * wo * s2 * (1.0 - s2) + ev * wo * s2).astype(jnp.bfloat16)
    eh1 = _nt(ea2, w2)
    ea1 = (es1 * s1 * (1.0 - s1) + eh1 * s1).astype(jnp.bfloat16)
    es_ref[...] = ed
    g1_ref[...] = g1
    ea1_ref[...] = ea1
    ec1_ref[...] = ec1.astype(jnp.float32).T.astype(jnp.bfloat16)
    g2_ref[...] = g2
    h1_ref[...] = h1.astype(jnp.float32).T.astype(jnp.bfloat16)
    ea2_ref[...] = ea2


def twin_fused(x_rows, z_rows, y_rows, params, place, mine, other, r_one, w_three):
    rows, assets = x_rows.shape
    chips, width, hidden = mine.shape
    bf, f32 = jnp.bfloat16, jnp.float32
    shapes = (
        jax.ShapeDtypeStruct((rows, assets), bf),
        jax.ShapeDtypeStruct((rows, hidden), bf),
        jax.ShapeDtypeStruct((rows, hidden), bf),
        jax.ShapeDtypeStruct((hidden, rows), bf),
        jax.ShapeDtypeStruct((rows, hidden), bf),
        jax.ShapeDtypeStruct((hidden, rows), bf),
        jax.ShapeDtypeStruct((rows, hidden), bf),
        jax.ShapeDtypeStruct((1, hidden), f32),
    )
    vmem = pl.BlockSpec(memory_space=pltpu.VMEM)
    smem = pl.BlockSpec(memory_space=pltpu.SMEM)
    flops = 2 * rows * hidden * (3 * assets + 4 * hidden)
    e_slope, g_one, e_aone, e_cone, g_two, h_one, e_atwo, grad_three = pl.pallas_call(
        functools.partial(twin_body, r_one, place),
        out_shape=shapes,
        in_specs=[smem] + [vmem] * 6,
        out_specs=[vmem] * 8,
        cost_estimate=pl.CostEstimate(
            flops=flops, transcendentals=6 * rows * hidden,
            bytes_accessed=4 * chips * width * hidden + 16 * rows * hidden),
    )(params, x_rows, z_rows, y_rows.astype(f32)[:, None], mine, other,
      w_three.astype(f32)[None, :])
    return (e_slope, g_one, e_aone, e_cone, g_two, h_one, e_atwo, grad_three[0])


def normalized(grad):
    return grad / jnp.sqrt(jnp.mean(grad * grad, axis=-1, keepdims=True) + 1e-06)


def ring_plan(n_blk):
    chips = n_blk // 2
    snake = list(range(0, chips, 2)) + list(range(chips - 1, 0, -2))
    place = [0] * chips
    for p, q in enumerate(snake):
        place[q] = p
    cw = [(2 * snake[p] + c, 2 * snake[(p + 1) % chips] + c) for p in range(chips) for c in range(2)]
    ccw = [(b, a) for a, b in cw]
    partner = [(b, b ^ 1) for b in range(n_blk)]
    return chips, snake, place, cw, ccw, partner


def ring_all_gather(x, n_blk, extra):
    chips, snake, place, cw, ccw, partner = ring_plan(n_blk)
    ahead = chips // 2
    behind = chips - 1 - ahead
    position = lax.axis_index("blk")
    core, chip = position % 2, position // 2
    spot = jnp.asarray(place, jnp.int32)[chip]
    rel = [None] * chips
    rel[0] = x
    left = right = x
    for s in range(1, ahead + 1):
        left = lax.ppermute(left, "blk", cw)
        if s == 1:
            left, extra = lax.optimization_barrier((left, extra))
        rel[chips - s] = left
        if s <= behind:
            right = lax.ppermute(right, "blk", ccw)
            rel[s] = right
    mine = jnp.stack(rel)
    other = lax.ppermute(mine, "blk", partner)
    dest = jnp.arange(n_blk, dtype=jnp.int32)
    dest_chip, dest_core = dest // 2, dest % 2
    k = (jnp.asarray(place, jnp.int32)[dest_chip] - spot) % chips
    index = jnp.where(dest_core == core, 0, chips) + k
    return mine, other, index, extra


def ring_reduce_scatter(summed, n_blk):
    chips, snake, place, cw, ccw, partner = ring_plan(n_blk)
    ahead = chips // 2
    behind = chips - 1 - ahead
    rows = summed.shape[1]
    split = (rows // 16) * 8

    def forward(part, window):
        acc = part[window % chips]
        for s in range(1, window + 1):
            acc = lax.ppermute(acc, "blk", cw) + part[(window - s) % chips]
        return acc

    def backward(part, window):
        acc = part[chips - window]
        for s in range(1, window + 1):
            acc = lax.ppermute(acc, "blk", ccw)
            if s < window:
                acc = acc + part[chips - window + s]
        return acc

    def both_ways(part, one, other):
        total = forward(part, one)
        if other:
            total = total + backward(part, other)
        return total

    if split == 0 or behind == ahead:
        return both_ways(summed, ahead, behind)
    first = both_ways(summed[:, :split], ahead, behind)
    second = both_ways(summed[:, split:], behind, ahead)
    return jnp.concatenate([first, second], axis=0)


def slots_product(left, right):
    return lax.dot_general(
        left, right, (((0,), (0,)), ((), ())), preferred_element_type=jnp.float32
    )


def per_device(
    paths, deltas, payoffs, counts, w_first, w_second, w_out, mom_first, mom_second, mom_out,
    n_blk,
):
    chips, snake, place, cw, ccw, partner = ring_plan(n_blk)
    position = lax.axis_index("blk")
    core = position % 2
    rows_dev = paths.shape[0]
    r_one, r_two = w_first.shape[0], w_second.shape[0]
    hidden = w_first.shape[1]
    total = jnp.sum(lax.dynamic_index_in_dim(counts, position, 0, keepdims=False))
    params = jnp.stack(
        [total, core, jnp.asarray(place, jnp.int32)[position // 2]]
    ).astype(jnp.int32)
    mine, other, index, params = ring_all_gather(
        jnp.concatenate([w_first, w_second], axis=0), n_blk, params
    )
    fused = r_one % 16 == 0 and r_two % 16 == 0
    if not fused:
        gathered = jnp.take(
            jnp.concatenate([mine, other], axis=0), index, axis=0, mode="clip"
        )
        w_one = gathered[:, :r_one].reshape(n_blk * r_one, hidden)
        w_two = gathered[:, r_one:].reshape(n_blk * r_two, hidden)
    sending = lax.dynamic_index_in_dim(counts, position, 0, keepdims=False)
    x_rows, z_rows, y_rows = (paths, deltas, payoffs)
    total = jnp.sum(sending)
    mask = (jnp.arange(rows_dev, dtype=jnp.int32) < total).astype(jnp.float32)
    if fused:
        terms = twin_fused(x_rows, z_rows, y_rows, params, place, mine, other, r_one, w_out)
    else:
        terms = twin_terms(x_rows, z_rows, y_rows, mask, w_one, w_two, w_out)
    e_slope, g_one, e_aone, e_cone, g_two, h_one, e_atwo, grad_three = terms
    if not fused:
        e_cone, h_one = e_cone.T, h_one.T
    chip = position // 2
    spot = jnp.asarray(place, jnp.int32)[chip]
    ring_chips = jnp.asarray(snake, jnp.int32)[(spot + jnp.arange(chips, dtype=jnp.int32)) % chips]

    def split_cols(f, width):
        f = jnp.take(
            f.reshape(rows_dev, chips, 2, width), ring_chips, axis=1, mode="clip"
        )
        keep = lax.dynamic_index_in_dim(f, core, 2, keepdims=False)
        give = lax.dynamic_index_in_dim(f, 1 - core, 2, keepdims=False)
        return keep, lax.ppermute(give, "blk", partner)

    def swap(f):
        return lax.ppermute(f, "blk", partner)

    def split_rows(f, width):
        f = jnp.take(f.reshape(chips, 2, width, rows_dev), ring_chips, axis=0, mode="clip")
        keep = lax.dynamic_index_in_dim(f, core, 1, keepdims=False)
        give = lax.dynamic_index_in_dim(f, 1 - core, 1, keepdims=False)
        return keep, lax.ppermute(give, "blk", partner)

    def rows_first(left, right):
        return lax.dot_general(
            left, right, (((2,), (0,)), ((), ())), preferred_element_type=jnp.float32
        )

    x_keep, x_got = split_cols(x_rows, r_one)
    h_keep, h_got = split_rows(h_one, r_two)
    g2_got = swap(g_two)
    g1_got = swap(g_one)
    ed_keep, ed_got = split_cols(e_slope, r_one)
    ec_keep, ec_got = split_rows(e_cone, r_two)
    ea2_got = swap(e_atwo)
    ea1_got = swap(e_aone)
    chip_out = grad_three + swap(grad_three)
    part_two = (
        rows_first(ec_keep, g_two) + rows_first(ec_got, g2_got)
        + rows_first(h_keep, e_atwo) + rows_first(h_got, ea2_got)
    )
    part_one = (
        slots_product(ed_keep, g_one) + slots_product(ed_got, g1_got)
        + slots_product(x_keep, e_aone) + slots_product(x_got, ea1_got)
    )
    own_row = jnp.arange(chips, dtype=jnp.int32)[:, None] == chip
    outs = jnp.where(own_row, chip_out[None, :], 0.0)
    summed = jnp.concatenate(
        [part_two, jnp.broadcast_to(outs, (chips,) + outs.shape), part_one], axis=1
    )
    reduced = ring_reduce_scatter(summed, n_blk)
    grad_two = reduced[:r_two]
    grad_out = jnp.sum(reduced[r_two:r_two + chips], axis=0)
    grad_one = reduced[r_two + chips:]
    new_first = 0.8 * mom_first + 0.2 * normalized(grad_one)
    new_second = 0.8 * mom_second + 0.2 * normalized(grad_two)
    new_out = 0.8 * mom_out + 0.2 * normalized(grad_out)
    return (new_first, new_second, new_out)


def solution(mesh):
    in_specs = (
        P(("groups", "blk"), None),
        P(("groups", "blk"), None),
        P(("groups", "blk")),
        P("groups", None),
        P(("groups", "blk"), None),
        P(("groups", "blk"), None),
        P("groups"),
        P(("groups", "blk"), None),
        P(("groups", "blk"), None),
        P("groups"),
    )
    out_specs = (P(("groups", "blk"), None), P(("groups", "blk"), None), P("groups"))
    return jax.shard_map(
        functools.partial(per_device, n_blk=mesh.shape["blk"]),
        mesh=mesh, in_specs=in_specs, out_specs=out_specs, check_vma=False,
    )
```

```python
import functools

import jax
import jax.numpy as jnp
from jax import lax
from jax.experimental import pallas as pl
from jax.experimental.pallas import tpu as pltpu
from jax.sharding import PartitionSpec as P


def rows_product(left, right):
    return lax.dot_general(
        left, right, (((0,), (0,)), ((), ())), preferred_element_type=jnp.float32
    )


def twin_terms(x_rows, z_rows, y_rows, mask, w_one, w_two, w_three):
    w_outf = w_three.astype(jnp.float32)
    a_one = jnp.dot(x_rows, w_one, preferred_element_type=jnp.float32)
    s_one = jax.nn.sigmoid(a_one)
    h_one = jax.nn.softplus(a_one).astype(jnp.bfloat16)
    a_two = jnp.dot(h_one, w_two, preferred_element_type=jnp.float32)
    s_two = jax.nn.sigmoid(a_two)
    h_two = jax.nn.softplus(a_two)
    value = jnp.sum(h_two * w_outf[None, :], axis=1)
    g_two = (s_two * w_outf[None, :]).astype(jnp.bfloat16)
    c_one = lax.dot_general(
        g_two, w_two, (((1,), (1,)), ((), ())), preferred_element_type=jnp.float32
    )
    g_one = (c_one * s_one).astype(jnp.bfloat16)
    slope = lax.dot_general(
        g_one, w_one, (((1,), (1,)), ((), ())), preferred_element_type=jnp.float32
    )
    e_value = 2.0 * mask * (value - y_rows.astype(jnp.float32))
    e_slope = (2.0 * mask[:, None] * (slope - z_rows.astype(jnp.float32))).astype(jnp.bfloat16)
    e_gone = jnp.dot(e_slope, w_one, preferred_element_type=jnp.float32)
    e_cone = (e_gone * s_one).astype(jnp.bfloat16)
    e_sone = e_gone * c_one
    e_gtwo = jnp.dot(e_cone, w_two, preferred_element_type=jnp.float32)
    grad_three = jnp.sum(e_gtwo * s_two + e_value[:, None] * h_two, axis=0)
    e_atwo = (
        e_gtwo * w_outf[None, :] * s_two * (1.0 - s_two)
        + e_value[:, None] * w_outf[None, :] * s_two
    ).astype(jnp.bfloat16)
    e_hone = lax.dot_general(
        e_atwo, w_two, (((1,), (1,)), ((), ())), preferred_element_type=jnp.float32
    )
    e_aone = (e_sone * s_one * (1.0 - s_one) + e_hone * s_one).astype(jnp.bfloat16)
    return (e_slope, g_one, e_aone, e_cone, g_two, h_one, e_atwo, grad_three)


def _nt(left, right):
    return lax.dot_general(left, right, (((1,), (1,)), ((), ())), preferred_element_type=jnp.float32)


def _sigmoid(a):
    return 1.0 / (1.0 + jnp.exp(-a))


def _softplus(a):
    return jnp.maximum(a, 0.0) + jnp.log1p(jnp.exp(-jnp.abs(a)))


def twin_body(r_one, place, par_ref, x_ref, z_ref, y_ref, mine_ref, other_ref, wo_ref,
              es_ref, g1_ref, ea1_ref, ec1_ref, g2_ref, h1_ref, ea2_ref, g3_ref):
    chips = mine_ref.shape[0]
    total, core, spot = par_ref[0], par_ref[1], par_ref[2]
    rows = x_ref.shape[0]
    mask = (lax.broadcasted_iota(jnp.int32, (rows, 1), 0) < total).astype(jnp.float32)
    ones, twos = [], []
    for b in range(2 * chips):
        k = (place[b // 2] - spot + chips) % chips
        same = (b % 2) == core
        block = jnp.where(same, mine_ref[k], other_ref[k])
        ones.append(block[:r_one])
        twos.append(block[r_one:])
    w1 = jnp.concatenate(ones, axis=0)
    w2 = jnp.concatenate(twos, axis=0)
    wo = wo_ref[...]
    a1 = jnp.dot(x_ref[...], w1, preferred_element_type=jnp.float32)
    s1 = _sigmoid(a1)
    h1 = _softplus(a1).astype(jnp.bfloat16)
    a2 = jnp.dot(h1, w2, preferred_element_type=jnp.float32)
    s2 = _sigmoid(a2)
    h2 = _softplus(a2)
    value = jnp.sum(h2 * wo, axis=1, keepdims=True)
    g2 = (s2 * wo).astype(jnp.bfloat16)
    c1 = _nt(g2, w2)
    g1 = (c1 * s1).astype(jnp.bfloat16)
    slope = _nt(g1, w1)
    ev = 2.0 * mask * (value - y_ref[...])
    ed = (2.0 * mask * (slope - z_ref[...].astype(jnp.float32))).astype(jnp.bfloat16)
    eg1 = jnp.dot(ed, w1, preferred_element_type=jnp.float32)
    ec1 = (eg1 * s1).astype(jnp.bfloat16)
    es1 = eg1 * c1
    eg2 = jnp.dot(ec1, w2, preferred_element_type=jnp.float32)
    g3_ref[...] = jnp.sum(eg2 * s2 + ev * h2, axis=0, keepdims=True)
    ea2 = (eg2 * wo * s2 * (1.0 - s2) + ev * wo * s2).astype(jnp.bfloat16)
    eh1 = _nt(ea2, w2)
    ea1 = (es1 * s1 * (1.0 - s1) + eh1 * s1).astype(jnp.bfloat16)
    es_ref[...] = ed.astype(jnp.float32).T.astype(jnp.bfloat16)
    g1_ref[...] = g1
    ea1_ref[...] = ea1
    ec1_ref[...] = ec1.astype(jnp.float32).T.astype(jnp.bfloat16)
    g2_ref[...] = g2
    h1_ref[...] = h1.astype(jnp.float32).T.astype(jnp.bfloat16)
    ea2_ref[...] = ea2


def twin_fused(x_rows, z_rows, y_rows, params, place, mine, other, r_one, w_three):
    rows, assets = x_rows.shape
    chips, width, hidden = mine.shape
    bf, f32 = jnp.bfloat16, jnp.float32
    shapes = (
        jax.ShapeDtypeStruct((assets, rows), bf),
        jax.ShapeDtypeStruct((rows, hidden), bf),
        jax.ShapeDtypeStruct((rows, hidden), bf),
        jax.ShapeDtypeStruct((hidden, rows), bf),
        jax.ShapeDtypeStruct((rows, hidden), bf),
        jax.ShapeDtypeStruct((hidden, rows), bf),
        jax.ShapeDtypeStruct((rows, hidden), bf),
        jax.ShapeDtypeStruct((1, hidden), f32),
    )
    vmem = pl.BlockSpec(memory_space=pltpu.VMEM)
    smem = pl.BlockSpec(memory_space=pltpu.SMEM)
    flops = 2 * rows * hidden * (3 * assets + 4 * hidden)
    e_slope, g_one, e_aone, e_cone, g_two, h_one, e_atwo, grad_three = pl.pallas_call(
        functools.partial(twin_body, r_one, place),
        out_shape=shapes,
        in_specs=[smem] + [vmem] * 6,
        out_specs=[vmem] * 8,
        cost_estimate=pl.CostEstimate(
            flops=flops, transcendentals=6 * rows * hidden,
            bytes_accessed=4 * chips * width * hidden + 16 * rows * hidden),
    )(params, x_rows, z_rows, y_rows.astype(f32)[:, None], mine, other,
      w_three.astype(f32)[None, :])
    return (e_slope, g_one, e_aone, e_cone, g_two, h_one, e_atwo, grad_three[0])


def normalized(grad):
    return grad / jnp.sqrt(jnp.mean(grad * grad, axis=-1, keepdims=True) + 1e-06)


def ring_plan(n_blk):
    chips = n_blk // 2
    snake = list(range(0, chips, 2)) + list(range(chips - 1, 0, -2))
    place = [0] * chips
    for p, q in enumerate(snake):
        place[q] = p
    cw = [(2 * snake[p] + c, 2 * snake[(p + 1) % chips] + c) for p in range(chips) for c in range(2)]
    ccw = [(b, a) for a, b in cw]
    partner = [(b, b ^ 1) for b in range(n_blk)]
    return chips, snake, place, cw, ccw, partner


def ring_all_gather(x, n_blk, extra):
    chips, snake, place, cw, ccw, partner = ring_plan(n_blk)
    ahead = chips // 2
    behind = chips - 1 - ahead
    position = lax.axis_index("blk")
    core, chip = position % 2, position // 2
    spot = jnp.asarray(place, jnp.int32)[chip]
    rel = [None] * chips
    rel[0] = x
    left = right = x
    for s in range(1, ahead + 1):
        left = lax.ppermute(left, "blk", cw)
        if s == 1:
            left, extra = lax.optimization_barrier((left, extra))
        rel[chips - s] = left
        if s <= behind:
            right = lax.ppermute(right, "blk", ccw)
            rel[s] = right
    mine = jnp.stack(rel)
    other = lax.ppermute(mine, "blk", partner)
    dest = jnp.arange(n_blk, dtype=jnp.int32)
    dest_chip, dest_core = dest // 2, dest % 2
    k = (jnp.asarray(place, jnp.int32)[dest_chip] - spot) % chips
    index = jnp.where(dest_core == core, 0, chips) + k
    return mine, other, index, extra


def ring_reduce_scatter(summed, n_blk):
    chips, snake, place, cw, ccw, partner = ring_plan(n_blk)
    ahead = chips // 2
    behind = chips - 1 - ahead
    rows = summed.shape[1]
    split = (rows // 16) * 8

    def forward(part, window):
        acc = part[window % chips]
        for s in range(1, window + 1):
            acc = lax.ppermute(acc, "blk", cw) + part[(window - s) % chips]
        return acc

    def backward(part, window):
        acc = part[chips - window]
        for s in range(1, window + 1):
            acc = lax.ppermute(acc, "blk", ccw)
            if s < window:
                acc = acc + part[chips - window + s]
        return acc

    def both_ways(part, one, other):
        total = forward(part, one)
        if other:
            total = total + backward(part, other)
        return total

    if split == 0 or behind == ahead:
        return both_ways(summed, ahead, behind)
    first = both_ways(summed[:, :split], ahead, behind)
    second = both_ways(summed[:, split:], behind, ahead)
    return jnp.concatenate([first, second], axis=0)


def slots_product(left, right):
    return lax.dot_general(
        left, right, (((0,), (0,)), ((), ())), preferred_element_type=jnp.float32
    )


def per_device(
    paths, deltas, payoffs, counts, w_first, w_second, w_out, mom_first, mom_second, mom_out,
    n_blk,
):
    chips, snake, place, cw, ccw, partner = ring_plan(n_blk)
    position = lax.axis_index("blk")
    core = position % 2
    rows_dev = paths.shape[0]
    r_one, r_two = w_first.shape[0], w_second.shape[0]
    hidden = w_first.shape[1]
    total = jnp.sum(lax.dynamic_index_in_dim(counts, position, 0, keepdims=False))
    params = jnp.stack(
        [total, core, jnp.asarray(place, jnp.int32)[position // 2]]
    ).astype(jnp.int32)
    mine, other, index, params = ring_all_gather(
        jnp.concatenate([w_first, w_second], axis=0), n_blk, params
    )
    fused = r_one % 16 == 0 and r_two % 16 == 0
    if not fused:
        gathered = jnp.take(
            jnp.concatenate([mine, other], axis=0), index, axis=0, mode="clip"
        )
        w_one = gathered[:, :r_one].reshape(n_blk * r_one, hidden)
        w_two = gathered[:, r_one:].reshape(n_blk * r_two, hidden)
    sending = lax.dynamic_index_in_dim(counts, position, 0, keepdims=False)
    x_rows, z_rows, y_rows = (paths, deltas, payoffs)
    total = jnp.sum(sending)
    mask = (jnp.arange(rows_dev, dtype=jnp.int32) < total).astype(jnp.float32)
    if fused:
        terms = twin_fused(x_rows, z_rows, y_rows, params, place, mine, other, r_one, w_out)
    else:
        terms = twin_terms(x_rows, z_rows, y_rows, mask, w_one, w_two, w_out)
    e_slope, g_one, e_aone, e_cone, g_two, h_one, e_atwo, grad_three = terms
    if not fused:
        e_cone, h_one, e_slope = e_cone.T, h_one.T, e_slope.T
    chip = position // 2
    spot = jnp.asarray(place, jnp.int32)[chip]
    ring_chips = jnp.asarray(snake, jnp.int32)[(spot + jnp.arange(chips, dtype=jnp.int32)) % chips]

    def split_cols(f, width):
        f = jnp.take(
            f.reshape(rows_dev, chips, 2, width), ring_chips, axis=1, mode="clip"
        )
        keep = lax.dynamic_index_in_dim(f, core, 2, keepdims=False)
        give = lax.dynamic_index_in_dim(f, 1 - core, 2, keepdims=False)
        return keep, lax.ppermute(give, "blk", partner)

    def swap(f):
        return lax.ppermute(f, "blk", partner)

    def split_rows(f, width):
        f = jnp.take(f.reshape(chips, 2, width, rows_dev), ring_chips, axis=0, mode="clip")
        keep = lax.dynamic_index_in_dim(f, core, 1, keepdims=False)
        give = lax.dynamic_index_in_dim(f, 1 - core, 1, keepdims=False)
        return keep, lax.ppermute(give, "blk", partner)

    def rows_first(left, right):
        return lax.dot_general(
            left, right, (((2,), (0,)), ((), ())), preferred_element_type=jnp.float32
        )

    x_keep, x_got = split_cols(x_rows, r_one)
    h_keep, h_got = split_rows(h_one, r_two)
    g2_got = swap(g_two)
    g1_got = swap(g_one)
    ed_keep, ed_got = split_rows(e_slope, r_one)
    ec_keep, ec_got = split_rows(e_cone, r_two)
    ea2_got = swap(e_atwo)
    ea1_got = swap(e_aone)
    chip_out = grad_three + swap(grad_three)
    part_two = (
        rows_first(ec_keep, g_two) + rows_first(ec_got, g2_got)
        + rows_first(h_keep, e_atwo) + rows_first(h_got, ea2_got)
    )
    part_one = (
        rows_first(ed_keep, g_one) + rows_first(ed_got, g1_got)
        + slots_product(x_keep, e_aone) + slots_product(x_got, ea1_got)
    )
    own_row = jnp.arange(chips, dtype=jnp.int32)[:, None] == chip
    outs = jnp.where(own_row, chip_out[None, :], 0.0)
    summed = jnp.concatenate(
        [part_two, jnp.broadcast_to(outs, (chips,) + outs.shape), part_one], axis=1
    )
    reduced = ring_reduce_scatter(summed, n_blk)
    grad_two = reduced[:r_two]
    grad_out = jnp.sum(reduced[r_two:r_two + chips], axis=0)
    grad_one = reduced[r_two + chips:]
    new_first = 0.8 * mom_first + 0.2 * normalized(grad_one)
    new_second = 0.8 * mom_second + 0.2 * normalized(grad_two)
    new_out = 0.8 * mom_out + 0.2 * normalized(grad_out)
    return (new_first, new_second, new_out)


def solution(mesh):
    in_specs = (
        P(("groups", "blk"), None),
        P(("groups", "blk"), None),
        P(("groups", "blk")),
        P("groups", None),
        P(("groups", "blk"), None),
        P(("groups", "blk"), None),
        P("groups"),
        P(("groups", "blk"), None),
        P(("groups", "blk"), None),
        P("groups"),
    )
    out_specs = (P(("groups", "blk"), None), P(("groups", "blk"), None), P("groups"))
    return jax.shard_map(
        functools.partial(per_device, n_blk=mesh.shape["blk"]),
        mesh=mesh, in_specs=in_specs, out_specs=out_specs, check_vma=False,
    )
```

```python
import functools

import jax
import jax.numpy as jnp
from jax import lax
from jax.experimental import pallas as pl
from jax.experimental.pallas import tpu as pltpu
from jax.sharding import PartitionSpec as P


def rows_product(left, right):
    return lax.dot_general(
        left, right, (((0,), (0,)), ((), ())), preferred_element_type=jnp.float32
    )


def twin_terms(x_rows, z_rows, y_rows, mask, w_one, w_two, w_three):
    w_outf = w_three.astype(jnp.float32)
    a_one = jnp.dot(x_rows, w_one, preferred_element_type=jnp.float32)
    s_one = jax.nn.sigmoid(a_one)
    h_one = jax.nn.softplus(a_one).astype(jnp.bfloat16)
    a_two = jnp.dot(h_one, w_two, preferred_element_type=jnp.float32)
    s_two = jax.nn.sigmoid(a_two)
    h_two = jax.nn.softplus(a_two)
    value = jnp.sum(h_two * w_outf[None, :], axis=1)
    g_two = (s_two * w_outf[None, :]).astype(jnp.bfloat16)
    c_one = lax.dot_general(
        g_two, w_two, (((1,), (1,)), ((), ())), preferred_element_type=jnp.float32
    )
    g_one = (c_one * s_one).astype(jnp.bfloat16)
    slope = lax.dot_general(
        g_one, w_one, (((1,), (1,)), ((), ())), preferred_element_type=jnp.float32
    )
    e_value = 2.0 * mask * (value - y_rows.astype(jnp.float32))
    e_slope = (2.0 * mask[:, None] * (slope - z_rows.astype(jnp.float32))).astype(jnp.bfloat16)
    e_gone = jnp.dot(e_slope, w_one, preferred_element_type=jnp.float32)
    e_cone = (e_gone * s_one).astype(jnp.bfloat16)
    e_sone = e_gone * c_one
    e_gtwo = jnp.dot(e_cone, w_two, preferred_element_type=jnp.float32)
    grad_three = jnp.sum(e_gtwo * s_two + e_value[:, None] * h_two, axis=0)
    e_atwo = (
        e_gtwo * w_outf[None, :] * s_two * (1.0 - s_two)
        + e_value[:, None] * w_outf[None, :] * s_two
    ).astype(jnp.bfloat16)
    e_hone = lax.dot_general(
        e_atwo, w_two, (((1,), (1,)), ((), ())), preferred_element_type=jnp.float32
    )
    e_aone = (e_sone * s_one * (1.0 - s_one) + e_hone * s_one).astype(jnp.bfloat16)
    return (e_slope, g_one, e_aone, e_cone, g_two, h_one, e_atwo, grad_three)


def _nt(left, right):
    return lax.dot_general(left, right, (((1,), (1,)), ((), ())), preferred_element_type=jnp.float32)


def _sigmoid(a):
    return 1.0 / (1.0 + jnp.exp(-a))


def _softplus(a):
    return jnp.maximum(a, 0.0) + jnp.log1p(jnp.exp(-jnp.abs(a)))


def twin_body(r_one, place, par_ref, x_ref, z_ref, y_ref, mine_ref, other_ref, wo_ref,
              es_ref, g1_ref, ea1_ref, ec1_ref, g2_ref, h1_ref, ea2_ref, g3_ref):
    chips = mine_ref.shape[0]
    total, core, spot = par_ref[0], par_ref[1], par_ref[2]
    rows = x_ref.shape[0]
    mask = (lax.broadcasted_iota(jnp.int32, (rows, 1), 0) < total).astype(jnp.float32)
    ones, twos = [], []
    for b in range(2 * chips):
        k = (place[b // 2] - spot + chips) % chips
        same = (b % 2) == core
        block = jnp.where(same, mine_ref[k], other_ref[k])
        ones.append(block[:r_one])
        twos.append(block[r_one:])
    w1 = jnp.concatenate(ones, axis=0)
    w2 = jnp.concatenate(twos, axis=0)
    wo = wo_ref[...]
    a1 = jnp.dot(x_ref[...], w1, preferred_element_type=jnp.float32)
    s1 = _sigmoid(a1)
    h1 = _softplus(a1).astype(jnp.bfloat16)
    a2 = jnp.dot(h1, w2, preferred_element_type=jnp.float32)
    s2 = _sigmoid(a2)
    h2 = _softplus(a2)
    value = jnp.sum(h2 * wo, axis=1, keepdims=True)
    g2 = (s2 * wo).astype(jnp.bfloat16)
    c1 = _nt(g2, w2)
    g1 = (c1 * s1).astype(jnp.bfloat16)
    slope = _nt(g1, w1)
    ev = 2.0 * mask * (value - y_ref[...])
    ed = (2.0 * mask * (slope - z_ref[...].astype(jnp.float32))).astype(jnp.bfloat16)
    eg1 = jnp.dot(ed, w1, preferred_element_type=jnp.float32)
    ec1 = (eg1 * s1).astype(jnp.bfloat16)
    es1 = eg1 * c1
    eg2 = jnp.dot(ec1, w2, preferred_element_type=jnp.float32)
    g3_ref[...] = jnp.sum(eg2 * s2 + ev * h2, axis=0, keepdims=True)
    ea2 = (eg2 * wo * s2 * (1.0 - s2) + ev * wo * s2).astype(jnp.bfloat16)
    eh1 = _nt(ea2, w2)
    ea1 = (es1 * s1 * (1.0 - s1) + eh1 * s1).astype(jnp.bfloat16)
    es_ref[...] = ed
    g1_ref[...] = g1
    ea1_ref[...] = ea1
    ec1_ref[...] = ec1.astype(jnp.float32).T.astype(jnp.bfloat16)
    g2_ref[...] = g2
    h1_ref[...] = h1.astype(jnp.float32).T.astype(jnp.bfloat16)
    ea2_ref[...] = ea2


def twin_fused(x_rows, z_rows, y_rows, params, place, mine, other, r_one, w_three):
    rows, assets = x_rows.shape
    chips, width, hidden = mine.shape
    bf, f32 = jnp.bfloat16, jnp.float32
    shapes = (
        jax.ShapeDtypeStruct((rows, assets), bf),
        jax.ShapeDtypeStruct((rows, hidden), bf),
        jax.ShapeDtypeStruct((rows, hidden), bf),
        jax.ShapeDtypeStruct((hidden, rows), bf),
        jax.ShapeDtypeStruct((rows, hidden), bf),
        jax.ShapeDtypeStruct((hidden, rows), bf),
        jax.ShapeDtypeStruct((rows, hidden), bf),
        jax.ShapeDtypeStruct((1, hidden), f32),
    )
    vmem = pl.BlockSpec(memory_space=pltpu.VMEM)
    smem = pl.BlockSpec(memory_space=pltpu.SMEM)
    flops = 2 * rows * hidden * (3 * assets + 4 * hidden)
    e_slope, g_one, e_aone, e_cone, g_two, h_one, e_atwo, grad_three = pl.pallas_call(
        functools.partial(twin_body, r_one, place),
        out_shape=shapes,
        in_specs=[smem] + [vmem] * 6,
        out_specs=[vmem] * 8,
        cost_estimate=pl.CostEstimate(
            flops=flops, transcendentals=6 * rows * hidden,
            bytes_accessed=4 * chips * width * hidden + 16 * rows * hidden),
    )(params, x_rows, z_rows, y_rows.astype(f32)[:, None], mine, other,
      w_three.astype(f32)[None, :])
    return (e_slope, g_one, e_aone, e_cone, g_two, h_one, e_atwo, grad_three[0])


def normalized(grad):
    return grad / jnp.sqrt(jnp.mean(grad * grad, axis=-1, keepdims=True) + 1e-06)


def ring_plan(n_blk):
    chips = n_blk // 2
    snake = list(range(0, chips, 2)) + list(range(chips - 1, 0, -2))
    place = [0] * chips
    for p, q in enumerate(snake):
        place[q] = p
    cw = [(2 * snake[p] + c, 2 * snake[(p + 1) % chips] + c) for p in range(chips) for c in range(2)]
    ccw = [(b, a) for a, b in cw]
    partner = [(b, b ^ 1) for b in range(n_blk)]
    return chips, snake, place, cw, ccw, partner


def ring_all_gather(x, n_blk, extra):
    chips, snake, place, cw, ccw, partner = ring_plan(n_blk)
    ahead = chips // 2
    behind = chips - 1 - ahead
    position = lax.axis_index("blk")
    core, chip = position % 2, position // 2
    spot = jnp.asarray(place, jnp.int32)[chip]
    rel = [None] * chips
    rel[0] = x
    left = right = x
    for s in range(1, ahead + 1):
        left = lax.ppermute(left, "blk", cw)
        if s == 1:
            left, extra = lax.optimization_barrier((left, extra))
        rel[chips - s] = left
        if s <= behind:
            right = lax.ppermute(right, "blk", ccw)
            rel[s] = right
    mine = jnp.stack(rel)
    other = lax.ppermute(mine, "blk", partner)
    dest = jnp.arange(n_blk, dtype=jnp.int32)
    dest_chip, dest_core = dest // 2, dest % 2
    k = (jnp.asarray(place, jnp.int32)[dest_chip] - spot) % chips
    index = jnp.where(dest_core == core, 0, chips) + k
    return mine, other, index, extra


def ring_reduce_scatter(summed, n_blk, got=(None, None)):
    chips, snake, place, cw, ccw, partner = ring_plan(n_blk)
    ahead = chips // 2
    behind = chips - 1 - ahead
    rows = summed.shape[1]
    split = (rows // 16) * 8

    def forward(part, window, got=None):
        acc = part[window % chips]
        for s in range(1, window + 1):
            sent = lax.ppermute(acc, "blk", cw) if got is None or s > 1 else got
            acc = sent + part[(window - s) % chips]
        return acc

    def backward(part, window, got=None):
        acc = part[chips - window]
        for s in range(1, window + 1):
            acc = lax.ppermute(acc, "blk", ccw) if got is None or s > 1 else got
            if s < window:
                acc = acc + part[chips - window + s]
        return acc

    def both_ways(part, one, other, got=(None, None)):
        total = forward(part, one, got[0])
        if other:
            total = total + backward(part, other, got[1])
        return total

    if split == 0 or behind == ahead:
        return both_ways(summed, ahead, behind)
    first = both_ways(summed[:, :split], ahead, behind, got)
    second = both_ways(summed[:, split:], behind, ahead)
    return jnp.concatenate([first, second], axis=0)


def slots_product(left, right):
    return lax.dot_general(
        left, right, (((0,), (0,)), ((), ())), preferred_element_type=jnp.float32
    )


def per_device(
    paths, deltas, payoffs, counts, w_first, w_second, w_out, mom_first, mom_second, mom_out,
    n_blk,
):
    chips, snake, place, cw, ccw, partner = ring_plan(n_blk)
    position = lax.axis_index("blk")
    core = position % 2
    rows_dev = paths.shape[0]
    r_one, r_two = w_first.shape[0], w_second.shape[0]
    hidden = w_first.shape[1]
    total = jnp.sum(lax.dynamic_index_in_dim(counts, position, 0, keepdims=False))
    params = jnp.stack(
        [total, core, jnp.asarray(place, jnp.int32)[position // 2]]
    ).astype(jnp.int32)
    mine, other, index, params = ring_all_gather(
        jnp.concatenate([w_first, w_second], axis=0), n_blk, params
    )
    fused = r_one % 16 == 0 and r_two % 16 == 0
    if not fused:
        gathered = jnp.take(
            jnp.concatenate([mine, other], axis=0), index, axis=0, mode="clip"
        )
        w_one = gathered[:, :r_one].reshape(n_blk * r_one, hidden)
        w_two = gathered[:, r_one:].reshape(n_blk * r_two, hidden)
    sending = lax.dynamic_index_in_dim(counts, position, 0, keepdims=False)
    x_rows, z_rows, y_rows = (paths, deltas, payoffs)
    total = jnp.sum(sending)
    mask = (jnp.arange(rows_dev, dtype=jnp.int32) < total).astype(jnp.float32)
    if fused:
        terms = twin_fused(x_rows, z_rows, y_rows, params, place, mine, other, r_one, w_out)
    else:
        terms = twin_terms(x_rows, z_rows, y_rows, mask, w_one, w_two, w_out)
    e_slope, g_one, e_aone, e_cone, g_two, h_one, e_atwo, grad_three = terms
    if not fused:
        e_cone, h_one = e_cone.T, h_one.T
    chip = position // 2
    spot = jnp.asarray(place, jnp.int32)[chip]
    ring_chips = jnp.asarray(snake, jnp.int32)[(spot + jnp.arange(chips, dtype=jnp.int32)) % chips]

    def split_cols(f, width):
        f = jnp.take(
            f.reshape(rows_dev, chips, 2, width), ring_chips, axis=1, mode="clip"
        )
        keep = lax.dynamic_index_in_dim(f, core, 2, keepdims=False)
        give = lax.dynamic_index_in_dim(f, 1 - core, 2, keepdims=False)
        return keep, lax.ppermute(give, "blk", partner)

    def swap(f):
        return lax.ppermute(f, "blk", partner)

    def split_rows(f, width):
        f = jnp.take(f.reshape(chips, 2, width, rows_dev), ring_chips, axis=0, mode="clip")
        keep = lax.dynamic_index_in_dim(f, core, 1, keepdims=False)
        give = lax.dynamic_index_in_dim(f, 1 - core, 1, keepdims=False)
        return keep, lax.ppermute(give, "blk", partner)

    def rows_first(left, right):
        return lax.dot_general(
            left, right, (((2,), (0,)), ((), ())), preferred_element_type=jnp.float32
        )

    x_keep, x_got = split_cols(x_rows, r_one)
    h_keep, h_got = split_rows(h_one, r_two)
    g2_got = swap(g_two)
    g1_got = swap(g_one)
    ed_keep, ed_got = split_cols(e_slope, r_one)
    ec_keep, ec_got = split_rows(e_cone, r_two)
    ea2_got = swap(e_atwo)
    ea1_got = swap(e_aone)
    chip_out = grad_three + swap(grad_three)
    part_two = (
        rows_first(ec_keep, g_two) + rows_first(ec_got, g2_got)
        + rows_first(h_keep, e_atwo) + rows_first(h_got, ea2_got)
    )
    total_rows = r_one + r_two + chips
    split = (total_rows // 16) * 8
    ahead, behind = chips // 2, chips - 1 - chips // 2
    got = (None, None)
    if 0 < split <= r_two and behind and behind != ahead:
        head = part_two[:, :split]
        got = (lax.ppermute(head[ahead], "blk", cw),
               lax.ppermute(head[chips - behind], "blk", ccw))
        got, e_aone, ea1_got = lax.optimization_barrier((got, e_aone, ea1_got))
    part_one = (
        slots_product(ed_keep, g_one) + slots_product(ed_got, g1_got)
        + slots_product(x_keep, e_aone) + slots_product(x_got, ea1_got)
    )
    own_row = jnp.arange(chips, dtype=jnp.int32)[:, None] == chip
    outs = jnp.where(own_row, chip_out[None, :], 0.0)
    summed = jnp.concatenate(
        [part_two, jnp.broadcast_to(outs, (chips,) + outs.shape), part_one], axis=1
    )
    reduced = ring_reduce_scatter(summed, n_blk, got)
    grad_two = reduced[:r_two]
    grad_out = jnp.sum(reduced[r_two:r_two + chips], axis=0)
    grad_one = reduced[r_two + chips:]
    new_first = 0.8 * mom_first + 0.2 * normalized(grad_one)
    new_second = 0.8 * mom_second + 0.2 * normalized(grad_two)
    new_out = 0.8 * mom_out + 0.2 * normalized(grad_out)
    return (new_first, new_second, new_out)


def solution(mesh):
    in_specs = (
        P(("groups", "blk"), None),
        P(("groups", "blk"), None),
        P(("groups", "blk")),
        P("groups", None),
        P(("groups", "blk"), None),
        P(("groups", "blk"), None),
        P("groups"),
        P(("groups", "blk"), None),
        P(("groups", "blk"), None),
        P("groups"),
    )
    out_specs = (P(("groups", "blk"), None), P(("groups", "blk"), None), P("groups"))
    return jax.shard_map(
        functools.partial(per_device, n_blk=mesh.shape["blk"]),
        mesh=mesh, in_specs=in_specs, out_specs=out_specs, check_vma=False,
    )
```

```python
import functools

import jax
import jax.numpy as jnp
from jax import lax
from jax.experimental import pallas as pl
from jax.experimental.pallas import tpu as pltpu
from jax.sharding import PartitionSpec as P


def rows_product(left, right):
    return lax.dot_general(
        left, right, (((0,), (0,)), ((), ())), preferred_element_type=jnp.float32
    )


def twin_terms(x_rows, z_rows, y_rows, mask, w_one, w_two, w_three):
    w_outf = w_three.astype(jnp.float32)
    a_one = jnp.dot(x_rows, w_one, preferred_element_type=jnp.float32)
    s_one = jax.nn.sigmoid(a_one)
    h_one = jax.nn.softplus(a_one).astype(jnp.bfloat16)
    a_two = jnp.dot(h_one, w_two, preferred_element_type=jnp.float32)
    s_two = jax.nn.sigmoid(a_two)
    h_two = jax.nn.softplus(a_two)
    value = jnp.sum(h_two * w_outf[None, :], axis=1)
    g_two = (s_two * w_outf[None, :]).astype(jnp.bfloat16)
    c_one = lax.dot_general(
        g_two, w_two, (((1,), (1,)), ((), ())), preferred_element_type=jnp.float32
    )
    g_one = (c_one * s_one).astype(jnp.bfloat16)
    slope = lax.dot_general(
        g_one, w_one, (((1,), (1,)), ((), ())), preferred_element_type=jnp.float32
    )
    e_value = 2.0 * mask * (value - y_rows.astype(jnp.float32))
    e_slope = (2.0 * mask[:, None] * (slope - z_rows.astype(jnp.float32))).astype(jnp.bfloat16)
    e_gone = jnp.dot(e_slope, w_one, preferred_element_type=jnp.float32)
    e_cone = (e_gone * s_one).astype(jnp.bfloat16)
    e_sone = e_gone * c_one
    e_gtwo = jnp.dot(e_cone, w_two, preferred_element_type=jnp.float32)
    grad_three = jnp.sum(e_gtwo * s_two + e_value[:, None] * h_two, axis=0)
    e_atwo = (
        e_gtwo * w_outf[None, :] * s_two * (1.0 - s_two)
        + e_value[:, None] * w_outf[None, :] * s_two
    ).astype(jnp.bfloat16)
    e_hone = lax.dot_general(
        e_atwo, w_two, (((1,), (1,)), ((), ())), preferred_element_type=jnp.float32
    )
    e_aone = (e_sone * s_one * (1.0 - s_one) + e_hone * s_one).astype(jnp.bfloat16)
    return (e_slope, g_one, e_aone, e_cone, g_two, h_one, e_atwo, grad_three)


def _nt(left, right):
    return lax.dot_general(left, right, (((1,), (1,)), ((), ())), preferred_element_type=jnp.float32)


def _sigmoid(a):
    return 1.0 / (1.0 + jnp.exp(-a))


def _softplus(a):
    return jnp.maximum(a, 0.0) + jnp.log1p(jnp.exp(-jnp.abs(a)))


def twin_body(r_one, place, par_ref, x_ref, z_ref, y_ref, mine_ref, other_ref, wo_ref,
              es_ref, g1_ref, ea1_ref, ec1_ref, g2_ref, h1_ref, ea2_ref, g3_ref):
    chips = mine_ref.shape[0]
    total, core, spot = par_ref[0], par_ref[1], par_ref[2]
    rows = x_ref.shape[0]
    mask = (lax.broadcasted_iota(jnp.int32, (rows, 1), 0) < total).astype(jnp.float32)
    ones, twos = [], []
    for b in range(2 * chips):
        k = (place[b // 2] - spot + chips) % chips
        same = (b % 2) == core
        block = jnp.where(same, mine_ref[k], other_ref[k])
        ones.append(block[:r_one])
        twos.append(block[r_one:])
    w1 = jnp.concatenate(ones, axis=0)
    w2 = jnp.concatenate(twos, axis=0)
    wo = wo_ref[...]
    a1 = jnp.dot(x_ref[...], w1, preferred_element_type=jnp.float32)
    s1 = _sigmoid(a1)
    h1 = _softplus(a1).astype(jnp.bfloat16)
    a2 = jnp.dot(h1, w2, preferred_element_type=jnp.float32)
    s2 = _sigmoid(a2)
    h2 = _softplus(a2)
    value = jnp.sum(h2 * wo, axis=1, keepdims=True)
    g2 = (s2 * wo).astype(jnp.bfloat16)
    c1 = _nt(g2, w2)
    g1 = (c1 * s1).astype(jnp.bfloat16)
    slope = _nt(g1, w1)
    ev = 2.0 * mask * (value - y_ref[...])
    ed = (2.0 * mask * (slope - z_ref[...].astype(jnp.float32))).astype(jnp.bfloat16)
    eg1 = jnp.dot(ed, w1, preferred_element_type=jnp.float32)
    ec1 = (eg1 * s1).astype(jnp.bfloat16)
    es1 = eg1 * c1
    eg2 = jnp.dot(ec1, w2, preferred_element_type=jnp.float32)
    g3_ref[...] = jnp.sum(eg2 * s2 + ev * h2, axis=0, keepdims=True)
    ea2 = (eg2 * wo * s2 * (1.0 - s2) + ev * wo * s2).astype(jnp.bfloat16)
    eh1 = _nt(ea2, w2)
    ea1 = (es1 * s1 * (1.0 - s1) + eh1 * s1).astype(jnp.bfloat16)
    es_ref[...] = ed
    g1_ref[...] = g1
    ea1_ref[...] = ea1
    ec1_ref[...] = ec1.astype(jnp.float32).T.astype(jnp.bfloat16)
    g2_ref[...] = g2
    h1_ref[...] = h1.astype(jnp.float32).T.astype(jnp.bfloat16)
    ea2_ref[...] = ea2


def twin_fused(x_rows, z_rows, y_rows, params, place, mine, other, r_one, w_three):
    rows, assets = x_rows.shape
    chips, width, hidden = mine.shape
    bf, f32 = jnp.bfloat16, jnp.float32
    shapes = (
        jax.ShapeDtypeStruct((rows, assets), bf),
        jax.ShapeDtypeStruct((rows, hidden), bf),
        jax.ShapeDtypeStruct((rows, hidden), bf),
        jax.ShapeDtypeStruct((hidden, rows), bf),
        jax.ShapeDtypeStruct((rows, hidden), bf),
        jax.ShapeDtypeStruct((hidden, rows), bf),
        jax.ShapeDtypeStruct((rows, hidden), bf),
        jax.ShapeDtypeStruct((1, hidden), f32),
    )
    vmem = pl.BlockSpec(memory_space=pltpu.VMEM)
    smem = pl.BlockSpec(memory_space=pltpu.SMEM)
    flops = 2 * rows * hidden * (3 * assets + 4 * hidden)
    e_slope, g_one, e_aone, e_cone, g_two, h_one, e_atwo, grad_three = pl.pallas_call(
        functools.partial(twin_body, r_one, place),
        out_shape=shapes,
        in_specs=[smem] + [vmem] * 6,
        out_specs=[vmem] * 8,
        cost_estimate=pl.CostEstimate(
            flops=flops, transcendentals=6 * rows * hidden,
            bytes_accessed=4 * chips * width * hidden + 16 * rows * hidden),
    )(params, x_rows, z_rows, y_rows, mine, other, w_three)
    return (e_slope, g_one, e_aone, e_cone, g_two, h_one, e_atwo, grad_three[0])


def normalized(grad):
    return grad / jnp.sqrt(jnp.mean(grad * grad, axis=-1, keepdims=True) + 1e-06)


def ring_plan(n_blk):
    chips = n_blk // 2
    snake = list(range(0, chips, 2)) + list(range(chips - 1, 0, -2))
    place = [0] * chips
    for p, q in enumerate(snake):
        place[q] = p
    cw = [(2 * snake[p] + c, 2 * snake[(p + 1) % chips] + c) for p in range(chips) for c in range(2)]
    ccw = [(b, a) for a, b in cw]
    partner = [(b, b ^ 1) for b in range(n_blk)]
    return chips, snake, place, cw, ccw, partner


def ring_all_gather(x, n_blk, extra):
    chips, snake, place, cw, ccw, partner = ring_plan(n_blk)
    ahead = chips // 2
    behind = chips - 1 - ahead
    position = lax.axis_index("blk")
    core, chip = position % 2, position // 2
    spot = jnp.asarray(place, jnp.int32)[chip]
    rel = [None] * chips
    rel[0] = x
    left = right = x
    for s in range(1, ahead + 1):
        left = lax.ppermute(left, "blk", cw)
        if s == 1:
            left, extra = lax.optimization_barrier((left, extra))
        rel[chips - s] = left
        if s <= behind:
            right = lax.ppermute(right, "blk", ccw)
            rel[s] = right
    mine = jnp.stack(rel)
    other = lax.ppermute(mine, "blk", partner)
    dest = jnp.arange(n_blk, dtype=jnp.int32)
    dest_chip, dest_core = dest // 2, dest % 2
    k = (jnp.asarray(place, jnp.int32)[dest_chip] - spot) % chips
    index = jnp.where(dest_core == core, 0, chips) + k
    return mine, other, index, extra


def ring_reduce_scatter(summed, n_blk):
    chips, snake, place, cw, ccw, partner = ring_plan(n_blk)
    ahead = chips // 2
    behind = chips - 1 - ahead
    rows = summed.shape[1]
    split = (rows // 16) * 8

    def forward(part, window):
        acc = part[window % chips]
        for s in range(1, window + 1):
            acc = lax.ppermute(acc, "blk", cw) + part[(window - s) % chips]
        return acc

    def backward(part, window):
        acc = part[chips - window]
        for s in range(1, window + 1):
            acc = lax.ppermute(acc, "blk", ccw)
            if s < window:
                acc = acc + part[chips - window + s]
        return acc

    def both_ways(part, one, other):
        total = forward(part, one)
        if other:
            total = total + backward(part, other)
        return total

    if split == 0 or behind == ahead:
        return both_ways(summed, ahead, behind)
    first = both_ways(summed[:, :split], ahead, behind)
    second = both_ways(summed[:, split:], behind, ahead)
    return jnp.concatenate([first, second], axis=0)


def slots_product(left, right):
    return lax.dot_general(
        left, right, (((0,), (0,)), ((), ())), preferred_element_type=jnp.float32
    )


def per_device(
    paths, deltas, payoffs, counts, w_first, w_second, w_out, mom_first, mom_second, mom_out,
    n_blk,
):
    chips, snake, place, cw, ccw, partner = ring_plan(n_blk)
    position = lax.axis_index("blk")
    core = position % 2
    rows_dev = paths.shape[0]
    r_one, r_two = w_first.shape[0], w_second.shape[0]
    hidden = w_first.shape[1]
    total = jnp.sum(lax.dynamic_index_in_dim(counts, position, 0, keepdims=False))
    params = jnp.stack(
        [total, core, jnp.asarray(place, jnp.int32)[position // 2]]
    ).astype(jnp.int32)
    side = (params, payoffs.astype(jnp.float32)[:, None], w_out.astype(jnp.float32)[None, :])
    mine, other, index, side = ring_all_gather(
        jnp.concatenate([w_first, w_second], axis=0), n_blk, side
    )
    params, y_col, out_row = side
    fused = r_one % 16 == 0 and r_two % 16 == 0
    if not fused:
        gathered = jnp.take(
            jnp.concatenate([mine, other], axis=0), index, axis=0, mode="clip"
        )
        w_one = gathered[:, :r_one].reshape(n_blk * r_one, hidden)
        w_two = gathered[:, r_one:].reshape(n_blk * r_two, hidden)
    sending = lax.dynamic_index_in_dim(counts, position, 0, keepdims=False)
    x_rows, z_rows, y_rows = (paths, deltas, payoffs)
    total = jnp.sum(sending)
    mask = (jnp.arange(rows_dev, dtype=jnp.int32) < total).astype(jnp.float32)
    if fused:
        terms = twin_fused(x_rows, z_rows, y_col, params, place, mine, other, r_one, out_row)
    else:
        terms = twin_terms(x_rows, z_rows, y_rows, mask, w_one, w_two, w_out)
    e_slope, g_one, e_aone, e_cone, g_two, h_one, e_atwo, grad_three = terms
    if not fused:
        e_cone, h_one = e_cone.T, h_one.T
    chip = position // 2
    spot = jnp.asarray(place, jnp.int32)[chip]
    ring_chips = jnp.asarray(snake, jnp.int32)[(spot + jnp.arange(chips, dtype=jnp.int32)) % chips]

    def split_cols(f, width):
        f = jnp.take(
            f.reshape(rows_dev, chips, 2, width), ring_chips, axis=1, mode="clip"
        )
        keep = lax.dynamic_index_in_dim(f, core, 2, keepdims=False)
        give = lax.dynamic_index_in_dim(f, 1 - core, 2, keepdims=False)
        return keep, lax.ppermute(give, "blk", partner)

    def swap(f):
        return lax.ppermute(f, "blk", partner)

    def split_rows(f, width):
        f = jnp.take(f.reshape(chips, 2, width, rows_dev), ring_chips, axis=0, mode="clip")
        keep = lax.dynamic_index_in_dim(f, core, 1, keepdims=False)
        give = lax.dynamic_index_in_dim(f, 1 - core, 1, keepdims=False)
        return keep, lax.ppermute(give, "blk", partner)

    def rows_first(left, right):
        return lax.dot_general(
            left, right, (((2,), (0,)), ((), ())), preferred_element_type=jnp.float32
        )

    x_keep, x_got = split_cols(x_rows, r_one)
    h_keep, h_got = split_rows(h_one, r_two)
    g2_got = swap(g_two)
    g1_got = swap(g_one)
    ed_keep, ed_got = split_cols(e_slope, r_one)
    ec_keep, ec_got = split_rows(e_cone, r_two)
    ea2_got = swap(e_atwo)
    ea1_got = swap(e_aone)
    chip_out = grad_three + swap(grad_three)
    part_two = (
        rows_first(ec_keep, g_two) + rows_first(ec_got, g2_got)
        + rows_first(h_keep, e_atwo) + rows_first(h_got, ea2_got)
    )
    part_one = (
        slots_product(ed_keep, g_one) + slots_product(ed_got, g1_got)
        + slots_product(x_keep, e_aone) + slots_product(x_got, ea1_got)
    )
    own_row = jnp.arange(chips, dtype=jnp.int32)[:, None] == chip
    outs = jnp.where(own_row, chip_out[None, :], 0.0)
    summed = jnp.concatenate(
        [part_two, jnp.broadcast_to(outs, (chips,) + outs.shape), part_one], axis=1
    )
    reduced = ring_reduce_scatter(summed, n_blk)
    grad_two = reduced[:r_two]
    grad_out = jnp.sum(reduced[r_two:r_two + chips], axis=0)
    grad_one = reduced[r_two + chips:]
    new_first = 0.8 * mom_first + 0.2 * normalized(grad_one)
    new_second = 0.8 * mom_second + 0.2 * normalized(grad_two)
    new_out = 0.8 * mom_out + 0.2 * normalized(grad_out)
    return (new_first, new_second, new_out)


def solution(mesh):
    in_specs = (
        P(("groups", "blk"), None),
        P(("groups", "blk"), None),
        P(("groups", "blk")),
        P("groups", None),
        P(("groups", "blk"), None),
        P(("groups", "blk"), None),
        P("groups"),
        P(("groups", "blk"), None),
        P(("groups", "blk"), None),
        P("groups"),
    )
    out_specs = (P(("groups", "blk"), None), P(("groups", "blk"), None), P("groups"))
    return jax.shard_map(
        functools.partial(per_device, n_blk=mesh.shape["blk"]),
        mesh=mesh, in_specs=in_specs, out_specs=out_specs, check_vma=False,
    )
```
